128 devices in a mesh: row: 64 (over z, y, x), col: 2 (over core).
Axes of the slice: x: 4, y: 4, z: 4, core: 2. Of those that a mesh axis runs over, the one named last changes fastest.
Arguments:
- basis: bfloat16 [512, 64, 512], P('row', 'col'), may hold values from -0.25 to 0.25
- positions: float32 [512, 3, 512], P('row'), may hold values from 0 to 1
- seglen: float32 [512, 512], P('row'), may hold values from 0.5 to 2
- radius: float32 [512, 512], P('row'), may hold values from 0.05 to 0.2
- neighbours: int32 [512, 16], P('row'), may hold values from 0 to 511, as said below
- counts: int32 [512], P('row'), may hold values from 1 to 16, as said below
Outputs:
- reduced: float32 [512, 64, 1024], P('row', 'col')
The draws below stay inside these ranges and needn't reach their ends.
Inputs may be any that keep to these rules, and one draw needn't show every extreme that they name: `neighbours`: each neighbour index differs from its own block's index by at most 8; slot 0 always differs by exactly 8. `counts`: the first block of every 8 has all 16 slots live.
All inputs are finite; a program needn't handle non-finite values.
Results may differ from the reference program's by a relative error of at most 0.019.
Values may be sent and summed in bfloat16 or wider, within the bound.
No kernel may reach another device: no remote copies, remote signals or barrier semaphores. Data moves between devices by JAX's collectives and lax.ppermute only.
A program may use at most 64 MiB of HBM per device.

```python
import math
import jax
import jax.numpy as jnp
from jax import lax

UNK = 512
NB = 64
NEAR = 16
BLK_DEV = 8
BLOCKS = 512


def draw_neighbours(key, part):
    first_key = jax.random.fold_in(key, 11)
    sign_key = jax.random.fold_in(key, 12)
    offsets = jax.random.randint(first_key, (BLOCKS, NEAR), -BLK_DEV, BLK_DEV + 1)
    signs = jax.random.randint(sign_key, (BLOCKS,), 0, 2) * 2 - 1
    offsets = offsets.at[:, 0].set(signs * BLK_DEV)
    own = jnp.arange(BLOCKS, dtype=jnp.int32)[:, None]
    forward = own + offsets
    mirrored = own - offsets
    outside = (forward < 0) | (forward >= BLOCKS)
    return jnp.where(outside, mirrored, forward).astype(jnp.int32)


def draw_counts(key, part):
    low_key = jax.random.fold_in(key, 21)
    each_key = jax.random.fold_in(key, 22)
    lowest = jax.random.randint(low_key, (BLOCKS // BLK_DEV, 1), 1, NEAR // 2 + 2)
    drawn = jax.random.randint(each_key, (BLOCKS // BLK_DEV, BLK_DEV), 0, 1 << 20)
    spread = NEAR + 1 - lowest
    values = lowest + drawn % spread
    values = values.at[:, 0].set(NEAR)
    return values.reshape(BLOCKS).astype(jnp.int32)


def steps_of(rng, extent, split, smallest, largest):
    loudness = 1.0
    for dim, parts in split:
        draws = jax.random.uniform(jax.random.fold_in(jax.random.fold_in(rng, 6), dim), (parts,), jnp.float32, smallest / len(split), largest / len(split))
        loudness = loudness * jnp.repeat(jnp.exp(draws), extent[dim] // parts).reshape((-1,) + (1,) * (len(extent) - 1 - dim))
    return loudness


def centred(stream_key, shape, scale, limit, shards=(), kind=jnp.bfloat16):
    entries = scale * jax.random.normal(stream_key, shape, jnp.float32)
    if shards:
        entries = entries * steps_of(stream_key, shape, shards, -0.22, 0.18)
    return jnp.clip(entries, -limit, limit).astype(kind)


def setup_inputs(seed: int = 0) -> dict:
    key_of = jax.random.split(jax.random.key(seed), 7)
    return {
        "basis": centred(key_of[0], (BLOCKS, NB, UNK), UNK ** -0.5, 0.25, ((0, 64), (1, 2))),
        "positions": jnp.clip(1.0 * jax.random.uniform(key_of[1], (BLOCKS, 3, UNK), jnp.float32) ** steps_of(key_of[1], (BLOCKS, 3, UNK), ((0, 64),), -0.2, 0.2), 0.0, 1.0),
        "seglen": jnp.clip(jnp.exp(math.log(2.0) - 1.3862944 * jax.random.uniform(key_of[2], (BLOCKS, UNK), jnp.float32) ** steps_of(key_of[2], (BLOCKS, UNK), ((0, 64),), -0.2, 0.2)), 0.5, 2.0),
        "radius": jnp.clip(jnp.exp(math.log(0.2) - 1.3862944 * jax.random.uniform(key_of[3], (BLOCKS, UNK), jnp.float32) ** steps_of(key_of[3], (BLOCKS, UNK), ((0, 64),), -0.2, 0.2)), 0.05, 0.2),
        "neighbours": draw_neighbours(jax.random.fold_in(key_of[6], 71), 0),
        "counts": draw_counts(jax.random.fold_in(key_of[6], 71), 0),
    }


def reference(basis, positions, seglen, radius, neighbours, counts):

    def one_block(items):
        own_basis, own_pos, own_len, own_rad, near_ids, live_count = items
        pos_near = jnp.take(positions, near_ids, axis=0)
        len_near = jnp.take(seglen, near_ids, axis=0)
        rad_near = jnp.take(radius, near_ids, axis=0)
        dist_sq = jnp.zeros((near_ids.shape[0], own_pos.shape[1], own_pos.shape[1]), jnp.float32)
        for coord in range(3):
            gap = own_pos[coord][None, :, None] - pos_near[:, coord][:, None, :]
            dist_sq = dist_sq + gap * gap
        coupling = own_len[None, :, None] * len_near[:, None, :] / jnp.sqrt(dist_sq + own_rad[None, :, None] * rad_near[:, None, :])
        coupling = coupling.astype(jnp.bfloat16)
        left = jnp.einsum('pm,kmn->kpn', own_basis.astype(jnp.float32), coupling.astype(jnp.float32)).astype(jnp.bfloat16)
        panels = jnp.take(basis, near_ids, axis=0)
        tiles = jnp.einsum('kpn,kqn->pkq', left.astype(jnp.float32), panels.astype(jnp.float32))
        live = (jnp.arange(near_ids.shape[0], dtype=jnp.int32) < live_count).astype(jnp.float32)
        tiles = tiles * live[None, :, None]
        return tiles.reshape(tiles.shape[0], -1)
    return lax.map(one_block, (basis, positions, seglen, radius, neighbours, counts))
```

```python
import functools

import jax
import jax.numpy as jnp
from jax import lax
from jax.experimental import pallas as pl
from jax.experimental.pallas import tpu as pltpu
from jax.sharding import PartitionSpec as P

CHUNK = 16


def halo(block, width):
    count = lax.axis_size("row")
    forward = [(i, i + 1) for i in range(count - 1)]
    backward = [(i + 1, i) for i in range(count - 1)]
    low = lax.ppermute(block[block.shape[0] - width:], "row", forward)
    high = lax.ppermute(block[:width], "row", backward)
    return jnp.concatenate([low, block, high], axis=0)


def col_swap(x):
    return lax.ppermute(x, "col", [(0, 1), (1, 0)])


def pair_kernel(needed_ref, own_geo_ref, basis_ref, win_geo_ref, win_pan_ref, out_ref,
                bc_ref, cs_ref, *, n_off, unk, half):
    b = pl.program_id(0)
    geo = own_geo_ref[0]
    for c in range(5):
        bc_ref[c] = jnp.broadcast_to(geo[:, c:c + 1], (unk, half))

    def per_offset(o, carry):
        flag = needed_ref[b * n_off + o]

        @pl.when(flag != 0)
        def _():
            j = b + o
            wg = win_geo_ref[j]
            y0 = jnp.broadcast_to(wg[0:1, :], (CHUNK, half))
            y1 = jnp.broadcast_to(wg[1:2, :], (CHUNK, half))
            y2 = jnp.broadcast_to(wg[2:3, :], (CHUNK, half))
            sj = jnp.broadcast_to(wg[3:4, :], (CHUNK, half))
            rj = jnp.broadcast_to(wg[4:5, :], (CHUNK, half))

            def per_chunk(mc, c2):
                rows = pl.ds(pl.multiple_of(mc * CHUNK, CHUNK), CHUNK)
                d0 = bc_ref[0, rows, :] - y0
                d1 = bc_ref[1, rows, :] - y1
                d2 = bc_ref[2, rows, :] - y2
                dd = d0 * d0 + d1 * d1 + d2 * d2 + bc_ref[4, rows, :] * rj
                cv = bc_ref[3, rows, :] * sj * lax.rsqrt(dd)
                cs_ref[rows, :] = cv.astype(jnp.bfloat16)
                return c2

            lax.fori_loop(0, unk // CHUNK, per_chunk, 0, unroll=4)
            left = jnp.dot(basis_ref[0], cs_ref[...], preferred_element_type=jnp.float32)
            left = left.astype(jnp.bfloat16)
            t = lax.dot_general(left, win_pan_ref[j], (((1,), (1,)), ((), ())),
                                preferred_element_type=jnp.float32)
            out_ref[0, o] = t

        @pl.when(flag == 0)
        def _():
            out_ref[0, o] = jnp.zeros(out_ref.shape[2:], out_ref.dtype)

        return carry

    lax.fori_loop(0, n_off, per_offset, 0)


def on_device(basis, positions, seglen, radius, neighbours, counts):
    blk, half_p, unk = basis.shape
    nb_p = 2 * half_p
    half = unk // 2
    near = neighbours.shape[1]
    n_off = 2 * blk + 1
    ci = lax.axis_index("col")
    ri = lax.axis_index("row")

    other = col_swap(basis)
    own_full = jnp.where(ci == 0, jnp.concatenate([basis, other], axis=1),
                         jnp.concatenate([other, basis], axis=1))
    own_half = lax.dynamic_slice_in_dim(own_full, ci * half, half, axis=2)
    win_pan = halo(own_half, blk)

    geo = jnp.concatenate([positions, seglen[:, None, :], radius[:, None, :],
                           jnp.zeros((blk, 3, unk), jnp.float32)], axis=1)
    geo_half = lax.dynamic_slice_in_dim(geo, ci * half, half, axis=2)
    win_geo = halo(geo_half, blk)
    own_geo_t = jnp.transpose(geo, (0, 2, 1))

    own_ids = ri * blk + jnp.arange(blk, dtype=jnp.int32)
    off = jnp.clip(neighbours - own_ids[:, None] + blk, 0, 2 * blk)
    live = jnp.arange(near, dtype=jnp.int32)[None, :] < counts[:, None]
    sel = (off[:, :, None] == jnp.arange(n_off, dtype=jnp.int32)[None, None, :]) & live[:, :, None]
    needed = jnp.any(sel, axis=1).astype(jnp.int32).reshape(-1)

    kernel = functools.partial(pair_kernel, n_off=n_off, unk=unk, half=half)
    part = pl.pallas_call(
        kernel,
        out_shape=jax.ShapeDtypeStruct((blk, n_off, nb_p, nb_p), jnp.float32),
        grid_spec=pltpu.PrefetchScalarGridSpec(
            num_scalar_prefetch=1,
            grid=(blk,),
            in_specs=[
                pl.BlockSpec((1, unk, 8), lambda b, nd: (b, 0, 0)),
                pl.BlockSpec((1, nb_p, unk), lambda b, nd: (b, 0, 0)),
                pl.BlockSpec((3 * blk, 8, half), lambda b, nd: (0, 0, 0)),
                pl.BlockSpec((3 * blk, nb_p, half), lambda b, nd: (0, 0, 0)),
            ],
            out_specs=pl.BlockSpec((1, n_off, nb_p, nb_p), lambda b, nd: (b, 0, 0, 0)),
            scratch_shapes=[
                pltpu.VMEM((5, unk, half), jnp.float32),
                pltpu.VMEM((unk, half), jnp.bfloat16),
            ],
        ),
        compiler_params=pltpu.CompilerParams(dimension_semantics=("arbitrary",)),
    )(needed, own_geo_t, own_full, win_geo, win_pan)

    mine = lax.dynamic_slice_in_dim(part, ci * half_p, half_p, axis=2)
    theirs = lax.dynamic_slice_in_dim(part, (1 - ci) * half_p, half_p, axis=2)
    tiles = mine + col_swap(theirs)
    result = jnp.einsum("bko,bopq->bpkq", sel.astype(jnp.float32), tiles,
                        precision=lax.Precision.HIGHEST)
    return result.reshape(blk, half_p, near * nb_p)


def solution(mesh):
    placed = (
        P("row", "col", None),
        P("row", None, None),
        P("row", None),
        P("row", None),
        P("row", None),
        P("row"),
    )
    return jax.shard_map(
        on_device, mesh=mesh, in_specs=placed, out_specs=P("row", "col", None), check_vma=False
    )
```

```python
import functools

import jax
import jax.numpy as jnp
from jax import lax
from jax.experimental import pallas as pl
from jax.experimental.pallas import tpu as pltpu
from jax.sharding import PartitionSpec as P


CHUNK = 8
LANES = 128


def split3(x):
    hi = x.astype(jnp.bfloat16)
    r1 = x - hi.astype(jnp.float32)
    mid = r1.astype(jnp.bfloat16)
    lo = (r1 - mid.astype(jnp.float32)).astype(jnp.bfloat16)
    return hi, mid, lo


def pair_kernel(needed_ref, off_ref, live_ref, own_geo_ref, basis_ref, win_geo_ref,
                win_pan_ref, out_ref, bc_ref, cs_ref, ts_ref, *, n_off, near, unk, half, nb_p):
    b = pl.program_id(0)
    geo = own_geo_ref[0]
    for c in range(4):
        bc_ref[c] = jnp.broadcast_to(geo[:, c:c + 1], (unk, LANES))
    n_tiles = half // LANES

    def per_offset(o, carry):
        @pl.when(needed_ref[b * n_off + o] != 0)
        def _():
            j = b + o
            wg = win_geo_ref[j]
            ys = [[jnp.broadcast_to(wg[c:c + 1, h * LANES:(h + 1) * LANES], (CHUNK, LANES))
                   for h in range(n_tiles)] for c in (0, 1, 2, 4)]
            for mc in range(unk // CHUNK):
                rows = slice(mc * CHUNK, (mc + 1) * CHUNK)
                xs = [bc_ref[c, rows, :] for c in range(4)]
                for h in range(n_tiles):
                    d0 = xs[0] - ys[0][h]
                    d1 = xs[1] - ys[1][h]
                    d2 = xs[2] - ys[2][h]
                    dd = d0 * d0 + d1 * d1 + d2 * d2 + xs[3] * ys[3][h]
                    cs_ref[rows, h * LANES:(h + 1) * LANES] = lax.rsqrt(dd).astype(jnp.bfloat16)
            left = jnp.dot(basis_ref[0], cs_ref[...], preferred_element_type=jnp.float32)
            left = (left * wg[3:4, :]).astype(jnp.bfloat16)
            ts_ref[o] = lax.dot_general(left, win_pan_ref[j], (((1,), (1,)), ((), ())),
                                        preferred_element_type=jnp.float32)

        return carry

    lax.fori_loop(0, n_off, per_offset, 0)

    half_p = nb_p // 2
    for k in range(near):
        o_k = off_ref[b * near + k]
        t = ts_ref[o_k]
        t = jnp.where(live_ref[b * near + k] != 0, t, jnp.zeros_like(t))
        for h in range(2):
            out_ref[h, 0, :, k * nb_p:(k + 1) * nb_p] = t[h * half_p:(h + 1) * half_p]


def on_device(basis, positions, seglen, radius, neighbours, counts):
    blk, half_p, unk = basis.shape
    nb_p = 2 * half_p
    half = unk // 2
    near = neighbours.shape[1]
    n_off = 2 * blk + 1
    n_row = lax.axis_size("row")
    ci = lax.axis_index("col")
    ri = lax.axis_index("row")

    other = lax.ppermute(basis, "col", [(0, 1), (1, 0)])
    own_full = jnp.where(ci == 0, jnp.concatenate([basis, other], axis=1),
                         jnp.concatenate([other, basis], axis=1))

    geo = jnp.concatenate([positions, seglen[:, None, :], radius[:, None, :]], axis=1)
    geo_mine = lax.dynamic_slice_in_dim(geo, ci * half, half, axis=2)
    parts = split3(geo_mine)
    pad = jnp.zeros((blk, 1, half), jnp.bfloat16)
    same_msg = jnp.concatenate(
        [lax.dynamic_slice_in_dim(basis, ci * half, half, axis=2)] + list(parts) + [pad], axis=1)
    cross_msg = lax.dynamic_slice_in_dim(basis, (1 - ci) * half, half, axis=2)

    fwd = [(i, i + 1) for i in range(n_row - 1)]
    bwd = [(i + 1, i) for i in range(n_row - 1)]
    fwd_x = [(2 * i + c, 2 * (i + 1) + 1 - c) for i in range(n_row - 1) for c in range(2)]
    bwd_x = [(2 * (i + 1) + c, 2 * i + 1 - c) for i in range(n_row - 1) for c in range(2)]
    same_lo = lax.ppermute(same_msg, "row", fwd)
    same_hi = lax.ppermute(same_msg, "row", bwd)
    cross_lo = lax.ppermute(cross_msg, ("row", "col"), fwd_x)
    cross_hi = lax.ppermute(cross_msg, ("row", "col"), bwd_x)

    def panels_of(same, cross):
        mine = same[:, :half_p]
        return jnp.where(ci == 0, jnp.concatenate([mine, cross], axis=1),
                         jnp.concatenate([cross, mine], axis=1))

    def geo_of(same):
        g = same[:, half_p:half_p + 15].astype(jnp.float32)
        g = g[:, 0:5] + g[:, 5:10] + g[:, 10:15]
        return jnp.concatenate([g, jnp.zeros((blk, 3, half), jnp.float32)], axis=1)

    own_half = lax.dynamic_slice_in_dim(own_full, ci * half, half, axis=2)
    win_pan = jnp.concatenate([panels_of(same_lo, cross_lo), own_half,
                               panels_of(same_hi, cross_hi)], axis=0)
    geo_mine8 = jnp.concatenate([geo_mine, jnp.zeros((blk, 3, half), jnp.float32)], axis=1)
    win_geo = jnp.concatenate([geo_of(same_lo), geo_mine8, geo_of(same_hi)], axis=0)

    own_geo_t = jnp.transpose(
        jnp.concatenate([positions, radius[:, None, :], jnp.zeros((blk, 4, unk), jnp.float32)],
                        axis=1), (0, 2, 1))
    basis_s = (own_full.astype(jnp.float32) * seglen[:, None, :]).astype(jnp.bfloat16)

    own_ids = ri * blk + jnp.arange(blk, dtype=jnp.int32)
    off = jnp.clip(neighbours - own_ids[:, None] + blk, 0, 2 * blk)
    live = jnp.arange(near, dtype=jnp.int32)[None, :] < counts[:, None]
    sel = (off[:, :, None] == jnp.arange(n_off, dtype=jnp.int32)[None, None, :]) & live[:, :, None]
    needed = jnp.any(sel, axis=1).astype(jnp.int32).reshape(-1)

    kernel = functools.partial(pair_kernel, n_off=n_off, near=near, unk=unk, half=half, nb_p=nb_p)
    part = pl.pallas_call(
        kernel,
        out_shape=jax.ShapeDtypeStruct((2, blk, half_p, near * nb_p), jnp.float32),
        grid_spec=pltpu.PrefetchScalarGridSpec(
            num_scalar_prefetch=3,
            grid=(blk,),
            in_specs=[
                pl.BlockSpec((1, unk, 8), lambda b, *_: (b, 0, 0)),
                pl.BlockSpec((1, nb_p, unk), lambda b, *_: (b, 0, 0)),
                pl.BlockSpec((3 * blk, 8, half), lambda b, *_: (0, 0, 0)),
                pl.BlockSpec((3 * blk, nb_p, half), lambda b, *_: (0, 0, 0)),
            ],
            out_specs=pl.BlockSpec((2, 1, half_p, near * nb_p), lambda b, *_: (0, b, 0, 0)),
            scratch_shapes=[
                pltpu.VMEM((4, unk, LANES), jnp.float32),
                pltpu.VMEM((unk, half), jnp.bfloat16),
                pltpu.VMEM((n_off, nb_p, nb_p), jnp.float32),
            ],
        ),
        compiler_params=pltpu.CompilerParams(dimension_semantics=("arbitrary",)),
    )(needed, off.reshape(-1), live.astype(jnp.int32).reshape(-1), own_geo_t, basis_s,
      win_geo, win_pan)

    mine = lax.dynamic_index_in_dim(part, ci, 0, keepdims=False)
    theirs = lax.dynamic_index_in_dim(part, 1 - ci, 0, keepdims=False)
    return mine + lax.ppermute(theirs, "col", [(0, 1), (1, 0)])


def solution(mesh):
    placed = (
        P("row", "col", None),
        P("row", None, None),
        P("row", None),
        P("row", None),
        P("row", None),
        P("row"),
    )
    return jax.shard_map(
        on_device, mesh=mesh, in_specs=placed, out_specs=P("row", "col", None), check_vma=False
    )
```

```python
import functools

import jax
import jax.numpy as jnp
from jax import lax
from jax.experimental import pallas as pl
from jax.experimental.pallas import tpu as pltpu
from jax.sharding import PartitionSpec as P


CHUNK = 8
GROUP = 128
LANES = 128


def split3(x):
    hi = x.astype(jnp.bfloat16)
    r1 = x - hi.astype(jnp.float32)
    mid = r1.astype(jnp.bfloat16)
    lo = (r1 - mid.astype(jnp.float32)).astype(jnp.bfloat16)
    return hi, mid, lo


def pair_kernel(nb_ref, cnt_ref, pos_ref, len_ref, rad_ref, basis_ref, other_ref,
                slo_ref, shi_ref, xlo_ref, xhi_ref, out_ref,
                wgeo_ref, wpan_ref, bc_ref, bs_ref, cs_ref, ts_ref,
                *, blk, near, unk, half, half_p):
    b = pl.program_id(0)
    ci = lax.axis_index("col")
    ri = lax.axis_index("row")
    n_off = 2 * blk + 1
    n_tiles = half // LANES

    @pl.when(b == 0)
    def _setup():
        for side, sref in ((0, slo_ref), (2, shi_ref)):
            for w in range(blk):
                g = sref[w, half_p:half_p + 32, :].astype(jnp.float32)
                wgeo_ref[side * blk + w] = g[0:8] + g[8:16] + g[16:24]
        for hsel in range(2):
            @pl.when(ci == hsel)
            def _():
                lanes = slice(hsel * half, (hsel + 1) * half)
                for w in range(blk):
                    wgeo_ref[blk + w, 0:3, :] = pos_ref[w, :, lanes]
                    wgeo_ref[blk + w, 3:4, :] = len_ref[w:w + 1, lanes]
                    wgeo_ref[blk + w, 4:5, :] = rad_ref[w:w + 1, lanes]
                    first, second = (basis_ref, other_ref) if hsel == 0 else (other_ref, basis_ref)
                    wpan_ref[blk + w, 0:half_p, :] = first[w, :, lanes]
                    wpan_ref[blk + w, half_p:, :] = second[w, :, lanes]
                    for side, sref, xref in ((0, slo_ref, xlo_ref), (2, shi_ref, xhi_ref)):
                        mine = sref[w, 0:half_p, :]
                        cross = xref[w]
                        lo_rows, hi_rows = (mine, cross) if hsel == 0 else (cross, mine)
                        wpan_ref[side * blk + w, 0:half_p, :] = lo_rows
                        wpan_ref[side * blk + w, half_p:, :] = hi_rows

    rows = jnp.concatenate([pos_ref[b], rad_ref[pl.ds(b, 1), :],
                            jnp.zeros((LANES - 4, unk), jnp.float32)], axis=0)
    cols = jnp.transpose(rows)
    for c in range(4):
        bc_ref[c] = jnp.broadcast_to(cols[:, c:c + 1], (unk, LANES))
    s_row = len_ref[pl.ds(b, 1), :]
    bs_ref[0:half_p, :] = (basis_ref[b].astype(jnp.float32) * s_row).astype(jnp.bfloat16)
    bs_ref[half_p:, :] = (other_ref[b].astype(jnp.float32) * s_row).astype(jnp.bfloat16)

    gb = ri * blk + b
    cnt = cnt_ref[b]
    mask = jnp.int32(0)
    slots = []
    for k in range(near):
        o_k = jnp.clip(nb_ref[b, k] - gb + blk, 0, 2 * blk)
        live_k = k < cnt
        mask = mask | jnp.where(live_k, jnp.left_shift(jnp.int32(1), o_k), 0)
        slots.append((o_k, live_k))

    def per_offset(o, carry):
        @pl.when((jnp.right_shift(mask, o) & 1) != 0)
        def _():
            j = b + o
            wg = wgeo_ref[j]
            ys = [[jnp.broadcast_to(wg[c:c + 1, h * LANES:(h + 1) * LANES], (CHUNK, LANES))
                   for h in range(n_tiles)] for c in (0, 1, 2, 4)]
            acc = None
            for g in range(unk // GROUP):
                for mc in range(GROUP // CHUNK):
                    r = slice(g * GROUP + mc * CHUNK, g * GROUP + (mc + 1) * CHUNK)
                    xs = [bc_ref[c, r, :] for c in range(4)]
                    for h in range(n_tiles):
                        d0 = xs[0] - ys[0][h]
                        d1 = xs[1] - ys[1][h]
                        d2 = xs[2] - ys[2][h]
                        dd = d0 * d0 + d1 * d1 + d2 * d2 + xs[3] * ys[3][h]
                        cs_ref[r, h * LANES:(h + 1) * LANES] = lax.rsqrt(dd).astype(jnp.bfloat16)
                gs = slice(g * GROUP, (g + 1) * GROUP)
                part = jnp.dot(bs_ref[:, gs], cs_ref[gs, :], preferred_element_type=jnp.float32)
                acc = part if acc is None else acc + part
            left = (acc * wg[3:4, :]).astype(jnp.bfloat16)
            ts_ref[o] = lax.dot_general(left, wpan_ref[j], (((1,), (1,)), ((), ())),
                                        preferred_element_type=jnp.float32)

        return carry

    lax.fori_loop(0, n_off, per_offset, 0)

    nb_p = 2 * half_p
    for k, (o_k, live_k) in enumerate(slots):
        t = ts_ref[o_k]
        t = jnp.where(live_k, t, jnp.zeros_like(t))
        out_ref[0, 0, :, k * nb_p:(k + 1) * nb_p] = t[0:half_p]
        out_ref[1, 0, :, k * nb_p:(k + 1) * nb_p] = t[half_p:]


def on_device(basis, positions, seglen, radius, neighbours, counts):
    blk, half_p, unk = basis.shape
    nb_p = 2 * half_p
    half = unk // 2
    near = neighbours.shape[1]
    n_row = lax.axis_size("row")
    ci = lax.axis_index("col")

    other = lax.ppermute(basis, "col", [(0, 1), (1, 0)])

    geo = jnp.concatenate([positions, seglen[:, None, :], radius[:, None, :]], axis=1)
    geo_mine = lax.dynamic_slice_in_dim(geo, ci * half, half, axis=2)
    z3 = jnp.zeros((blk, 3, half), jnp.bfloat16)
    hi, mid, lo = split3(geo_mine)
    same_msg = jnp.concatenate(
        [lax.dynamic_slice_in_dim(basis, ci * half, half, axis=2), hi, z3, mid, z3, lo, z3,
         jnp.zeros((blk, 8, half), jnp.bfloat16)], axis=1)
    cross_msg = lax.dynamic_slice_in_dim(basis, (1 - ci) * half, half, axis=2)

    fwd = [(i, i + 1) for i in range(n_row - 1)]
    bwd = [(i + 1, i) for i in range(n_row - 1)]
    fwd_x = [(2 * i + c, 2 * (i + 1) + 1 - c) for i in range(n_row - 1) for c in range(2)]
    bwd_x = [(2 * (i + 1) + c, 2 * i + 1 - c) for i in range(n_row - 1) for c in range(2)]
    same_lo = lax.ppermute(same_msg, "row", fwd)
    same_hi = lax.ppermute(same_msg, "row", bwd)
    cross_lo = lax.ppermute(cross_msg, ("row", "col"), fwd_x)
    cross_hi = lax.ppermute(cross_msg, ("row", "col"), bwd_x)

    kernel = functools.partial(pair_kernel, blk=blk, near=near, unk=unk, half=half,
                               half_p=half_p)
    n_off = 2 * blk + 1

    def whole(shape):
        return pl.BlockSpec(shape, lambda b, *_: (0,) * len(shape))

    part = pl.pallas_call(
        kernel,
        out_shape=jax.ShapeDtypeStruct((2, blk, half_p, near * nb_p), jnp.float32),
        grid_spec=pltpu.PrefetchScalarGridSpec(
            num_scalar_prefetch=2,
            grid=(blk,),
            in_specs=[
                whole(positions.shape), whole(seglen.shape), whole(radius.shape),
                whole(basis.shape), whole(other.shape),
                whole(same_lo.shape), whole(same_hi.shape),
                whole(cross_lo.shape), whole(cross_hi.shape),
            ],
            out_specs=pl.BlockSpec((2, 1, half_p, near * nb_p), lambda b, *_: (0, b, 0, 0)),
            scratch_shapes=[
                pltpu.VMEM((3 * blk, 8, half), jnp.float32),
                pltpu.VMEM((3 * blk, nb_p, half), jnp.bfloat16),
                pltpu.VMEM((4, unk, LANES), jnp.float32),
                pltpu.VMEM((nb_p, unk), jnp.bfloat16),
                pltpu.VMEM((unk, half), jnp.bfloat16),
                pltpu.VMEM((n_off, nb_p, nb_p), jnp.float32),
            ],
        ),
        compiler_params=pltpu.CompilerParams(dimension_semantics=("arbitrary",)),
    )(neighbours, counts, positions, seglen, radius, basis, other,
      same_lo, same_hi, cross_lo, cross_hi)

    return part[0] + lax.ppermute(part[1], "col", [(0, 1), (1, 0)])


def solution(mesh):
    placed = (
        P("row", "col", None),
        P("row", None, None),
        P("row", None),
        P("row", None),
        P("row", None),
        P("row"),
    )
    return jax.shard_map(
        on_device, mesh=mesh, in_specs=placed, out_specs=P("row", "col", None), check_vma=False
    )
```

```python
import functools

import jax
import jax.numpy as jnp
from jax import lax
from jax.experimental import pallas as pl
from jax.experimental.pallas import tpu as pltpu
from jax.sharding import PartitionSpec as P


CHUNK = 8
GROUP = 128
LANES = 128


def split3(x):
    hi = x.astype(jnp.bfloat16)
    r1 = x - hi.astype(jnp.float32)
    mid = r1.astype(jnp.bfloat16)
    lo = (r1 - mid.astype(jnp.float32)).astype(jnp.bfloat16)
    return hi, mid, lo


def pair_kernel(nb_ref, cnt_ref, pos_ref, len_ref, rad_ref, basis_ref, other_ref,
                slo_ref, shi_ref, xlo_ref, xhi_ref, out_ref,
                wgeo_ref, wgt_ref, wpan_ref, bs_ref, cs_ref, ts_ref,
                *, blk, near, unk, half, half_p):
    b = pl.program_id(0)
    ci = lax.axis_index("col")
    ri = lax.axis_index("row")
    n_off = 2 * blk + 1
    m_tiles = unk // LANES

    @pl.when(b == 0)
    def _setup():
        for side, sref in ((0, slo_ref), (2, shi_ref)):
            for w in range(blk):
                g = sref[w, half_p:half_p + 32, :].astype(jnp.float32)
                wgeo_ref[side * blk + w] = g[0:8] + g[8:16] + g[16:24]
        for hsel in range(2):
            @pl.when(ci == hsel)
            def _():
                lanes = slice(hsel * half, (hsel + 1) * half)
                for w in range(blk):
                    wgeo_ref[blk + w, 0:3, :] = pos_ref[w, :, lanes]
                    wgeo_ref[blk + w, 3:4, :] = len_ref[w:w + 1, lanes]
                    wgeo_ref[blk + w, 4:5, :] = rad_ref[w:w + 1, lanes]
                    wgeo_ref[blk + w, 5:8, :] = jnp.zeros((3, half), jnp.float32)
                    first, second = (basis_ref, other_ref) if hsel == 0 else (other_ref, basis_ref)
                    wpan_ref[blk + w, 0:half_p, :] = first[w, :, lanes]
                    wpan_ref[blk + w, half_p:, :] = second[w, :, lanes]
                    for side, sref, xref in ((0, slo_ref, xlo_ref), (2, shi_ref, xhi_ref)):
                        mine = sref[w, 0:half_p, :]
                        cross = xref[w]
                        lo_rows, hi_rows = (mine, cross) if hsel == 0 else (cross, mine)
                        wpan_ref[side * blk + w, 0:half_p, :] = lo_rows
                        wpan_ref[side * blk + w, half_p:, :] = hi_rows
        for w in range(3 * blk):
            rows = jnp.concatenate([wgeo_ref[w], jnp.zeros((LANES - 8, half), jnp.float32)], axis=0)
            wgt_ref[w] = jnp.transpose(rows)

    own = [jnp.broadcast_to(pos_ref[b, c:c + 1, :], (CHUNK, unk)) for c in range(3)]
    own.append(jnp.broadcast_to(rad_ref[pl.ds(b, 1), :], (CHUNK, unk)))
    s_row = len_ref[pl.ds(b, 1), :]
    bs_ref[0:half_p, :] = (basis_ref[b].astype(jnp.float32) * s_row).astype(jnp.bfloat16)
    bs_ref[half_p:, :] = (other_ref[b].astype(jnp.float32) * s_row).astype(jnp.bfloat16)

    gb = ri * blk + b
    cnt = cnt_ref[b]
    mask = jnp.int32(0)
    slots = []
    for k in range(near):
        o_k = jnp.clip(nb_ref[b, k] - gb + blk, 0, 2 * blk)
        live_k = k < cnt
        mask = mask | jnp.where(live_k, jnp.left_shift(jnp.int32(1), o_k), 0)
        slots.append((o_k, live_k))

    def per_offset(o, carry):
        @pl.when((jnp.right_shift(mask, o) & 1) != 0)
        def _():
            j = b + o
            lefts = []
            for g in range(half // GROUP):
                for nc in range(GROUP // CHUNK):
                    r = slice(g * GROUP + nc * CHUNK, g * GROUP + (nc + 1) * CHUNK)
                    yv = wgt_ref[j, r, :]
                    ys = [jnp.broadcast_to(yv[:, c:c + 1], (CHUNK, LANES)) for c in (0, 1, 2, 4)]
                    for h in range(m_tiles):
                        lanes = slice(h * LANES, (h + 1) * LANES)
                        d0 = own[0][:, lanes] - ys[0]
                        d1 = own[1][:, lanes] - ys[1]
                        d2 = own[2][:, lanes] - ys[2]
                        dd = d0 * d0 + d1 * d1 + d2 * d2 + own[3][:, lanes] * ys[3]
                        cs_ref[r, lanes] = lax.rsqrt(dd).astype(jnp.bfloat16)
                gs = slice(g * GROUP, (g + 1) * GROUP)
                lefts.append(lax.dot_general(bs_ref[...], cs_ref[gs, :], (((1,), (1,)), ((), ())),
                                             preferred_element_type=jnp.float32))
            left = jnp.concatenate(lefts, axis=1)
            left = (left * wgeo_ref[j, 3:4, :]).astype(jnp.bfloat16)
            ts_ref[o] = lax.dot_general(left, wpan_ref[j], (((1,), (1,)), ((), ())),
                                        preferred_element_type=jnp.float32)

        return carry

    lax.fori_loop(0, n_off, per_offset, 0)

    nb_p = 2 * half_p
    for k, (o_k, live_k) in enumerate(slots):
        t = ts_ref[o_k]
        t = jnp.where(live_k, t, jnp.zeros_like(t))
        out_ref[0, 0, :, k * nb_p:(k + 1) * nb_p] = t[0:half_p]
        out_ref[1, 0, :, k * nb_p:(k + 1) * nb_p] = t[half_p:]


def on_device(basis, positions, seglen, radius, neighbours, counts):
    blk, half_p, unk = basis.shape
    nb_p = 2 * half_p
    half = unk // 2
    near = neighbours.shape[1]
    n_row = lax.axis_size("row")
    ci = lax.axis_index("col")

    other = lax.ppermute(basis, "col", [(0, 1), (1, 0)])

    geo = jnp.concatenate([positions, seglen[:, None, :], radius[:, None, :]], axis=1)
    geo_mine = lax.dynamic_slice_in_dim(geo, ci * half, half, axis=2)
    z3 = jnp.zeros((blk, 3, half), jnp.bfloat16)
    hi, mid, lo = split3(geo_mine)
    same_msg = jnp.concatenate(
        [lax.dynamic_slice_in_dim(basis, ci * half, half, axis=2), hi, z3, mid, z3, lo, z3,
         jnp.zeros((blk, 8, half), jnp.bfloat16)], axis=1)
    cross_msg = lax.dynamic_slice_in_dim(basis, (1 - ci) * half, half, axis=2)

    fwd = [(i, i + 1) for i in range(n_row - 1)]
    bwd = [(i + 1, i) for i in range(n_row - 1)]
    fwd_x = [(2 * i + c, 2 * (i + 1) + 1 - c) for i in range(n_row - 1) for c in range(2)]
    bwd_x = [(2 * (i + 1) + c, 2 * i + 1 - c) for i in range(n_row - 1) for c in range(2)]
    same_lo = lax.ppermute(same_msg, "row", fwd)
    same_hi = lax.ppermute(same_msg, "row", bwd)
    cross_lo = lax.ppermute(cross_msg, ("row", "col"), fwd_x)
    cross_hi = lax.ppermute(cross_msg, ("row", "col"), bwd_x)

    kernel = functools.partial(pair_kernel, blk=blk, near=near, unk=unk, half=half,
                               half_p=half_p)
    n_off = 2 * blk + 1

    def whole(shape):
        return pl.BlockSpec(shape, lambda b, *_: (0,) * len(shape))

    part = pl.pallas_call(
        kernel,
        out_shape=jax.ShapeDtypeStruct((2, blk, half_p, near * nb_p), jnp.float32),
        grid_spec=pltpu.PrefetchScalarGridSpec(
            num_scalar_prefetch=2,
            grid=(blk,),
            in_specs=[
                whole(positions.shape), whole(seglen.shape), whole(radius.shape),
                whole(basis.shape), whole(other.shape),
                whole(same_lo.shape), whole(same_hi.shape),
                whole(cross_lo.shape), whole(cross_hi.shape),
            ],
            out_specs=pl.BlockSpec((2, 1, half_p, near * nb_p), lambda b, *_: (0, b, 0, 0)),
            scratch_shapes=[
                pltpu.VMEM((3 * blk, 8, half), jnp.float32),
                pltpu.VMEM((3 * blk, half, LANES), jnp.float32),
                pltpu.VMEM((3 * blk, nb_p, half), jnp.bfloat16),
                pltpu.VMEM((nb_p, unk), jnp.bfloat16),
                pltpu.VMEM((half, unk), jnp.bfloat16),
                pltpu.VMEM((n_off, nb_p, nb_p), jnp.float32),
            ],
        ),
        compiler_params=pltpu.CompilerParams(dimension_semantics=("arbitrary",)),
    )(neighbours, counts, positions, seglen, radius, basis, other,
      same_lo, same_hi, cross_lo, cross_hi)

    return part[0] + lax.ppermute(part[1], "col", [(0, 1), (1, 0)])


def solution(mesh):
    placed = (
        P("row", "col", None),
        P("row", None, None),
        P("row", None),
        P("row", None),
        P("row", None),
        P("row"),
    )
    return jax.shard_map(
        on_device, mesh=mesh, in_specs=placed, out_specs=P("row", "col", None), check_vma=False
    )
```

```python
import functools

import jax
import jax.numpy as jnp
from jax import lax
from jax.experimental import pallas as pl
from jax.experimental.pallas import tpu as pltpu
from jax.sharding import PartitionSpec as P


CHUNK = 8
GROUP = 128
LANES = 128


def split3(x):
    hi = x.astype(jnp.bfloat16)
    r1 = x - hi.astype(jnp.float32)
    mid = r1.astype(jnp.bfloat16)
    lo = (r1 - mid.astype(jnp.float32)).astype(jnp.bfloat16)
    return hi, mid, lo


def slot_table(nb_ref, cnt_ref, b, blk, near):
    gb = lax.axis_index("row") * blk + b
    cnt = cnt_ref[b]
    mask = jnp.int32(0)
    slots = []
    for k in range(near):
        o_k = jnp.clip(nb_ref[b, k] - gb + blk, 0, 2 * blk)
        live_k = k < cnt
        mask = mask | jnp.where(live_k, jnp.left_shift(jnp.int32(1), o_k), 0)
        slots.append((o_k, live_k))
    return mask, slots


def scaled_basis(bs_ref, basis_ref, other_ref, len_ref, b, half_p):
    s_row = len_ref[pl.ds(b, 1), :]
    bs_ref[0:half_p, :] = (basis_ref[b].astype(jnp.float32) * s_row).astype(jnp.bfloat16)
    bs_ref[half_p:, :] = (other_ref[b].astype(jnp.float32) * s_row).astype(jnp.bfloat16)


def pair_tile(bc_ref, bs_ref, cs_ref, wg, pan, unk, half):
    n_tiles = half // LANES
    ys = [[jnp.broadcast_to(wg[c:c + 1, h * LANES:(h + 1) * LANES], (CHUNK, LANES))
           for h in range(n_tiles)] for c in (0, 1, 2, 4)]
    acc = None
    for g in range(unk // GROUP):
        for mc in range(GROUP // CHUNK):
            r = slice(g * GROUP + mc * CHUNK, g * GROUP + (mc + 1) * CHUNK)
            xs = [bc_ref[c, r, :] for c in range(4)]
            for h in range(n_tiles):
                d0 = xs[0] - ys[0][h]
                d1 = xs[1] - ys[1][h]
                d2 = xs[2] - ys[2][h]
                dd = d0 * d0 + d1 * d1 + d2 * d2 + xs[3] * ys[3][h]
                cs_ref[r, h * LANES:(h + 1) * LANES] = lax.rsqrt(dd).astype(jnp.bfloat16)
        gs = slice(g * GROUP, (g + 1) * GROUP)
        part = jnp.dot(bs_ref[:, gs], cs_ref[gs, :], preferred_element_type=jnp.float32)
        acc = part if acc is None else acc + part
    left = (acc * wg[3:4, :]).astype(jnp.bfloat16)
    return lax.dot_general(left, pan, (((1,), (1,)), ((), ())), preferred_element_type=jnp.float32)


def own_kernel(nb_ref, cnt_ref, pos_ref, len_ref, rad_ref, basis_ref, other_ref,
               out_ref, bc_ref, wgeo_ref, wpan_ref, bs_ref, cs_ref, ts_ref,
               *, blk, near, unk, half, half_p):
    b = pl.program_id(0)
    ci = lax.axis_index("col")
    n_off = 2 * blk + 1

    @pl.when(b == 0)
    def _setup():
        for hsel in range(2):
            @pl.when(ci == hsel)
            def _():
                lanes = slice(hsel * half, (hsel + 1) * half)
                for w in range(blk):
                    wgeo_ref[w, 0:3, :] = pos_ref[w, :, lanes]
                    wgeo_ref[w, 3:4, :] = len_ref[w:w + 1, lanes]
                    wgeo_ref[w, 4:5, :] = rad_ref[w:w + 1, lanes]
                    first, second = (basis_ref, other_ref) if hsel == 0 else (other_ref, basis_ref)
                    wpan_ref[w, 0:half_p, :] = first[w, :, lanes]
                    wpan_ref[w, half_p:, :] = second[w, :, lanes]

    rows = jnp.concatenate([pos_ref[b], rad_ref[pl.ds(b, 1), :],
                            jnp.zeros((LANES - 4, unk), jnp.float32)], axis=0)
    cols = jnp.transpose(rows)
    for c in range(4):
        bc_ref[0, c] = jnp.broadcast_to(cols[:, c:c + 1], (unk, LANES))
    scaled_basis(bs_ref, basis_ref, other_ref, len_ref, b, half_p)
    mask, slots = slot_table(nb_ref, cnt_ref, b, blk, near)

    def per_offset(o, carry):
        j = b + o
        on_dev = (j >= blk) & (j < 2 * blk)

        @pl.when(on_dev & ((jnp.right_shift(mask, o) & 1) != 0))
        def _():
            w = j - blk
            ts_ref[o] = pair_tile(bc_ref.at[0], bs_ref, cs_ref, wgeo_ref[w], wpan_ref[w], unk, half)

        return carry

    lax.fori_loop(0, n_off, per_offset, 0)

    nb_p = 2 * half_p
    for k, (o_k, live_k) in enumerate(slots):
        t = ts_ref[o_k]
        j = b + o_k
        use = live_k & (j >= blk) & (j < 2 * blk)
        t = jnp.where(use, t, jnp.zeros_like(t))
        out_ref[0, 0, :, k * nb_p:(k + 1) * nb_p] = t[0:half_p]
        out_ref[1, 0, :, k * nb_p:(k + 1) * nb_p] = t[half_p:]


def halo_kernel(nb_ref, cnt_ref, bc_ref, prev_ref, len_ref, basis_ref, other_ref,
                slo_ref, shi_ref, xlo_ref, xhi_ref, out_ref,
                wgeo_ref, wpan_ref, bs_ref, cs_ref, ts_ref,
                *, blk, near, unk, half, half_p):
    b = pl.program_id(0)
    ci = lax.axis_index("col")
    n_off = 2 * blk + 1

    @pl.when(b == 0)
    def _setup():
        for side, sref in ((0, slo_ref), (1, shi_ref)):
            for w in range(blk):
                g = sref[w, half_p:half_p + 32, :].astype(jnp.float32)
                wgeo_ref[side * blk + w] = g[0:8] + g[8:16] + g[16:24]
        for hsel in range(2):
            @pl.when(ci == hsel)
            def _():
                for w in range(blk):
                    for side, sref, xref in ((0, slo_ref, xlo_ref), (1, shi_ref, xhi_ref)):
                        mine = sref[w, 0:half_p, :]
                        cross = xref[w]
                        lo_rows, hi_rows = (mine, cross) if hsel == 0 else (cross, mine)
                        wpan_ref[side * blk + w, 0:half_p, :] = lo_rows
                        wpan_ref[side * blk + w, half_p:, :] = hi_rows

    scaled_basis(bs_ref, basis_ref, other_ref, len_ref, b, half_p)
    mask, slots = slot_table(nb_ref, cnt_ref, b, blk, near)

    def per_offset(o, carry):
        j = b + o
        off_dev = (j < blk) | (j >= 2 * blk)

        @pl.when(off_dev & ((jnp.right_shift(mask, o) & 1) != 0))
        def _():
            w = jnp.where(j < blk, j, j - blk)
            ts_ref[o] = pair_tile(bc_ref.at[0], bs_ref, cs_ref, wgeo_ref[w], wpan_ref[w], unk, half)

        return carry

    lax.fori_loop(0, n_off, per_offset, 0)

    nb_p = 2 * half_p
    for k, (o_k, live_k) in enumerate(slots):
        t = ts_ref[o_k]
        j = b + o_k
        use = live_k & ((j < blk) | (j >= 2 * blk))
        cols = slice(k * nb_p, (k + 1) * nb_p)
        out_ref[0, 0, :, cols] = jnp.where(use, t[0:half_p], prev_ref[0, 0, :, cols])
        out_ref[1, 0, :, cols] = jnp.where(use, t[half_p:], prev_ref[1, 0, :, cols])


def on_device(basis, positions, seglen, radius, neighbours, counts):
    blk, half_p, unk = basis.shape
    nb_p = 2 * half_p
    half = unk // 2
    near = neighbours.shape[1]
    n_row = lax.axis_size("row")
    n_off = 2 * blk + 1
    ci = lax.axis_index("col")

    other = lax.ppermute(basis, "col", [(0, 1), (1, 0)])

    geo = jnp.concatenate([positions, seglen[:, None, :], radius[:, None, :]], axis=1)
    geo_mine = lax.dynamic_slice_in_dim(geo, ci * half, half, axis=2)
    z3 = jnp.zeros((blk, 3, half), jnp.bfloat16)
    hi, mid, lo = split3(geo_mine)
    same_msg = jnp.concatenate(
        [lax.dynamic_slice_in_dim(basis, ci * half, half, axis=2), hi, z3, mid, z3, lo, z3,
         jnp.zeros((blk, 8, half), jnp.bfloat16)], axis=1)
    cross_msg = lax.dynamic_slice_in_dim(basis, (1 - ci) * half, half, axis=2)

    fwd = [(i, i + 1) for i in range(n_row - 1)]
    bwd = [(i + 1, i) for i in range(n_row - 1)]
    fwd_x = [(2 * i + c, 2 * (i + 1) + 1 - c) for i in range(n_row - 1) for c in range(2)]
    bwd_x = [(2 * (i + 1) + c, 2 * i + 1 - c) for i in range(n_row - 1) for c in range(2)]
    same_lo = lax.ppermute(same_msg, "row", fwd)
    same_hi = lax.ppermute(same_msg, "row", bwd)
    cross_lo = lax.ppermute(cross_msg, ("row", "col"), fwd_x)
    cross_hi = lax.ppermute(cross_msg, ("row", "col"), bwd_x)

    def whole(shape):
        return pl.BlockSpec(shape, lambda b, *_: (0,) * len(shape))

    out_shape = jax.ShapeDtypeStruct((2, blk, half_p, near * nb_p), jnp.float32)
    out_spec = pl.BlockSpec((2, 1, half_p, near * nb_p), lambda b, *_: (0, b, 0, 0))
    bc_shape = jax.ShapeDtypeStruct((blk, 4, unk, LANES), jnp.float32)
    bc_spec = pl.BlockSpec((1, 4, unk, LANES), lambda b, *_: (b, 0, 0, 0))
    sizes = dict(blk=blk, near=near, unk=unk, half=half, half_p=half_p)
    work = [
        pltpu.VMEM((nb_p, unk), jnp.bfloat16),
        pltpu.VMEM((unk, half), jnp.bfloat16),
        pltpu.VMEM((n_off, nb_p, nb_p), jnp.float32),
    ]
    params = pltpu.CompilerParams(dimension_semantics=("arbitrary",))

    part_own, bc = pl.pallas_call(
        functools.partial(own_kernel, **sizes),
        out_shape=(out_shape, bc_shape),
        grid_spec=pltpu.PrefetchScalarGridSpec(
            num_scalar_prefetch=2,
            grid=(blk,),
            in_specs=[
                whole(positions.shape), whole(seglen.shape), whole(radius.shape),
                whole(basis.shape), whole(other.shape),
            ],
            out_specs=(out_spec, bc_spec),
            scratch_shapes=[
                pltpu.VMEM((blk, 8, half), jnp.float32),
                pltpu.VMEM((blk, nb_p, half), jnp.bfloat16),
            ] + work,
        ),
        compiler_params=params,
    )(neighbours, counts, positions, seglen, radius, basis, other)

    part = pl.pallas_call(
        functools.partial(halo_kernel, **sizes),
        out_shape=out_shape,
        grid_spec=pltpu.PrefetchScalarGridSpec(
            num_scalar_prefetch=2,
            grid=(blk,),
            in_specs=[
                bc_spec, out_spec, whole(seglen.shape), whole(basis.shape), whole(other.shape),
                whole(same_lo.shape), whole(same_hi.shape),
                whole(cross_lo.shape), whole(cross_hi.shape),
            ],
            out_specs=out_spec,
            scratch_shapes=[
                pltpu.VMEM((2 * blk, 8, half), jnp.float32),
                pltpu.VMEM((2 * blk, nb_p, half), jnp.bfloat16),
            ] + work,
        ),
        compiler_params=params,
    )(neighbours, counts, bc, part_own, seglen, basis, other, same_lo, same_hi, cross_lo, cross_hi)

    return part[0] + lax.ppermute(part[1], "col", [(0, 1), (1, 0)])


def solution(mesh):
    placed = (
        P("row", "col", None),
        P("row", None, None),
        P("row", None),
        P("row", None),
        P("row", None),
        P("row"),
    )
    return jax.shard_map(
        on_device, mesh=mesh, in_specs=placed, out_specs=P("row", "col", None), check_vma=False
    )
```

```python
import functools

import jax
import jax.numpy as jnp
from jax import lax
from jax.experimental import pallas as pl
from jax.experimental.pallas import tpu as pltpu
from jax.sharding import PartitionSpec as P


CHUNK = 8
GROUP = 128
LANES = 128


def split3(x):
    hi = x.astype(jnp.bfloat16)
    r1 = x - hi.astype(jnp.float32)
    mid = r1.astype(jnp.bfloat16)
    lo = (r1 - mid.astype(jnp.float32)).astype(jnp.bfloat16)
    return hi, mid, lo


def pair_kernel(nb_ref, cnt_ref, pos_ref, len_ref, rad_ref, basis_ref, other_ref,
                slo_ref, shi_ref, xlo_ref, xhi_ref, mine_ref, theirs_ref,
                wgeo_ref, wpan_ref, bc_ref, bs_ref, cs_ref, ts_ref,
                *, blk, near, unk, half, half_p):
    b = pl.program_id(0)
    ci = lax.axis_index("col")
    ri = lax.axis_index("row")
    n_off = 2 * blk + 1
    n_tiles = half // LANES

    @pl.when(b == 0)
    def _setup():
        for side, sref in ((0, slo_ref), (2, shi_ref)):
            for w in range(blk):
                g = sref[w, half_p:half_p + 16, :].astype(jnp.float32)
                wgeo_ref[side * blk + w, 0:5, :] = g[0:5] + g[5:10] + g[10:15]
        for hsel in range(2):
            @pl.when(ci == hsel)
            def _():
                lanes = slice(hsel * half, (hsel + 1) * half)
                for w in range(blk):
                    wgeo_ref[blk + w, 0:3, :] = pos_ref[w, :, lanes]
                    wgeo_ref[blk + w, 3:4, :] = len_ref[w:w + 1, lanes]
                    wgeo_ref[blk + w, 4:5, :] = rad_ref[w:w + 1, lanes]
                    first, second = (basis_ref, other_ref) if hsel == 0 else (other_ref, basis_ref)
                    wpan_ref[blk + w, 0:half_p, :] = first[w, :, lanes]
                    wpan_ref[blk + w, half_p:, :] = second[w, :, lanes]
                    for side, sref, xref in ((0, slo_ref, xlo_ref), (2, shi_ref, xhi_ref)):
                        mine = sref[w, 0:half_p, :]
                        cross = xref[w]
                        lo_rows, hi_rows = (mine, cross) if hsel == 0 else (cross, mine)
                        wpan_ref[side * blk + w, 0:half_p, :] = lo_rows
                        wpan_ref[side * blk + w, half_p:, :] = hi_rows

    rows = jnp.concatenate([pos_ref[b], rad_ref[pl.ds(b, 1), :],
                            jnp.zeros((LANES - 4, unk), jnp.float32)], axis=0)
    cols = jnp.transpose(rows)
    for c in range(4):
        bc_ref[c] = jnp.broadcast_to(cols[:, c:c + 1], (unk, LANES))
    s_row = len_ref[pl.ds(b, 1), :]
    bs_ref[0:half_p, :] = (basis_ref[b].astype(jnp.float32) * s_row).astype(jnp.bfloat16)
    bs_ref[half_p:, :] = (other_ref[b].astype(jnp.float32) * s_row).astype(jnp.bfloat16)

    gb = ri * blk + b
    cnt = cnt_ref[b]
    mask = jnp.int32(0)
    slots = []
    for k in range(near):
        o_k = jnp.clip(nb_ref[b, k] - gb + blk, 0, 2 * blk)
        live_k = k < cnt
        mask = mask | jnp.where(live_k, jnp.left_shift(jnp.int32(1), o_k), 0)
        slots.append((o_k, live_k))

    def per_offset(o, carry):
        @pl.when((jnp.right_shift(mask, o) & 1) != 0)
        def _():
            j = b + o
            wg = wgeo_ref[j]
            ys = [[jnp.broadcast_to(wg[c:c + 1, h * LANES:(h + 1) * LANES], (CHUNK, LANES))
                   for h in range(n_tiles)] for c in (0, 1, 2, 4)]
            acc = None
            for g in range(unk // GROUP):
                for mc in range(GROUP // CHUNK):
                    r = slice(g * GROUP + mc * CHUNK, g * GROUP + (mc + 1) * CHUNK)
                    xs = [bc_ref[c, r, :] for c in range(4)]
                    for h in range(n_tiles):
                        d0 = xs[0] - ys[0][h]
                        d1 = xs[1] - ys[1][h]
                        d2 = xs[2] - ys[2][h]
                        dd = d0 * d0 + d1 * d1 + d2 * d2 + xs[3] * ys[3][h]
                        cs_ref[r, h * LANES:(h + 1) * LANES] = lax.rsqrt(dd).astype(jnp.bfloat16)
                gs = slice(g * GROUP, (g + 1) * GROUP)
                part = jnp.dot(bs_ref[:, gs], cs_ref[gs, :], preferred_element_type=jnp.float32)
                acc = part if acc is None else acc + part
            left = (acc * wg[3:4, :]).astype(jnp.bfloat16)
            ts_ref[o] = lax.dot_general(left, wpan_ref[j], (((1,), (1,)), ((), ())),
                                        preferred_element_type=jnp.float32)

        return carry

    lax.fori_loop(0, n_off, per_offset, 0)

    nb_p = 2 * half_p
    for k, (o_k, live_k) in enumerate(slots):
        t = ts_ref[o_k]
        t = jnp.where(live_k, t, jnp.zeros_like(t))
        mine_ref[0, :, k * nb_p:(k + 1) * nb_p] = t[0:half_p]
        theirs_ref[0, :, k * nb_p:(k + 1) * nb_p] = t[half_p:]


def on_device(basis, positions, seglen, radius, neighbours, counts):
    blk, half_p, unk = basis.shape
    nb_p = 2 * half_p
    half = unk // 2
    near = neighbours.shape[1]
    n_row = lax.axis_size("row")
    ci = lax.axis_index("col")

    other = lax.ppermute(basis, "col", [(0, 1), (1, 0)])

    geo = jnp.concatenate([positions, seglen[:, None, :], radius[:, None, :]], axis=1)
    geo_mine = lax.dynamic_slice_in_dim(geo, ci * half, half, axis=2)
    hi, mid, lo = split3(geo_mine)
    same_msg = jnp.concatenate(
        [lax.dynamic_slice_in_dim(basis, ci * half, half, axis=2), hi, mid, lo,
         jnp.zeros((blk, 1, half), jnp.bfloat16)], axis=1)
    cross_msg = lax.dynamic_slice_in_dim(basis, (1 - ci) * half, half, axis=2)

    fwd = [(i, i + 1) for i in range(n_row - 1)]
    bwd = [(i + 1, i) for i in range(n_row - 1)]
    fwd_x = [(2 * i + c, 2 * (i + 1) + 1 - c) for i in range(n_row - 1) for c in range(2)]
    bwd_x = [(2 * (i + 1) + c, 2 * i + 1 - c) for i in range(n_row - 1) for c in range(2)]
    same_lo = lax.ppermute(same_msg, "row", fwd)
    same_hi = lax.ppermute(same_msg, "row", bwd)
    cross_lo = lax.ppermute(cross_msg, ("row", "col"), fwd_x)
    cross_hi = lax.ppermute(cross_msg, ("row", "col"), bwd_x)

    kernel = functools.partial(pair_kernel, blk=blk, near=near, unk=unk, half=half,
                               half_p=half_p)
    n_off = 2 * blk + 1

    def whole(shape):
        return pl.BlockSpec(shape, lambda b, *_: (0,) * len(shape))

    mine, theirs = pl.pallas_call(
        kernel,
        out_shape=(jax.ShapeDtypeStruct((blk, half_p, near * nb_p), jnp.float32),) * 2,
        grid_spec=pltpu.PrefetchScalarGridSpec(
            num_scalar_prefetch=2,
            grid=(blk,),
            in_specs=[
                whole(positions.shape), whole(seglen.shape), whole(radius.shape),
                whole(basis.shape), whole(other.shape),
                whole(same_lo.shape), whole(same_hi.shape),
                whole(cross_lo.shape), whole(cross_hi.shape),
            ],
            out_specs=(pl.BlockSpec((1, half_p, near * nb_p), lambda b, *_: (b, 0, 0)),) * 2,
            scratch_shapes=[
                pltpu.VMEM((3 * blk, 8, half), jnp.float32),
                pltpu.VMEM((3 * blk, nb_p, half), jnp.bfloat16),
                pltpu.VMEM((4, unk, LANES), jnp.float32),
                pltpu.VMEM((nb_p, unk), jnp.bfloat16),
                pltpu.VMEM((unk, half), jnp.bfloat16),
                pltpu.VMEM((n_off, nb_p, nb_p), jnp.float32),
            ],
        ),
        compiler_params=pltpu.CompilerParams(dimension_semantics=("arbitrary",)),
    )(neighbours, counts, positions, seglen, radius, basis, other,
      same_lo, same_hi, cross_lo, cross_hi)

    return mine + lax.ppermute(theirs, "col", [(0, 1), (1, 0)])


def solution(mesh):
    placed = (
        P("row", "col", None),
        P("row", None, None),
        P("row", None),
        P("row", None),
        P("row", None),
        P("row"),
    )
    return jax.shard_map(
        on_device, mesh=mesh, in_specs=placed, out_specs=P("row", "col", None), check_vma=False
    )
```

```python
import functools

import jax
import jax.numpy as jnp
from jax import lax
from jax.experimental import pallas as pl
from jax.experimental.pallas import tpu as pltpu
from jax.sharding import PartitionSpec as P


CHUNK = 8
GROUP = 128
LANES = 128


def split3(x):
    hi = x.astype(jnp.bfloat16)
    r1 = x - hi.astype(jnp.float32)
    mid = r1.astype(jnp.bfloat16)
    lo = (r1 - mid.astype(jnp.float32)).astype(jnp.bfloat16)
    return hi, mid, lo


def pair_kernel(nb_ref, cnt_ref, pos_ref, len_ref, rad_ref, basis_ref, other_ref,
                slo_ref, shi_ref, xlo_ref, xhi_ref, mine_ref, theirs_ref,
                wgeo_ref, wpan_ref, bc_ref, bs_ref, cs0_ref, cs1_ref, ts_ref, lst_ref,
                *, blk, near, unk, half, half_p):
    b = pl.program_id(0)
    ci = lax.axis_index("col")
    ri = lax.axis_index("row")
    n_off = 2 * blk + 1
    n_tiles = half // LANES

    @pl.when(b == 0)
    def _setup():
        for side, sref in ((0, slo_ref), (2, shi_ref)):
            for w in range(blk):
                g = sref[w, half_p:half_p + 16, :].astype(jnp.float32)
                wgeo_ref[side * blk + w, 0:5, :] = g[0:5] + g[5:10] + g[10:15]
        for hsel in range(2):
            @pl.when(ci == hsel)
            def _():
                lanes = slice(hsel * half, (hsel + 1) * half)
                for w in range(blk):
                    wgeo_ref[blk + w, 0:3, :] = pos_ref[w, :, lanes]
                    wgeo_ref[blk + w, 3:4, :] = len_ref[w:w + 1, lanes]
                    wgeo_ref[blk + w, 4:5, :] = rad_ref[w:w + 1, lanes]
                    first, second = (basis_ref, other_ref) if hsel == 0 else (other_ref, basis_ref)
                    wpan_ref[blk + w, 0:half_p, :] = first[w, :, lanes]
                    wpan_ref[blk + w, half_p:, :] = second[w, :, lanes]
                    for side, sref, xref in ((0, slo_ref, xlo_ref), (2, shi_ref, xhi_ref)):
                        mine = sref[w, 0:half_p, :]
                        cross = xref[w]
                        lo_rows, hi_rows = (mine, cross) if hsel == 0 else (cross, mine)
                        wpan_ref[side * blk + w, 0:half_p, :] = lo_rows
                        wpan_ref[side * blk + w, half_p:, :] = hi_rows

    rows = jnp.concatenate([pos_ref[b], rad_ref[pl.ds(b, 1), :],
                            jnp.zeros((LANES - 4, unk), jnp.float32)], axis=0)
    cols = jnp.transpose(rows)
    for c in range(4):
        bc_ref[c] = jnp.broadcast_to(cols[:, c:c + 1], (unk, LANES))
    s_row = len_ref[pl.ds(b, 1), :]
    bs_ref[0:half_p, :] = (basis_ref[b].astype(jnp.float32) * s_row).astype(jnp.bfloat16)
    bs_ref[half_p:, :] = (other_ref[b].astype(jnp.float32) * s_row).astype(jnp.bfloat16)

    gb = ri * blk + b
    cnt = cnt_ref[b]
    mask = jnp.int32(0)
    slots = []
    for k in range(near):
        o_k = jnp.clip(nb_ref[b, k] - gb + blk, 0, 2 * blk)
        live_k = k < cnt
        mask = mask | jnp.where(live_k, jnp.left_shift(jnp.int32(1), o_k), 0)
        slots.append((o_k, live_k))

    n_need = jnp.int32(0)
    for o in range(n_off):
        lst_ref[n_need] = jnp.int32(o)
        n_need = n_need + (jnp.right_shift(mask, o) & 1)

    def coupling(o, cs_ref):
        wg = wgeo_ref[b + o]
        ys = [[jnp.broadcast_to(wg[c:c + 1, h * LANES:(h + 1) * LANES], (CHUNK, LANES))
               for h in range(n_tiles)] for c in (0, 1, 2, 4)]
        for mc in range(unk // CHUNK):
            r = slice(mc * CHUNK, (mc + 1) * CHUNK)
            xs = [bc_ref[c, r, :] for c in range(4)]
            for h in range(n_tiles):
                d0 = xs[0] - ys[0][h]
                d1 = xs[1] - ys[1][h]
                d2 = xs[2] - ys[2][h]
                dd = d0 * d0 + d1 * d1 + d2 * d2 + xs[3] * ys[3][h]
                cs_ref[r, h * LANES:(h + 1) * LANES] = lax.rsqrt(dd).astype(jnp.bfloat16)

    def finish(o, cs_ref):
        j = b + o
        left = jnp.dot(bs_ref[...], cs_ref[...], preferred_element_type=jnp.float32)
        left = (left * wgeo_ref[j, 3:4, :]).astype(jnp.bfloat16)
        ts_ref[o] = lax.dot_general(left, wpan_ref[j], (((1,), (1,)), ((), ())),
                                    preferred_element_type=jnp.float32)

    coupling(lst_ref[0], cs0_ref)

    def two_steps(t, carry):
        i = 2 * t + 1
        coupling(lst_ref[i], cs1_ref)
        finish(lst_ref[i - 1], cs0_ref)
        coupling(lst_ref[i + 1], cs0_ref)
        finish(lst_ref[i], cs1_ref)
        return carry

    lax.fori_loop(0, (n_need - 1) // 2, two_steps, 0)

    @pl.when(n_need % 2 == 0)
    def _():
        coupling(lst_ref[n_need - 1], cs1_ref)
        finish(lst_ref[n_need - 2], cs0_ref)
        finish(lst_ref[n_need - 1], cs1_ref)

    @pl.when(n_need % 2 == 1)
    def _():
        finish(lst_ref[n_need - 1], cs0_ref)

    nb_p = 2 * half_p
    for k, (o_k, live_k) in enumerate(slots):
        t = ts_ref[o_k]
        t = jnp.where(live_k, t, jnp.zeros_like(t))
        mine_ref[0, :, k * nb_p:(k + 1) * nb_p] = t[0:half_p]
        theirs_ref[0, :, k * nb_p:(k + 1) * nb_p] = t[half_p:]


def on_device(basis, positions, seglen, radius, neighbours, counts):
    blk, half_p, unk = basis.shape
    nb_p = 2 * half_p
    half = unk // 2
    near = neighbours.shape[1]
    n_row = lax.axis_size("row")
    ci = lax.axis_index("col")

    other = lax.ppermute(basis, "col", [(0, 1), (1, 0)])

    geo = jnp.concatenate([positions, seglen[:, None, :], radius[:, None, :]], axis=1)
    geo_mine = lax.dynamic_slice_in_dim(geo, ci * half, half, axis=2)
    hi, mid, lo = split3(geo_mine)
    same_msg = jnp.concatenate(
        [lax.dynamic_slice_in_dim(basis, ci * half, half, axis=2), hi, mid, lo,
         jnp.zeros((blk, 1, half), jnp.bfloat16)], axis=1)
    cross_msg = lax.dynamic_slice_in_dim(basis, (1 - ci) * half, half, axis=2)

    fwd = [(i, i + 1) for i in range(n_row - 1)]
    bwd = [(i + 1, i) for i in range(n_row - 1)]
    fwd_x = [(2 * i + c, 2 * (i + 1) + 1 - c) for i in range(n_row - 1) for c in range(2)]
    bwd_x = [(2 * (i + 1) + c, 2 * i + 1 - c) for i in range(n_row - 1) for c in range(2)]
    same_lo = lax.ppermute(same_msg, "row", fwd)
    same_hi = lax.ppermute(same_msg, "row", bwd)
    cross_lo = lax.ppermute(cross_msg, ("row", "col"), fwd_x)
    cross_hi = lax.ppermute(cross_msg, ("row", "col"), bwd_x)

    kernel = functools.partial(pair_kernel, blk=blk, near=near, unk=unk, half=half,
                               half_p=half_p)
    n_off = 2 * blk + 1

    def whole(shape):
        return pl.BlockSpec(shape, lambda b, *_: (0,) * len(shape))

    mine, theirs = pl.pallas_call(
        kernel,
        out_shape=(jax.ShapeDtypeStruct((blk, half_p, near * nb_p), jnp.float32),) * 2,
        grid_spec=pltpu.PrefetchScalarGridSpec(
            num_scalar_prefetch=2,
            grid=(blk,),
            in_specs=[
                whole(positions.shape), whole(seglen.shape), whole(radius.shape),
                whole(basis.shape), whole(other.shape),
                whole(same_lo.shape), whole(same_hi.shape),
                whole(cross_lo.shape), whole(cross_hi.shape),
            ],
            out_specs=(pl.BlockSpec((1, half_p, near * nb_p), lambda b, *_: (b, 0, 0)),) * 2,
            scratch_shapes=[
                pltpu.VMEM((3 * blk, 8, half), jnp.float32),
                pltpu.VMEM((3 * blk, nb_p, half), jnp.bfloat16),
                pltpu.VMEM((4, unk, LANES), jnp.float32),
                pltpu.VMEM((nb_p, unk), jnp.bfloat16),
                pltpu.VMEM((unk, half), jnp.bfloat16),
                pltpu.VMEM((unk, half), jnp.bfloat16),
                pltpu.VMEM((n_off, nb_p, nb_p), jnp.float32),
                pltpu.SMEM((32,), jnp.int32),
            ],
        ),
        compiler_params=pltpu.CompilerParams(dimension_semantics=("arbitrary",)),
    )(neighbours, counts, positions, seglen, radius, basis, other,
      same_lo, same_hi, cross_lo, cross_hi)

    return mine + lax.ppermute(theirs, "col", [(0, 1), (1, 0)])


def solution(mesh):
    placed = (
        P("row", "col", None),
        P("row", None, None),
        P("row", None),
        P("row", None),
        P("row", None),
        P("row"),
    )
    return jax.shard_map(
        on_device, mesh=mesh, in_specs=placed, out_specs=P("row", "col", None), check_vma=False
    )
```

```python
import functools

import jax
import jax.numpy as jnp
from jax import lax
from jax.experimental import pallas as pl
from jax.experimental.pallas import tpu as pltpu
from jax.sharding import PartitionSpec as P


CHUNK = 8
GROUP = 128
LANES = 128


def split3(x):
    hi = x.astype(jnp.bfloat16)
    r1 = x - hi.astype(jnp.float32)
    mid = r1.astype(jnp.bfloat16)
    lo = (r1 - mid.astype(jnp.float32)).astype(jnp.bfloat16)
    return hi, mid, lo


def pair_kernel(nb_ref, cnt_ref, pos_ref, len_ref, rad_ref, basis_ref, other_ref,
                hrecv_ref, hx_ref, mine_ref, theirs_ref,
                wgeo_ref, wpan_ref, bc_ref, bs_ref, cs0_ref, cs1_ref, ts_ref, lst_ref,
                *, blk, near, unk, half, half_p):
    b = pl.program_id(0)
    ci = lax.axis_index("col")
    ri = lax.axis_index("row")
    n_off = 2 * blk + 1
    n_tiles = half // LANES
    nb_p = 2 * half_p

    @pl.when(b == 0)
    def _setup():
        for hsel in range(2):
            @pl.when(ci == hsel)
            def _():
                lanes = slice(hsel * half, (hsel + 1) * half)
                if hsel == 0:
                    sides = ((0, hrecv_ref, lanes, False), (2, hx_ref, slice(0, half), True))
                else:
                    sides = ((2, hrecv_ref, lanes, True), (0, hx_ref, slice(0, half), False))
                for side, href, hl, swapped in sides:
                    for w in range(blk):
                        g = href[w, nb_p:nb_p + 16, hl].astype(jnp.float32)
                        wgeo_ref[side * blk + w, 0:5, :] = g[0:5] + g[5:10] + g[10:15]
                        first = href[w, 0:half_p, hl]
                        second = href[w, half_p:nb_p, hl]
                        lo_rows, hi_rows = (second, first) if swapped else (first, second)
                        wpan_ref[side * blk + w, 0:half_p, :] = lo_rows
                        wpan_ref[side * blk + w, half_p:, :] = hi_rows
                for w in range(blk):
                    wgeo_ref[blk + w, 0:3, :] = pos_ref[w, :, lanes]
                    wgeo_ref[blk + w, 3:4, :] = len_ref[w:w + 1, lanes]
                    wgeo_ref[blk + w, 4:5, :] = rad_ref[w:w + 1, lanes]
                    first, second = (basis_ref, other_ref) if hsel == 0 else (other_ref, basis_ref)
                    wpan_ref[blk + w, 0:half_p, :] = first[w, :, lanes]
                    wpan_ref[blk + w, half_p:, :] = second[w, :, lanes]

    rows = jnp.concatenate([pos_ref[b], rad_ref[pl.ds(b, 1), :],
                            jnp.zeros((LANES - 4, unk), jnp.float32)], axis=0)
    cols = jnp.transpose(rows)
    for c in range(4):
        bc_ref[c] = jnp.broadcast_to(cols[:, c:c + 1], (unk, LANES))
    s_row = len_ref[pl.ds(b, 1), :]
    bs_ref[0:half_p, :] = (basis_ref[b].astype(jnp.float32) * s_row).astype(jnp.bfloat16)
    bs_ref[half_p:, :] = (other_ref[b].astype(jnp.float32) * s_row).astype(jnp.bfloat16)

    gb = ri * blk + b
    cnt = cnt_ref[b]
    mask = jnp.int32(0)
    slots = []
    for k in range(near):
        o_k = jnp.clip(nb_ref[b, k] - gb + blk, 0, 2 * blk)
        live_k = k < cnt
        mask = mask | jnp.where(live_k, jnp.left_shift(jnp.int32(1), o_k), 0)
        slots.append((o_k, live_k))

    n_need = jnp.int32(0)
    for o in range(n_off):
        lst_ref[n_need] = jnp.int32(o)
        n_need = n_need + (jnp.right_shift(mask, o) & 1)

    def coupling(o, cs_ref):
        wg = wgeo_ref[b + o]
        ys = [[jnp.broadcast_to(wg[c:c + 1, h * LANES:(h + 1) * LANES], (CHUNK, LANES))
               for h in range(n_tiles)] for c in (0, 1, 2, 4)]
        for mc in range(unk // CHUNK):
            r = slice(mc * CHUNK, (mc + 1) * CHUNK)
            xs = [bc_ref[c, r, :] for c in range(4)]
            for h in range(n_tiles):
                d0 = xs[0] - ys[0][h]
                d1 = xs[1] - ys[1][h]
                d2 = xs[2] - ys[2][h]
                dd = d0 * d0 + d1 * d1 + d2 * d2 + xs[3] * ys[3][h]
                cs_ref[r, h * LANES:(h + 1) * LANES] = lax.rsqrt(dd).astype(jnp.bfloat16)

    def finish(o, cs_ref):
        j = b + o
        left = jnp.dot(bs_ref[...], cs_ref[...], preferred_element_type=jnp.float32)
        left = (left * wgeo_ref[j, 3:4, :]).astype(jnp.bfloat16)
        ts_ref[o] = lax.dot_general(left, wpan_ref[j], (((1,), (1,)), ((), ())),
                                    preferred_element_type=jnp.float32)

    coupling(lst_ref[0], cs0_ref)

    def two_steps(t, carry):
        i = 2 * t + 1
        coupling(lst_ref[i], cs1_ref)
        finish(lst_ref[i - 1], cs0_ref)
        coupling(lst_ref[i + 1], cs0_ref)
        finish(lst_ref[i], cs1_ref)
        return carry

    lax.fori_loop(0, (n_need - 1) // 2, two_steps, 0)

    @pl.when(n_need % 2 == 0)
    def _():
        coupling(lst_ref[n_need - 1], cs1_ref)
        finish(lst_ref[n_need - 2], cs0_ref)
        finish(lst_ref[n_need - 1], cs1_ref)

    @pl.when(n_need % 2 == 1)
    def _():
        finish(lst_ref[n_need - 1], cs0_ref)

    for k, (o_k, live_k) in enumerate(slots):
        t = ts_ref[o_k]
        t = jnp.where(live_k, t, jnp.zeros_like(t))
        mine_ref[0, :, k * nb_p:(k + 1) * nb_p] = t[0:half_p]
        theirs_ref[0, :, k * nb_p:(k + 1) * nb_p] = t[half_p:]


def on_device(basis, positions, seglen, radius, neighbours, counts):
    blk, half_p, unk = basis.shape
    nb_p = 2 * half_p
    half = unk // 2
    near = neighbours.shape[1]
    n_row = lax.axis_size("row")
    ci = lax.axis_index("col")

    other = lax.ppermute(basis, "col", [(0, 1), (1, 0)])

    geo = jnp.concatenate([positions, seglen[:, None, :], radius[:, None, :]], axis=1)
    hi, mid, lo = split3(geo)
    msg = jnp.concatenate([basis, other, hi, mid, lo, jnp.zeros((blk, 1, unk), jnp.bfloat16)],
                          axis=1)
    pairs = [(2 * i, 2 * (i + 1)) for i in range(n_row - 1)]
    pairs += [(2 * (i + 1) + 1, 2 * i + 1) for i in range(n_row - 1)]
    hrecv = lax.ppermute(msg, ("row", "col"), pairs)
    hx = lax.ppermute(lax.dynamic_slice_in_dim(hrecv, (1 - ci) * half, half, axis=2),
                      "col", [(0, 1), (1, 0)])

    kernel = functools.partial(pair_kernel, blk=blk, near=near, unk=unk, half=half,
                               half_p=half_p)
    n_off = 2 * blk + 1

    def whole(shape):
        return pl.BlockSpec(shape, lambda b, *_: (0,) * len(shape))

    mine, theirs = pl.pallas_call(
        kernel,
        out_shape=(jax.ShapeDtypeStruct((blk, half_p, near * nb_p), jnp.float32),) * 2,
        grid_spec=pltpu.PrefetchScalarGridSpec(
            num_scalar_prefetch=2,
            grid=(blk,),
            in_specs=[
                whole(positions.shape), whole(seglen.shape), whole(radius.shape),
                whole(basis.shape), whole(other.shape),
                whole(hrecv.shape), whole(hx.shape),
            ],
            out_specs=(pl.BlockSpec((1, half_p, near * nb_p), lambda b, *_: (b, 0, 0)),) * 2,
            scratch_shapes=[
                pltpu.VMEM((3 * blk, 8, half), jnp.float32),
                pltpu.VMEM((3 * blk, nb_p, half), jnp.bfloat16),
                pltpu.VMEM((4, unk, LANES), jnp.float32),
                pltpu.VMEM((nb_p, unk), jnp.bfloat16),
                pltpu.VMEM((unk, half), jnp.bfloat16),
                pltpu.VMEM((unk, half), jnp.bfloat16),
                pltpu.VMEM((n_off, nb_p, nb_p), jnp.float32),
                pltpu.SMEM((32,), jnp.int32),
            ],
        ),
        compiler_params=pltpu.CompilerParams(dimension_semantics=("arbitrary",)),
    )(neighbours, counts, positions, seglen, radius, basis, other,
      hrecv, hx)

    return mine + lax.ppermute(theirs, "col", [(0, 1), (1, 0)])


def solution(mesh):
    placed = (
        P("row", "col", None),
        P("row", None, None),
        P("row", None),
        P("row", None),
        P("row", None),
        P("row"),
    )
    return jax.shard_map(
        on_device, mesh=mesh, in_specs=placed, out_specs=P("row", "col", None), check_vma=False
    )
```

```python
import functools

import jax
import jax.numpy as jnp
from jax import lax
from jax.experimental import pallas as pl
from jax.experimental.pallas import tpu as pltpu
from jax.sharding import PartitionSpec as P


CHUNK = 8
GROUP = 128
LANES = 128


def split3(x):
    hi = x.astype(jnp.bfloat16)
    r1 = x - hi.astype(jnp.float32)
    mid = r1.astype(jnp.bfloat16)
    lo = (r1 - mid.astype(jnp.float32)).astype(jnp.bfloat16)
    return hi, mid, lo


def pair_kernel(nb_ref, cnt_ref, pos_ref, len_ref, rad_ref, basis_ref, other_ref, *refs,
                phase, blk, near, unk, half, half_p):
    if phase == "own":
        (mine_ref, theirs_ref, bco_ref,
         wgeo_ref, wpan_ref, bs_ref, cs0_ref, cs1_ref, ts_ref, lst_ref) = refs
        bc_ref = bco_ref.at[0]
    else:
        (hrecv_ref, hx_ref, bci_ref, pmine_ref, ptheirs_ref, mine_ref, theirs_ref,
         wgeo_ref, wpan_ref, bs_ref, cs0_ref, cs1_ref, ts_ref, lst_ref) = refs
        bc_ref = bci_ref.at[0]
    b = pl.program_id(0)
    ci = lax.axis_index("col")
    ri = lax.axis_index("row")
    n_off = 2 * blk + 1
    n_tiles = half // LANES
    nb_p = 2 * half_p

    @pl.when(b == 0)
    def _setup():
        for hsel in range(2):
            @pl.when(ci == hsel)
            def _():
                lanes = slice(hsel * half, (hsel + 1) * half)
                if phase == "own":
                    for w in range(blk):
                        wgeo_ref[blk + w, 0:3, :] = pos_ref[w, :, lanes]
                        wgeo_ref[blk + w, 3:4, :] = len_ref[w:w + 1, lanes]
                        wgeo_ref[blk + w, 4:5, :] = rad_ref[w:w + 1, lanes]
                        first, second = ((basis_ref, other_ref) if hsel == 0
                                         else (other_ref, basis_ref))
                        wpan_ref[blk + w, 0:half_p, :] = first[w, :, lanes]
                        wpan_ref[blk + w, half_p:, :] = second[w, :, lanes]
                    return
                if hsel == 0:
                    sides = ((0, hrecv_ref, lanes, False), (2, hx_ref, slice(0, half), True))
                else:
                    sides = ((2, hrecv_ref, lanes, True), (0, hx_ref, slice(0, half), False))
                for side, href, hl, swapped in sides:
                    for w in range(blk):
                        g = href[w, nb_p:nb_p + 16, hl].astype(jnp.float32)
                        wgeo_ref[side * blk + w, 0:5, :] = g[0:5] + g[5:10] + g[10:15]
                        first = href[w, 0:half_p, hl]
                        second = href[w, half_p:nb_p, hl]
                        lo_rows, hi_rows = (second, first) if swapped else (first, second)
                        wpan_ref[side * blk + w, 0:half_p, :] = lo_rows
                        wpan_ref[side * blk + w, half_p:, :] = hi_rows

    if phase == "own":
        rows = jnp.concatenate([pos_ref[b], rad_ref[pl.ds(b, 1), :],
                                jnp.zeros((LANES - 4, unk), jnp.float32)], axis=0)
        cols = jnp.transpose(rows)
        for c in range(4):
            bc_ref[c] = jnp.broadcast_to(cols[:, c:c + 1], (unk, LANES))
    s_row = len_ref[pl.ds(b, 1), :]
    bs_ref[0:half_p, :] = (basis_ref[b].astype(jnp.float32) * s_row).astype(jnp.bfloat16)
    bs_ref[half_p:, :] = (other_ref[b].astype(jnp.float32) * s_row).astype(jnp.bfloat16)

    gb = ri * blk + b
    cnt = cnt_ref[b]
    mask = jnp.int32(0)
    slots = []
    for k in range(near):
        o_k = jnp.clip(nb_ref[b, k] - gb + blk, 0, 2 * blk)
        on_dev = (b + o_k >= blk) & (b + o_k < 2 * blk)
        use_k = (k < cnt) & (on_dev if phase == "own" else jnp.logical_not(on_dev))
        mask = mask | jnp.where(use_k, jnp.left_shift(jnp.int32(1), o_k), 0)
        slots.append((o_k, use_k))

    n_need = jnp.int32(0)
    for o in range(n_off):
        lst_ref[n_need] = jnp.int32(o)
        n_need = n_need + (jnp.right_shift(mask, o) & 1)

    def coupling(o, cs_ref):
        wg = wgeo_ref[b + o]
        ys = [[jnp.broadcast_to(wg[c:c + 1, h * LANES:(h + 1) * LANES], (CHUNK, LANES))
               for h in range(n_tiles)] for c in (0, 1, 2, 4)]
        for mc in range(unk // CHUNK):
            r = slice(mc * CHUNK, (mc + 1) * CHUNK)
            xs = [bc_ref[c, r, :] for c in range(4)]
            for h in range(n_tiles):
                d0 = xs[0] - ys[0][h]
                d1 = xs[1] - ys[1][h]
                d2 = xs[2] - ys[2][h]
                dd = d0 * d0 + d1 * d1 + d2 * d2 + xs[3] * ys[3][h]
                cs_ref[r, h * LANES:(h + 1) * LANES] = lax.rsqrt(dd).astype(jnp.bfloat16)

    def finish(o, cs_ref):
        j = b + o
        left = jnp.dot(bs_ref[...], cs_ref[...], preferred_element_type=jnp.float32)
        left = (left * wgeo_ref[j, 3:4, :]).astype(jnp.bfloat16)
        ts_ref[o] = lax.dot_general(left, wpan_ref[j], (((1,), (1,)), ((), ())),
                                    preferred_element_type=jnp.float32)

    @pl.when(n_need > 0)
    def _():
        coupling(lst_ref[0], cs0_ref)

    def two_steps(t, carry):
        i = 2 * t + 1
        coupling(lst_ref[i], cs1_ref)
        finish(lst_ref[i - 1], cs0_ref)
        coupling(lst_ref[i + 1], cs0_ref)
        finish(lst_ref[i], cs1_ref)
        return carry

    lax.fori_loop(0, jnp.maximum(n_need - 1, 0) // 2, two_steps, 0)

    @pl.when((n_need % 2 == 0) & (n_need > 0))
    def _():
        coupling(lst_ref[n_need - 1], cs1_ref)
        finish(lst_ref[n_need - 2], cs0_ref)
        finish(lst_ref[n_need - 1], cs1_ref)

    @pl.when(n_need % 2 == 1)
    def _():
        finish(lst_ref[n_need - 1], cs0_ref)

    for k, (o_k, use_k) in enumerate(slots):
        t = ts_ref[o_k]
        cols_k = slice(k * nb_p, (k + 1) * nb_p)
        if phase == "own":
            t = jnp.where(use_k, t, jnp.zeros_like(t))
            mine_ref[0, :, cols_k] = t[0:half_p]
            theirs_ref[0, :, cols_k] = t[half_p:]
        else:
            mine_ref[0, :, cols_k] = jnp.where(use_k, t[0:half_p], pmine_ref[0, :, cols_k])
            theirs_ref[0, :, cols_k] = jnp.where(use_k, t[half_p:], ptheirs_ref[0, :, cols_k])


def on_device(basis, positions, seglen, radius, neighbours, counts):
    blk, half_p, unk = basis.shape
    nb_p = 2 * half_p
    half = unk // 2
    near = neighbours.shape[1]
    n_row = lax.axis_size("row")
    ci = lax.axis_index("col")

    other = lax.ppermute(basis, "col", [(0, 1), (1, 0)])

    geo = jnp.concatenate([positions, seglen[:, None, :], radius[:, None, :]], axis=1)
    hi, mid, lo = split3(geo)
    msg = jnp.concatenate([basis, other, hi, mid, lo, jnp.zeros((blk, 1, unk), jnp.bfloat16)],
                          axis=1)
    pairs = [(2 * i, 2 * (i + 1)) for i in range(n_row - 1)]
    pairs += [(2 * (i + 1) + 1, 2 * i + 1) for i in range(n_row - 1)]
    hrecv = lax.ppermute(msg, ("row", "col"), pairs)
    n_off = 2 * blk + 1
    sizes = dict(blk=blk, near=near, unk=unk, half=half, half_p=half_p)

    def whole(shape):
        return pl.BlockSpec(shape, lambda b, *_: (0,) * len(shape))

    part_shape = jax.ShapeDtypeStruct((blk, half_p, near * nb_p), jnp.float32)
    part_spec = pl.BlockSpec((1, half_p, near * nb_p), lambda b, *_: (b, 0, 0))
    bc_shape = jax.ShapeDtypeStruct((blk, 4, unk, LANES), jnp.float32)
    bc_spec = pl.BlockSpec((1, 4, unk, LANES), lambda b, *_: (b, 0, 0, 0))
    own_specs = [whole(positions.shape), whole(seglen.shape), whole(radius.shape),
                 whole(basis.shape), whole(other.shape)]
    scratch = [
        pltpu.VMEM((3 * blk, 8, half), jnp.float32),
        pltpu.VMEM((3 * blk, nb_p, half), jnp.bfloat16),
        pltpu.VMEM((nb_p, unk), jnp.bfloat16),
        pltpu.VMEM((unk, half), jnp.bfloat16),
        pltpu.VMEM((unk, half), jnp.bfloat16),
        pltpu.VMEM((n_off, nb_p, nb_p), jnp.float32),
        pltpu.SMEM((32,), jnp.int32),
    ]
    params = pltpu.CompilerParams(dimension_semantics=("arbitrary",))
    own_args = (neighbours, counts, positions, seglen, radius, basis, other)

    mine0, theirs0, bc = pl.pallas_call(
        functools.partial(pair_kernel, phase="own", **sizes),
        out_shape=(part_shape, part_shape, bc_shape),
        grid_spec=pltpu.PrefetchScalarGridSpec(
            num_scalar_prefetch=2, grid=(blk,), in_specs=own_specs,
            out_specs=(part_spec, part_spec, bc_spec), scratch_shapes=scratch),
        compiler_params=params,
    )(*own_args)

    hrecv, mine0, theirs0, bc = lax.optimization_barrier((hrecv, mine0, theirs0, bc))
    hx = lax.ppermute(lax.dynamic_slice_in_dim(hrecv, (1 - ci) * half, half, axis=2),
                      "col", [(0, 1), (1, 0)])

    mine, theirs = pl.pallas_call(
        functools.partial(pair_kernel, phase="halo", **sizes),
        out_shape=(part_shape, part_shape),
        grid_spec=pltpu.PrefetchScalarGridSpec(
            num_scalar_prefetch=2, grid=(blk,),
            in_specs=own_specs + [whole(hrecv.shape), whole(hx.shape), bc_spec,
                                  part_spec, part_spec],
            out_specs=(part_spec, part_spec), scratch_shapes=scratch),
        compiler_params=params,
    )(*own_args, hrecv, hx, bc, mine0, theirs0)

    return mine + lax.ppermute(theirs, "col", [(0, 1), (1, 0)])


def solution(mesh):
    placed = (
        P("row", "col", None),
        P("row", None, None),
        P("row", None),
        P("row", None),
        P("row", None),
        P("row"),
    )
    return jax.shard_map(
        on_device, mesh=mesh, in_specs=placed, out_specs=P("row", "col", None), check_vma=False
    )
```

```python
import functools

import jax
import jax.numpy as jnp
from jax import lax
from jax.experimental import pallas as pl
from jax.experimental.pallas import tpu as pltpu
from jax.sharding import PartitionSpec as P


CHUNK = 8
GROUP = 128
LANES = 128


def pair_kernel(nb_ref, cnt_ref, pos_ref, len_ref, rad_ref, basis_ref, other_ref, *refs,
                phase, blk, near, unk, half, half_p):
    if phase == "own":
        (mine_ref, theirs_ref, bco_ref,
         wgeo_ref, wpan_ref, bs_ref, cs0_ref, cs1_ref, ts_ref, lst_ref) = refs
        bc_ref = bco_ref.at[0]
    else:
        (hrecv_ref, hx_ref, bci_ref, pmine_ref, ptheirs_ref, mine_ref, theirs_ref,
         wgeo_ref, wpan_ref, bs_ref, cs0_ref, cs1_ref, ts_ref, lst_ref) = refs
        bc_ref = bci_ref.at[0]
    b = pl.program_id(0)
    ci = lax.axis_index("col")
    ri = lax.axis_index("row")
    n_off = 2 * blk + 1
    n_tiles = half // LANES
    nb_p = 2 * half_p

    @pl.when(b == 0)
    def _setup():
        for hsel in range(2):
            @pl.when(ci == hsel)
            def _():
                lanes = slice(hsel * half, (hsel + 1) * half)
                if phase == "own":
                    for w in range(blk):
                        wgeo_ref[blk + w, 0:3, :] = pos_ref[w, :, lanes]
                        wgeo_ref[blk + w, 3:4, :] = len_ref[w:w + 1, lanes]
                        wgeo_ref[blk + w, 4:5, :] = rad_ref[w:w + 1, lanes]
                        first, second = ((basis_ref, other_ref) if hsel == 0
                                         else (other_ref, basis_ref))
                        wpan_ref[blk + w, 0:half_p, :] = first[w, :, lanes]
                        wpan_ref[blk + w, half_p:, :] = second[w, :, lanes]
                    return
                if hsel == 0:
                    sides = ((0, hrecv_ref, lanes, False), (2, hx_ref, slice(0, half), True))
                else:
                    sides = ((2, hrecv_ref, lanes, True), (0, hx_ref, slice(0, half), False))
                for side, href, hl, swapped in sides:
                    for w in range(blk):
                        g = href[w, nb_p:nb_p + 16, hl].astype(jnp.float32)
                        wgeo_ref[side * blk + w, 0:5, :] = g[0:5] + g[5:10] + g[10:15]
                        first = href[w, 0:half_p, hl]
                        second = href[w, half_p:nb_p, hl]
                        lo_rows, hi_rows = (second, first) if swapped else (first, second)
                        wpan_ref[side * blk + w, 0:half_p, :] = lo_rows
                        wpan_ref[side * blk + w, half_p:, :] = hi_rows

    if phase == "own":
        rows = jnp.concatenate([pos_ref[b], rad_ref[pl.ds(b, 1), :],
                                jnp.zeros((LANES - 4, unk), jnp.float32)], axis=0)
        cols = jnp.transpose(rows)
        for c in range(4):
            bc_ref[c] = jnp.broadcast_to(cols[:, c:c + 1], (unk, LANES))
    s_row = len_ref[pl.ds(b, 1), :]
    bs_ref[0:half_p, :] = (basis_ref[b].astype(jnp.float32) * s_row).astype(jnp.bfloat16)
    bs_ref[half_p:, :] = (other_ref[b].astype(jnp.float32) * s_row).astype(jnp.bfloat16)

    gb = ri * blk + b
    cnt = cnt_ref[b]
    mask = jnp.int32(0)
    slots = []
    for k in range(near):
        o_k = jnp.clip(nb_ref[b, k] - gb + blk, 0, 2 * blk)
        on_dev = (b + o_k >= blk) & (b + o_k < 2 * blk)
        use_k = (k < cnt) & (on_dev if phase == "own" else jnp.logical_not(on_dev))
        mask = mask | jnp.where(use_k, jnp.left_shift(jnp.int32(1), o_k), 0)
        slots.append((o_k, use_k))

    n_need = jnp.int32(0)
    for o in range(n_off):
        lst_ref[n_need] = jnp.int32(o)
        n_need = n_need + (jnp.right_shift(mask, o) & 1)

    def coupling(o, cs_ref):
        wg = wgeo_ref[b + o]
        ys = [[jnp.broadcast_to(wg[c:c + 1, h * LANES:(h + 1) * LANES], (CHUNK, LANES))
               for h in range(n_tiles)] for c in (0, 1, 2, 4)]
        for mc in range(unk // CHUNK):
            r = slice(mc * CHUNK, (mc + 1) * CHUNK)
            xs = [bc_ref[c, r, :] for c in range(4)]
            for h in range(n_tiles):
                d0 = xs[0] - ys[0][h]
                d1 = xs[1] - ys[1][h]
                d2 = xs[2] - ys[2][h]
                dd = d0 * d0 + d1 * d1 + d2 * d2 + xs[3] * ys[3][h]
                cs_ref[r, h * LANES:(h + 1) * LANES] = lax.rsqrt(dd).astype(jnp.bfloat16)

    def finish(o, cs_ref):
        j = b + o
        left = jnp.dot(bs_ref[...], cs_ref[...], preferred_element_type=jnp.float32)
        left = (left * wgeo_ref[j, 3:4, :]).astype(jnp.bfloat16)
        ts_ref[o] = lax.dot_general(left, wpan_ref[j], (((1,), (1,)), ((), ())),
                                    preferred_element_type=jnp.float32)

    @pl.when(n_need > 0)
    def _():
        coupling(lst_ref[0], cs0_ref)

    def two_steps(t, carry):
        i = 2 * t + 1
        coupling(lst_ref[i], cs1_ref)
        finish(lst_ref[i - 1], cs0_ref)
        coupling(lst_ref[i + 1], cs0_ref)
        finish(lst_ref[i], cs1_ref)
        return carry

    lax.fori_loop(0, jnp.maximum(n_need - 1, 0) // 2, two_steps, 0)

    @pl.when((n_need % 2 == 0) & (n_need > 0))
    def _():
        coupling(lst_ref[n_need - 1], cs1_ref)
        finish(lst_ref[n_need - 2], cs0_ref)
        finish(lst_ref[n_need - 1], cs1_ref)

    @pl.when(n_need % 2 == 1)
    def _():
        finish(lst_ref[n_need - 1], cs0_ref)

    for k, (o_k, use_k) in enumerate(slots):
        t = ts_ref[o_k]
        cols_k = slice(k * nb_p, (k + 1) * nb_p)
        if phase == "own":
            t = jnp.where(use_k, t, jnp.zeros_like(t))
            mine_ref[0, :, cols_k] = t[0:half_p]
            theirs_ref[0, :, cols_k] = t[half_p:]
        else:
            mine_ref[0, :, cols_k] = jnp.where(use_k, t[0:half_p], pmine_ref[0, :, cols_k])
            theirs_ref[0, :, cols_k] = jnp.where(use_k, t[half_p:], ptheirs_ref[0, :, cols_k]
                                                 ).astype(theirs_ref.dtype)


def pack_kernel(pos_ref, len_ref, rad_ref, basis_ref, other_ref, msg_ref, *, blk, half_p):
    nb_p = 2 * half_p
    for w in range(blk):
        msg_ref[w, 0:half_p, :] = basis_ref[w]
        msg_ref[w, half_p:nb_p, :] = other_ref[w]
        g = jnp.concatenate([pos_ref[w], len_ref[w:w + 1, :], rad_ref[w:w + 1, :]], axis=0)
        hi = g.astype(jnp.bfloat16)
        r1 = g - hi.astype(jnp.float32)
        mid = r1.astype(jnp.bfloat16)
        lo = (r1 - mid.astype(jnp.float32)).astype(jnp.bfloat16)
        parts = jnp.concatenate([hi.astype(jnp.float32), mid.astype(jnp.float32),
                                 lo.astype(jnp.float32), jnp.zeros_like(g[0:1])], axis=0)
        msg_ref[w, nb_p:nb_p + 16, :] = parts.astype(jnp.bfloat16)


def on_device(basis, positions, seglen, radius, neighbours, counts):
    blk, half_p, unk = basis.shape
    nb_p = 2 * half_p
    half = unk // 2
    near = neighbours.shape[1]
    n_row = lax.axis_size("row")
    ci = lax.axis_index("col")

    other = lax.ppermute(basis, "col", [(0, 1), (1, 0)])

    msg = pl.pallas_call(
        functools.partial(pack_kernel, blk=blk, half_p=half_p),
        out_shape=jax.ShapeDtypeStruct((blk, nb_p + 16, unk), jnp.bfloat16),
    )(positions, seglen, radius, basis, other)
    pairs = [(2 * i, 2 * (i + 1)) for i in range(n_row - 1)]
    pairs += [(2 * (i + 1) + 1, 2 * i + 1) for i in range(n_row - 1)]
    hrecv = lax.ppermute(msg, ("row", "col"), pairs)
    n_off = 2 * blk + 1
    sizes = dict(blk=blk, near=near, unk=unk, half=half, half_p=half_p)

    def whole(shape):
        return pl.BlockSpec(shape, lambda b, *_: (0,) * len(shape))

    part_shape = jax.ShapeDtypeStruct((blk, half_p, near * nb_p), jnp.float32)
    part_spec = pl.BlockSpec((1, half_p, near * nb_p), lambda b, *_: (b, 0, 0))
    bc_shape = jax.ShapeDtypeStruct((blk, 4, unk, LANES), jnp.float32)
    bc_spec = pl.BlockSpec((1, 4, unk, LANES), lambda b, *_: (b, 0, 0, 0))
    own_specs = [whole(positions.shape), whole(seglen.shape), whole(radius.shape),
                 whole(basis.shape), whole(other.shape)]
    scratch = [
        pltpu.VMEM((3 * blk, 8, half), jnp.float32),
        pltpu.VMEM((3 * blk, nb_p, half), jnp.bfloat16),
        pltpu.VMEM((nb_p, unk), jnp.bfloat16),
        pltpu.VMEM((unk, half), jnp.bfloat16),
        pltpu.VMEM((unk, half), jnp.bfloat16),
        pltpu.VMEM((n_off, nb_p, nb_p), jnp.float32),
        pltpu.SMEM((32,), jnp.int32),
    ]
    params = pltpu.CompilerParams(dimension_semantics=("arbitrary",))
    own_args = (neighbours, counts, positions, seglen, radius, basis, other)

    mine0, theirs0, bc = pl.pallas_call(
        functools.partial(pair_kernel, phase="own", **sizes),
        out_shape=(part_shape, part_shape, bc_shape),
        grid_spec=pltpu.PrefetchScalarGridSpec(
            num_scalar_prefetch=2, grid=(blk,), in_specs=own_specs,
            out_specs=(part_spec, part_spec, bc_spec), scratch_shapes=scratch),
        compiler_params=params,
    )(*own_args)

    hrecv, mine0, theirs0, bc = lax.optimization_barrier((hrecv, mine0, theirs0, bc))
    hx = lax.ppermute(lax.dynamic_slice_in_dim(hrecv, (1 - ci) * half, half, axis=2),
                      "col", [(0, 1), (1, 0)])

    mine, theirs = pl.pallas_call(
        functools.partial(pair_kernel, phase="halo", **sizes),
        out_shape=(part_shape, jax.ShapeDtypeStruct(part_shape.shape, jnp.bfloat16)),
        grid_spec=pltpu.PrefetchScalarGridSpec(
            num_scalar_prefetch=2, grid=(blk,),
            in_specs=own_specs + [whole(hrecv.shape), whole(hx.shape), bc_spec,
                                  part_spec, part_spec],
            out_specs=(part_spec, part_spec), scratch_shapes=scratch),
        compiler_params=params,
    )(*own_args, hrecv, hx, bc, mine0, theirs0)

    return mine + lax.ppermute(theirs, "col", [(0, 1), (1, 0)]).astype(jnp.float32)


def solution(mesh):
    placed = (
        P("row", "col", None),
        P("row", None, None),
        P("row", None),
        P("row", None),
        P("row", None),
        P("row"),
    )
    return jax.shard_map(
        on_device, mesh=mesh, in_specs=placed, out_specs=P("row", "col", None), check_vma=False
    )
```

```python
import functools

import jax
import jax.numpy as jnp
from jax import lax
from jax.experimental import pallas as pl
from jax.experimental.pallas import tpu as pltpu
from jax.sharding import PartitionSpec as P


CHUNK = 8
GROUP = 128
LANES = 128


def pair_kernel(nb_ref, cnt_ref, pos_ref, len_ref, rad_ref, basis_ref, other_ref,
                hrecv_ref, hx_ref, mine_ref, theirs_ref,
                wgeo_ref, wpan_ref, bc_ref, bs_ref, cs0_ref, cs1_ref, ts_ref, lst_ref,
                *, blk, near, unk, half, half_p):
    ci = lax.axis_index("col")
    ri = lax.axis_index("row")
    n_off = 2 * blk + 1
    n_tiles = half // LANES
    nb_p = 2 * half_p

    for hsel in range(2):
        @pl.when(ci == hsel)
        def _():
            lanes = slice(hsel * half, (hsel + 1) * half)
            if hsel == 0:
                sides = ((0, hrecv_ref, lanes, False), (2, hx_ref, slice(0, half), True))
            else:
                sides = ((2, hrecv_ref, lanes, True), (0, hx_ref, slice(0, half), False))
            for side, href, hl, swapped in sides:
                for w in range(blk):
                    g = href[w, nb_p:nb_p + 16, hl].astype(jnp.float32)
                    wgeo_ref[side * blk + w, 0:5, :] = g[0:5] + g[5:10] + g[10:15]
                    first = href[w, 0:half_p, hl]
                    second = href[w, half_p:nb_p, hl]
                    lo_rows, hi_rows = (second, first) if swapped else (first, second)
                    wpan_ref[side * blk + w, 0:half_p, :] = lo_rows
                    wpan_ref[side * blk + w, half_p:, :] = hi_rows
            for w in range(blk):
                wgeo_ref[blk + w, 0:3, :] = pos_ref[w, :, lanes]
                wgeo_ref[blk + w, 3:4, :] = len_ref[w:w + 1, lanes]
                wgeo_ref[blk + w, 4:5, :] = rad_ref[w:w + 1, lanes]
                first, second = (basis_ref, other_ref) if hsel == 0 else (other_ref, basis_ref)
                wpan_ref[blk + w, 0:half_p, :] = first[w, :, lanes]
                wpan_ref[blk + w, half_p:, :] = second[w, :, lanes]

    def slot_table(b):
        gb = ri * blk + b
        cnt = cnt_ref[b]
        out = []
        for k in range(near):
            o_k = jnp.clip(nb_ref[b, k] - gb + blk, 0, 2 * blk)
            out.append((o_k, k < cnt))
        return out

    n_need = jnp.int32(0)
    for b in range(blk):
        rows = jnp.concatenate([pos_ref[b], rad_ref[b:b + 1, :],
                                jnp.zeros((LANES - 4, unk), jnp.float32)], axis=0)
        cols = jnp.transpose(rows)
        for c in range(4):
            bc_ref[b, c] = jnp.broadcast_to(cols[:, c:c + 1], (unk, LANES))
        s_row = len_ref[b:b + 1, :]
        bs_ref[b, 0:half_p, :] = (basis_ref[b].astype(jnp.float32) * s_row).astype(jnp.bfloat16)
        bs_ref[b, half_p:, :] = (other_ref[b].astype(jnp.float32) * s_row).astype(jnp.bfloat16)
        mask = jnp.int32(0)
        for o_k, live_k in slot_table(b):
            mask = mask | jnp.where(live_k, jnp.left_shift(jnp.int32(1), o_k), 0)
        for o in range(n_off):
            lst_ref[n_need] = jnp.int32(b * 32 + o)
            n_need = n_need + (jnp.right_shift(mask, o) & 1)

    def coupling(idx, cs_ref):
        b = jnp.right_shift(idx, 5)
        o = idx & 31
        wg = wgeo_ref[b + o]
        ys = [[jnp.broadcast_to(wg[c:c + 1, h * LANES:(h + 1) * LANES], (CHUNK, LANES))
               for h in range(n_tiles)] for c in (0, 1, 2, 4)]
        for mc in range(unk // CHUNK):
            r = slice(mc * CHUNK, (mc + 1) * CHUNK)
            xs = [bc_ref[b, c, r, :] for c in range(4)]
            for h in range(n_tiles):
                d0 = xs[0] - ys[0][h]
                d1 = xs[1] - ys[1][h]
                d2 = xs[2] - ys[2][h]
                dd = d0 * d0 + d1 * d1 + d2 * d2 + xs[3] * ys[3][h]
                cs_ref[r, h * LANES:(h + 1) * LANES] = lax.rsqrt(dd).astype(jnp.bfloat16)

    def finish(idx, cs_ref):
        b = jnp.right_shift(idx, 5)
        o = idx & 31
        j = b + o
        left = jnp.dot(bs_ref[b], cs_ref[...], preferred_element_type=jnp.float32)
        left = (left * wgeo_ref[j, 3:4, :]).astype(jnp.bfloat16)
        ts_ref[b * n_off + o] = lax.dot_general(left, wpan_ref[j], (((1,), (1,)), ((), ())),
                                                preferred_element_type=jnp.float32)

    coupling(lst_ref[0], cs0_ref)

    def two_steps(t, carry):
        i = 2 * t + 1
        coupling(lst_ref[i], cs1_ref)
        finish(lst_ref[i - 1], cs0_ref)
        coupling(lst_ref[i + 1], cs0_ref)
        finish(lst_ref[i], cs1_ref)
        return carry

    lax.fori_loop(0, (n_need - 1) // 2, two_steps, 0)

    @pl.when(n_need % 2 == 0)
    def _():
        coupling(lst_ref[n_need - 1], cs1_ref)
        finish(lst_ref[n_need - 2], cs0_ref)
        finish(lst_ref[n_need - 1], cs1_ref)

    @pl.when(n_need % 2 == 1)
    def _():
        finish(lst_ref[n_need - 1], cs0_ref)

    for b in range(blk):
        for k, (o_k, live_k) in enumerate(slot_table(b)):
            t = ts_ref[b * n_off + o_k]
            t = jnp.where(live_k, t, jnp.zeros_like(t))
            cols_k = slice(k * nb_p, (k + 1) * nb_p)
            mine_ref[b, :, cols_k] = t[0:half_p]
            theirs_ref[b, :, cols_k] = t[half_p:].astype(theirs_ref.dtype)


def pack_kernel(pos_ref, len_ref, rad_ref, basis_ref, other_ref, msg_ref, *, blk, half_p):
    nb_p = 2 * half_p
    for w in range(blk):
        msg_ref[w, 0:half_p, :] = basis_ref[w]
        msg_ref[w, half_p:nb_p, :] = other_ref[w]
        g = jnp.concatenate([pos_ref[w], len_ref[w:w + 1, :], rad_ref[w:w + 1, :]], axis=0)
        hi = g.astype(jnp.bfloat16)
        r1 = g - hi.astype(jnp.float32)
        mid = r1.astype(jnp.bfloat16)
        lo = (r1 - mid.astype(jnp.float32)).astype(jnp.bfloat16)
        parts = jnp.concatenate([hi.astype(jnp.float32), mid.astype(jnp.float32),
                                 lo.astype(jnp.float32), jnp.zeros_like(g[0:1])], axis=0)
        msg_ref[w, nb_p:nb_p + 16, :] = parts.astype(jnp.bfloat16)


def on_device(basis, positions, seglen, radius, neighbours, counts):
    blk, half_p, unk = basis.shape
    nb_p = 2 * half_p
    half = unk // 2
    near = neighbours.shape[1]
    n_row = lax.axis_size("row")
    ci = lax.axis_index("col")

    other = lax.ppermute(basis, "col", [(0, 1), (1, 0)])

    msg = pl.pallas_call(
        functools.partial(pack_kernel, blk=blk, half_p=half_p),
        out_shape=jax.ShapeDtypeStruct((blk, nb_p + 16, unk), jnp.bfloat16),
    )(positions, seglen, radius, basis, other)
    pairs = [(2 * i, 2 * (i + 1)) for i in range(n_row - 1)]
    pairs += [(2 * (i + 1) + 1, 2 * i + 1) for i in range(n_row - 1)]
    hrecv = lax.ppermute(msg, ("row", "col"), pairs)
    hx = lax.ppermute(lax.dynamic_slice_in_dim(hrecv, (1 - ci) * half, half, axis=2),
                      "col", [(0, 1), (1, 0)])
    n_off = 2 * blk + 1

    def whole(shape):
        return pl.BlockSpec(shape, lambda i, *_: (0,) * len(shape))

    part_shape = (blk, half_p, near * nb_p)
    mine, theirs = pl.pallas_call(
        functools.partial(pair_kernel, blk=blk, near=near, unk=unk, half=half, half_p=half_p),
        out_shape=(jax.ShapeDtypeStruct(part_shape, jnp.float32),
                   jax.ShapeDtypeStruct(part_shape, jnp.bfloat16)),
        grid_spec=pltpu.PrefetchScalarGridSpec(
            num_scalar_prefetch=2,
            grid=(1,),
            in_specs=[whole(positions.shape), whole(seglen.shape), whole(radius.shape),
                      whole(basis.shape), whole(other.shape),
                      whole(hrecv.shape), whole(hx.shape)],
            out_specs=(whole(part_shape), whole(part_shape)),
            scratch_shapes=[
                pltpu.VMEM((3 * blk, 8, half), jnp.float32),
                pltpu.VMEM((3 * blk, nb_p, half), jnp.bfloat16),
                pltpu.VMEM((blk, 4, unk, LANES), jnp.float32),
                pltpu.VMEM((blk, nb_p, unk), jnp.bfloat16),
                pltpu.VMEM((unk, half), jnp.bfloat16),
                pltpu.VMEM((unk, half), jnp.bfloat16),
                pltpu.VMEM((blk * n_off, nb_p, nb_p), jnp.float32),
                pltpu.SMEM((blk * 32,), jnp.int32),
            ],
        ),
        compiler_params=pltpu.CompilerParams(dimension_semantics=("arbitrary",)),
    )(neighbours, counts, positions, seglen, radius, basis, other, hrecv, hx)

    return mine + lax.ppermute(theirs, "col", [(0, 1), (1, 0)]).astype(jnp.float32)


def solution(mesh):
    placed = (
        P("row", "col", None),
        P("row", None, None),
        P("row", None),
        P("row", None),
        P("row", None),
        P("row"),
    )
    return jax.shard_map(
        on_device, mesh=mesh, in_specs=placed, out_specs=P("row", "col", None), check_vma=False
    )
```

```python
import functools

import jax
import jax.numpy as jnp
from jax import lax
from jax.experimental import pallas as pl
from jax.experimental.pallas import tpu as pltpu
from jax.sharding import PartitionSpec as P


CHUNK = 8
GROUP = 128
LANES = 128


def pair_kernel(nb_ref, cnt_ref, pos_ref, len_ref, rad_ref, basis_ref, other_ref, *refs,
                phase, blk, near, unk, half, half_p):
    if phase == "own":
        (mine_ref, theirs_ref, bc_hbm,
         wgeo_ref, wpan_ref, bc_ref, bs_ref, cs0_ref, cs1_ref, ts_ref, lst_ref, sem) = refs
    else:
        (hrecv_ref, hx_ref, bc_hbm, pmine_ref, ptheirs_ref, mine_ref, theirs_ref,
         wgeo_ref, wpan_ref, bc_ref, bs_ref, cs0_ref, cs1_ref, ts_ref, lst_ref, sem) = refs
        bc_copy = pltpu.make_async_copy(bc_hbm, bc_ref, sem)
        bc_copy.start()
    ci = lax.axis_index("col")
    ri = lax.axis_index("row")
    n_off = 2 * blk + 1
    n_tiles = half // LANES
    nb_p = 2 * half_p

    for hsel in range(2):
        @pl.when(ci == hsel)
        def _():
            lanes = slice(hsel * half, (hsel + 1) * half)
            if phase == "own":
                for w in range(blk):
                    wgeo_ref[blk + w, 0:3, :] = pos_ref[w, :, lanes]
                    wgeo_ref[blk + w, 3:4, :] = len_ref[w:w + 1, lanes]
                    wgeo_ref[blk + w, 4:5, :] = rad_ref[w:w + 1, lanes]
                    first, second = (basis_ref, other_ref) if hsel == 0 else (other_ref, basis_ref)
                    wpan_ref[blk + w, 0:half_p, :] = first[w, :, lanes]
                    wpan_ref[blk + w, half_p:, :] = second[w, :, lanes]
                return
            if hsel == 0:
                sides = ((0, hrecv_ref, lanes, False), (2, hx_ref, slice(0, half), True))
            else:
                sides = ((2, hrecv_ref, lanes, True), (0, hx_ref, slice(0, half), False))
            for side, href, hl, swapped in sides:
                for w in range(blk):
                    g = href[w, nb_p:nb_p + 16, hl].astype(jnp.float32)
                    wgeo_ref[side * blk + w, 0:5, :] = g[0:5] + g[5:10] + g[10:15]
                    first = href[w, 0:half_p, hl]
                    second = href[w, half_p:nb_p, hl]
                    lo_rows, hi_rows = (second, first) if swapped else (first, second)
                    wpan_ref[side * blk + w, 0:half_p, :] = lo_rows
                    wpan_ref[side * blk + w, half_p:, :] = hi_rows

    def slot_table(b):
        gb = ri * blk + b
        cnt = cnt_ref[b]
        out = []
        for k in range(near):
            o_k = jnp.clip(nb_ref[b, k] - gb + blk, 0, 2 * blk)
            on_dev = (b + o_k >= blk) & (b + o_k < 2 * blk)
            use_k = (k < cnt) & (on_dev if phase == "own" else jnp.logical_not(on_dev))
            out.append((o_k, use_k))
        return out

    n_need = jnp.int32(0)
    for b in range(blk):
        if phase == "own":
            rows = jnp.concatenate([pos_ref[b], rad_ref[b:b + 1, :],
                                    jnp.zeros((LANES - 4, unk), jnp.float32)], axis=0)
            cols = jnp.transpose(rows)
            for c in range(4):
                bc_ref[b, c] = jnp.broadcast_to(cols[:, c:c + 1], (unk, LANES))
        s_row = len_ref[b:b + 1, :]
        bs_ref[b, 0:half_p, :] = (basis_ref[b].astype(jnp.float32) * s_row).astype(jnp.bfloat16)
        bs_ref[b, half_p:, :] = (other_ref[b].astype(jnp.float32) * s_row).astype(jnp.bfloat16)
        mask = jnp.int32(0)
        for o_k, live_k in slot_table(b):
            mask = mask | jnp.where(live_k, jnp.left_shift(jnp.int32(1), o_k), 0)
        for o in range(n_off):
            lst_ref[n_need] = jnp.int32(b * 32 + o)
            n_need = n_need + (jnp.right_shift(mask, o) & 1)

    def coupling(idx, cs_ref):
        b = jnp.right_shift(idx, 5)
        o = idx & 31
        wg = wgeo_ref[b + o]
        ys = [[jnp.broadcast_to(wg[c:c + 1, h * LANES:(h + 1) * LANES], (CHUNK, LANES))
               for h in range(n_tiles)] for c in (0, 1, 2, 4)]
        for mc in range(unk // CHUNK):
            r = slice(mc * CHUNK, (mc + 1) * CHUNK)
            xs = [bc_ref[b, c, r, :] for c in range(4)]
            for h in range(n_tiles):
                d0 = xs[0] - ys[0][h]
                d1 = xs[1] - ys[1][h]
                d2 = xs[2] - ys[2][h]
                dd = d0 * d0 + d1 * d1 + d2 * d2 + xs[3] * ys[3][h]
                cs_ref[r, h * LANES:(h + 1) * LANES] = lax.rsqrt(dd).astype(jnp.bfloat16)

    def finish(idx, cs_ref):
        b = jnp.right_shift(idx, 5)
        o = idx & 31
        j = b + o
        left = jnp.dot(bs_ref[b], cs_ref[...], preferred_element_type=jnp.float32)
        left = (left * wgeo_ref[j, 3:4, :]).astype(jnp.bfloat16)
        ts_ref[b * n_off + o] = lax.dot_general(left, wpan_ref[j], (((1,), (1,)), ((), ())),
                                                preferred_element_type=jnp.float32)

    if phase == "own":
        bc_copy = pltpu.make_async_copy(bc_ref, bc_hbm, sem)
        bc_copy.start()
    bc_copy.wait() if phase == "halo" else None

    @pl.when(n_need > 0)
    def _():
        coupling(lst_ref[0], cs0_ref)

    def two_steps(t, carry):
        i = 2 * t + 1
        coupling(lst_ref[i], cs1_ref)
        finish(lst_ref[i - 1], cs0_ref)
        coupling(lst_ref[i + 1], cs0_ref)
        finish(lst_ref[i], cs1_ref)
        return carry

    lax.fori_loop(0, jnp.maximum(n_need - 1, 0) // 2, two_steps, 0)

    @pl.when((n_need % 2 == 0) & (n_need > 0))
    def _():
        coupling(lst_ref[n_need - 1], cs1_ref)
        finish(lst_ref[n_need - 2], cs0_ref)
        finish(lst_ref[n_need - 1], cs1_ref)

    @pl.when(n_need % 2 == 1)
    def _():
        finish(lst_ref[n_need - 1], cs0_ref)

    for b in range(blk):
        for k, (o_k, live_k) in enumerate(slot_table(b)):
            t = ts_ref[b * n_off + o_k]
            cols_k = slice(k * nb_p, (k + 1) * nb_p)
            if phase == "own":
                t = jnp.where(live_k, t, jnp.zeros_like(t))
                mine_ref[b, :, cols_k] = t[0:half_p]
                theirs_ref[b, :, cols_k] = t[half_p:]
            else:
                mine_ref[b, :, cols_k] = jnp.where(live_k, t[0:half_p], pmine_ref[b, :, cols_k])
                theirs_ref[b, :, cols_k] = jnp.where(live_k, t[half_p:], ptheirs_ref[b, :, cols_k]
                                                     ).astype(theirs_ref.dtype)

    if phase == "own":
        bc_copy.wait()


def pack_kernel(pos_ref, len_ref, rad_ref, basis_ref, other_ref, msg_ref, *, blk, half_p):
    nb_p = 2 * half_p
    for w in range(blk):
        msg_ref[w, 0:half_p, :] = basis_ref[w]
        msg_ref[w, half_p:nb_p, :] = other_ref[w]
        g = jnp.concatenate([pos_ref[w], len_ref[w:w + 1, :], rad_ref[w:w + 1, :]], axis=0)
        hi = g.astype(jnp.bfloat16)
        r1 = g - hi.astype(jnp.float32)
        mid = r1.astype(jnp.bfloat16)
        lo = (r1 - mid.astype(jnp.float32)).astype(jnp.bfloat16)
        parts = jnp.concatenate([hi.astype(jnp.float32), mid.astype(jnp.float32),
                                 lo.astype(jnp.float32), jnp.zeros_like(g[0:1])], axis=0)
        msg_ref[w, nb_p:nb_p + 16, :] = parts.astype(jnp.bfloat16)


def on_device(basis, positions, seglen, radius, neighbours, counts):
    blk, half_p, unk = basis.shape
    nb_p = 2 * half_p
    half = unk // 2
    near = neighbours.shape[1]
    n_row = lax.axis_size("row")
    ci = lax.axis_index("col")

    other = lax.ppermute(basis, "col", [(0, 1), (1, 0)])

    msg = pl.pallas_call(
        functools.partial(pack_kernel, blk=blk, half_p=half_p),
        out_shape=jax.ShapeDtypeStruct((blk, nb_p + 16, unk), jnp.bfloat16),
    )(positions, seglen, radius, basis, other)
    pairs = [(2 * i, 2 * (i + 1)) for i in range(n_row - 1)]
    pairs += [(2 * (i + 1) + 1, 2 * i + 1) for i in range(n_row - 1)]
    hrecv = lax.ppermute(msg, ("row", "col"), pairs)
    n_off = 2 * blk + 1
    sizes = dict(blk=blk, near=near, unk=unk, half=half, half_p=half_p)

    def whole(shape):
        return pl.BlockSpec(shape, lambda i, *_: (0,) * len(shape))

    part_shape = (blk, half_p, near * nb_p)
    f32_part = jax.ShapeDtypeStruct(part_shape, jnp.float32)
    bc_shape = (blk, 4, unk, LANES)
    hbm = pl.BlockSpec(memory_space=pl.ANY)
    own_specs = [whole(positions.shape), whole(seglen.shape), whole(radius.shape),
                 whole(basis.shape), whole(other.shape)]
    scratch = [
        pltpu.VMEM((3 * blk, 8, half), jnp.float32),
        pltpu.VMEM((3 * blk, nb_p, half), jnp.bfloat16),
        pltpu.VMEM(bc_shape, jnp.float32),
        pltpu.VMEM((blk, nb_p, unk), jnp.bfloat16),
        pltpu.VMEM((unk, half), jnp.bfloat16),
        pltpu.VMEM((unk, half), jnp.bfloat16),
        pltpu.VMEM((blk * n_off, nb_p, nb_p), jnp.float32),
        pltpu.SMEM((blk * 32,), jnp.int32),
        pltpu.SemaphoreType.DMA(()),
    ]
    params = pltpu.CompilerParams(dimension_semantics=("arbitrary",))
    own_args = (neighbours, counts, positions, seglen, radius, basis, other)

    mine0, theirs0, bc = pl.pallas_call(
        functools.partial(pair_kernel, phase="own", **sizes),
        out_shape=(f32_part, f32_part, jax.ShapeDtypeStruct(bc_shape, jnp.float32)),
        grid_spec=pltpu.PrefetchScalarGridSpec(
            num_scalar_prefetch=2, grid=(1,), in_specs=own_specs,
            out_specs=(whole(part_shape), whole(part_shape), hbm), scratch_shapes=scratch),
        compiler_params=params,
    )(*own_args)

    hrecv, mine0, theirs0, bc = lax.optimization_barrier((hrecv, mine0, theirs0, bc))
    hx = lax.ppermute(lax.dynamic_slice_in_dim(hrecv, (1 - ci) * half, half, axis=2),
                      "col", [(0, 1), (1, 0)])

    mine, theirs = pl.pallas_call(
        functools.partial(pair_kernel, phase="halo", **sizes),
        out_shape=(f32_part, jax.ShapeDtypeStruct(part_shape, jnp.bfloat16)),
        grid_spec=pltpu.PrefetchScalarGridSpec(
            num_scalar_prefetch=2, grid=(1,),
            in_specs=own_specs + [whole(hrecv.shape), whole(hx.shape), hbm,
                                  whole(part_shape), whole(part_shape)],
            out_specs=(whole(part_shape), whole(part_shape)), scratch_shapes=scratch),
        compiler_params=params,
    )(*own_args, hrecv, hx, bc, mine0, theirs0)

    return mine + lax.ppermute(theirs, "col", [(0, 1), (1, 0)]).astype(jnp.float32)


def solution(mesh):
    placed = (
        P("row", "col", None),
        P("row", None, None),
        P("row", None),
        P("row", None),
        P("row", None),
        P("row"),
    )
    return jax.shard_map(
        on_device, mesh=mesh, in_specs=placed, out_specs=P("row", "col", None), check_vma=False
    )
```

```python
import functools

import jax
import jax.numpy as jnp
from jax import lax
from jax.experimental import pallas as pl
from jax.experimental.pallas import tpu as pltpu
from jax.sharding import PartitionSpec as P


CHUNK = 8
GROUP = 128
LANES = 128


def pair_kernel(nb_ref, cnt_ref, pos_ref, len_ref, rad_ref, basis_ref, other_ref,
                hrecv_ref, hx_ref, mine_ref, theirs_ref,
                wgeo_ref, wpan_ref, bc_ref, bs_ref, cs0_ref, cs1_ref, ts_ref, lst_ref,
                *, blk, near, unk, half, half_p):
    ci = lax.axis_index("col")
    ri = lax.axis_index("row")
    n_off = 2 * blk + 1
    n_tiles = half // LANES
    nb_p = 2 * half_p

    for hsel in range(2):
        @pl.when(ci == hsel)
        def _():
            lanes = slice(hsel * half, (hsel + 1) * half)
            if hsel == 0:
                sides = ((0, hrecv_ref, lanes, False), (2, hx_ref, slice(0, half), True))
            else:
                sides = ((2, hrecv_ref, lanes, True), (0, hx_ref, slice(0, half), False))
            for side, href, hl, swapped in sides:
                for w in range(blk):
                    g = href[w, nb_p:nb_p + 16, hl].astype(jnp.float32)
                    wgeo_ref[side * blk + w, 0:5, :] = g[0:5] + g[5:10] + g[10:15]
                    first = href[w, 0:half_p, hl]
                    second = href[w, half_p:nb_p, hl]
                    lo_rows, hi_rows = (second, first) if swapped else (first, second)
                    wpan_ref[side * blk + w, 0:half_p, :] = lo_rows
                    wpan_ref[side * blk + w, half_p:, :] = hi_rows
            for w in range(blk):
                wgeo_ref[blk + w, 0:3, :] = pos_ref[w, :, lanes]
                wgeo_ref[blk + w, 3:4, :] = len_ref[w:w + 1, lanes]
                wgeo_ref[blk + w, 4:5, :] = rad_ref[w:w + 1, lanes]
                first, second = (basis_ref, other_ref) if hsel == 0 else (other_ref, basis_ref)
                wpan_ref[blk + w, 0:half_p, :] = first[w, :, lanes]
                wpan_ref[blk + w, half_p:, :] = second[w, :, lanes]

    def slot_table(b):
        gb = ri * blk + b
        cnt = cnt_ref[b]
        out = []
        for k in range(near):
            o_k = jnp.clip(nb_ref[b, k] - gb + blk, 0, 2 * blk)
            out.append((o_k, k < cnt))
        return out

    n_need = jnp.int32(0)
    for b in range(blk):
        px = pos_ref[b] - 0.5
        sq = px[0:1] * px[0:1] + px[1:2] * px[1:2] + px[2:3] * px[2:3]
        rows = jnp.concatenate([px, rad_ref[b:b + 1, :], sq,
                                jnp.zeros((LANES - 5, unk), jnp.float32)], axis=0)
        cols = jnp.transpose(rows)
        for c in range(5):
            bc_ref[b, c] = jnp.broadcast_to(cols[:, c:c + 1], (unk, LANES))
        s_row = len_ref[b:b + 1, :]
        bs_ref[b, 0:half_p, :] = (basis_ref[b].astype(jnp.float32) * s_row).astype(jnp.bfloat16)
        bs_ref[b, half_p:, :] = (other_ref[b].astype(jnp.float32) * s_row).astype(jnp.bfloat16)
        mask = jnp.int32(0)
        for o_k, live_k in slot_table(b):
            mask = mask | jnp.where(live_k, jnp.left_shift(jnp.int32(1), o_k), 0)
        for o in range(n_off):
            lst_ref[n_need] = jnp.int32(b * 32 + o)
            n_need = n_need + (jnp.right_shift(mask, o) & 1)

    def coupling(idx, cs_ref):
        b = jnp.right_shift(idx, 5)
        o = idx & 31
        wg = wgeo_ref[b + o]
        yc = wg[0:3] - 0.5
        ysq = yc[0:1] * yc[0:1] + yc[1:2] * yc[1:2] + yc[2:3] * yc[2:3]
        yrows = [-2.0 * yc[0:1], -2.0 * yc[1:2], -2.0 * yc[2:3], wg[4:5], ysq]
        ys = [[jnp.broadcast_to(v[:, h * LANES:(h + 1) * LANES], (CHUNK, LANES))
               for h in range(n_tiles)] for v in yrows]
        for mc in range(unk // CHUNK):
            r = slice(mc * CHUNK, (mc + 1) * CHUNK)
            xs = [bc_ref[b, c, r, :] for c in range(5)]
            for h in range(n_tiles):
                dd = xs[4] + ys[4][h]
                dd = dd + xs[0] * ys[0][h]
                dd = dd + xs[1] * ys[1][h]
                dd = dd + xs[2] * ys[2][h]
                dd = dd + xs[3] * ys[3][h]
                cs_ref[r, h * LANES:(h + 1) * LANES] = lax.rsqrt(dd).astype(jnp.bfloat16)

    def finish(idx, cs_ref):
        b = jnp.right_shift(idx, 5)
        o = idx & 31
        j = b + o
        left = jnp.dot(bs_ref[b], cs_ref[...], preferred_element_type=jnp.float32)
        left = (left * wgeo_ref[j, 3:4, :]).astype(jnp.bfloat16)
        ts_ref[b * n_off + o] = lax.dot_general(left, wpan_ref[j], (((1,), (1,)), ((), ())),
                                                preferred_element_type=jnp.float32)

    coupling(lst_ref[0], cs0_ref)

    def two_steps(t, carry):
        i = 2 * t + 1
        coupling(lst_ref[i], cs1_ref)
        finish(lst_ref[i - 1], cs0_ref)
        coupling(lst_ref[i + 1], cs0_ref)
        finish(lst_ref[i], cs1_ref)
        return carry

    lax.fori_loop(0, (n_need - 1) // 2, two_steps, 0)

    @pl.when(n_need % 2 == 0)
    def _():
        coupling(lst_ref[n_need - 1], cs1_ref)
        finish(lst_ref[n_need - 2], cs0_ref)
        finish(lst_ref[n_need - 1], cs1_ref)

    @pl.when(n_need % 2 == 1)
    def _():
        finish(lst_ref[n_need - 1], cs0_ref)

    for b in range(blk):
        for k, (o_k, live_k) in enumerate(slot_table(b)):
            t = ts_ref[b * n_off + o_k]
            t = jnp.where(live_k, t, jnp.zeros_like(t))
            cols_k = slice(k * nb_p, (k + 1) * nb_p)
            mine_ref[b, :, cols_k] = t[0:half_p]
            theirs_ref[b, :, cols_k] = t[half_p:].astype(theirs_ref.dtype)


def pack_kernel(pos_ref, len_ref, rad_ref, basis_ref, other_ref, msg_ref, *, blk, half_p):
    nb_p = 2 * half_p
    for w in range(blk):
        msg_ref[w, 0:half_p, :] = basis_ref[w]
        msg_ref[w, half_p:nb_p, :] = other_ref[w]
        g = jnp.concatenate([pos_ref[w], len_ref[w:w + 1, :], rad_ref[w:w + 1, :]], axis=0)
        hi = g.astype(jnp.bfloat16)
        r1 = g - hi.astype(jnp.float32)
        mid = r1.astype(jnp.bfloat16)
        lo = (r1 - mid.astype(jnp.float32)).astype(jnp.bfloat16)
        parts = jnp.concatenate([hi.astype(jnp.float32), mid.astype(jnp.float32),
                                 lo.astype(jnp.float32), jnp.zeros_like(g[0:1])], axis=0)
        msg_ref[w, nb_p:nb_p + 16, :] = parts.astype(jnp.bfloat16)


def on_device(basis, positions, seglen, radius, neighbours, counts):
    blk, half_p, unk = basis.shape
    nb_p = 2 * half_p
    half = unk // 2
    near = neighbours.shape[1]
    n_row = lax.axis_size("row")
    ci = lax.axis_index("col")

    other = lax.ppermute(basis, "col", [(0, 1), (1, 0)])

    msg = pl.pallas_call(
        functools.partial(pack_kernel, blk=blk, half_p=half_p),
        out_shape=jax.ShapeDtypeStruct((blk, nb_p + 16, unk), jnp.bfloat16),
    )(positions, seglen, radius, basis, other)
    pairs = [(2 * i, 2 * (i + 1)) for i in range(n_row - 1)]
    pairs += [(2 * (i + 1) + 1, 2 * i + 1) for i in range(n_row - 1)]
    hrecv = lax.ppermute(msg, ("row", "col"), pairs)
    hx = lax.ppermute(lax.dynamic_slice_in_dim(hrecv, (1 - ci) * half, half, axis=2),
                      "col", [(0, 1), (1, 0)])
    n_off = 2 * blk + 1

    def whole(shape):
        return pl.BlockSpec(shape, lambda i, *_: (0,) * len(shape))

    part_shape = (blk, half_p, near * nb_p)
    mine, theirs = pl.pallas_call(
        functools.partial(pair_kernel, blk=blk, near=near, unk=unk, half=half, half_p=half_p),
        out_shape=(jax.ShapeDtypeStruct(part_shape, jnp.float32),
                   jax.ShapeDtypeStruct(part_shape, jnp.bfloat16)),
        grid_spec=pltpu.PrefetchScalarGridSpec(
            num_scalar_prefetch=2,
            grid=(1,),
            in_specs=[whole(positions.shape), whole(seglen.shape), whole(radius.shape),
                      whole(basis.shape), whole(other.shape),
                      whole(hrecv.shape), whole(hx.shape)],
            out_specs=(whole(part_shape), whole(part_shape)),
            scratch_shapes=[
                pltpu.VMEM((3 * blk, 8, half), jnp.float32),
                pltpu.VMEM((3 * blk, nb_p, half), jnp.bfloat16),
                pltpu.VMEM((blk, 5, unk, LANES), jnp.float32),
                pltpu.VMEM((blk, nb_p, unk), jnp.bfloat16),
                pltpu.VMEM((unk, half), jnp.bfloat16),
                pltpu.VMEM((unk, half), jnp.bfloat16),
                pltpu.VMEM((blk * n_off, nb_p, nb_p), jnp.float32),
                pltpu.SMEM((blk * 32,), jnp.int32),
            ],
        ),
        compiler_params=pltpu.CompilerParams(dimension_semantics=("arbitrary",)),
    )(neighbours, counts, positions, seglen, radius, basis, other, hrecv, hx)

    return mine + lax.ppermute(theirs, "col", [(0, 1), (1, 0)]).astype(jnp.float32)


def solution(mesh):
    placed = (
        P("row", "col", None),
        P("row", None, None),
        P("row", None),
        P("row", None),
        P("row", None),
        P("row"),
    )
    return jax.shard_map(
        on_device, mesh=mesh, in_specs=placed, out_specs=P("row", "col", None), check_vma=False
    )
```

```python
import functools

import jax
import jax.numpy as jnp
from jax import lax
from jax.experimental import pallas as pl
from jax.experimental.pallas import tpu as pltpu
from jax.sharding import PartitionSpec as P


CHUNK = 8
GROUP = 128
LANES = 128


def pair_kernel(nb_ref, cnt_ref, pos_ref, len_ref, rad_ref, basis_ref, other_ref,
                lo_ref, hi_ref, mine_ref, theirs_ref,
                wgeo_ref, wpan_ref, bc_ref, bs_ref, cs0_ref, cs1_ref, ts_ref, lst_ref,
                *, blk, near, unk, half, half_p):
    ci = lax.axis_index("col")
    ri = lax.axis_index("row")
    n_off = 2 * blk + 1
    n_tiles = half // LANES
    nb_p = 2 * half_p

    for hsel in range(2):
        @pl.when(ci == hsel)
        def _():
            lanes = slice(hsel * half, (hsel + 1) * half)
            sides = ((0, lo_ref, slice(0, half), hsel == 1), (2, hi_ref, slice(0, half), hsel == 1))
            for side, href, hl, swapped in sides:
                for w in range(blk):
                    g = href[w, nb_p:nb_p + 16, hl].astype(jnp.float32)
                    wgeo_ref[side * blk + w, 0:5, :] = g[0:5] + g[5:10] + g[10:15]
                    first = href[w, 0:half_p, hl]
                    second = href[w, half_p:nb_p, hl]
                    lo_rows, hi_rows = (second, first) if swapped else (first, second)
                    wpan_ref[side * blk + w, 0:half_p, :] = lo_rows
                    wpan_ref[side * blk + w, half_p:, :] = hi_rows
            for w in range(blk):
                wgeo_ref[blk + w, 0:3, :] = pos_ref[w, :, lanes]
                wgeo_ref[blk + w, 3:4, :] = len_ref[w:w + 1, lanes]
                wgeo_ref[blk + w, 4:5, :] = rad_ref[w:w + 1, lanes]
                first, second = (basis_ref, other_ref) if hsel == 0 else (other_ref, basis_ref)
                wpan_ref[blk + w, 0:half_p, :] = first[w, :, lanes]
                wpan_ref[blk + w, half_p:, :] = second[w, :, lanes]

    def slot_table(b):
        gb = ri * blk + b
        cnt = cnt_ref[b]
        out = []
        for k in range(near):
            o_k = jnp.clip(nb_ref[b, k] - gb + blk, 0, 2 * blk)
            out.append((o_k, k < cnt))
        return out

    n_need = jnp.int32(0)
    for b in range(blk):
        rows = jnp.concatenate([pos_ref[b], rad_ref[b:b + 1, :],
                                jnp.zeros((LANES - 4, unk), jnp.float32)], axis=0)
        cols = jnp.transpose(rows)
        for c in range(4):
            bc_ref[b, c] = jnp.broadcast_to(cols[:, c:c + 1], (unk, LANES))
        s_row = len_ref[b:b + 1, :]
        bs_ref[b, 0:half_p, :] = (basis_ref[b].astype(jnp.float32) * s_row).astype(jnp.bfloat16)
        bs_ref[b, half_p:, :] = (other_ref[b].astype(jnp.float32) * s_row).astype(jnp.bfloat16)
        mask = jnp.int32(0)
        for o_k, live_k in slot_table(b):
            mask = mask | jnp.where(live_k, jnp.left_shift(jnp.int32(1), o_k), 0)
        for o in range(n_off):
            lst_ref[n_need] = jnp.int32(b * 32 + o)
            n_need = n_need + (jnp.right_shift(mask, o) & 1)

    def coupling(idx, cs_ref):
        b = jnp.right_shift(idx, 5)
        o = idx & 31
        wg = wgeo_ref[b + o]
        ys = [[jnp.broadcast_to(wg[c:c + 1, h * LANES:(h + 1) * LANES], (CHUNK, LANES))
               for h in range(n_tiles)] for c in (0, 1, 2, 4)]
        for mc in range(unk // CHUNK):
            r = slice(mc * CHUNK, (mc + 1) * CHUNK)
            xs = [bc_ref[b, c, r, :] for c in range(4)]
            for h in range(n_tiles):
                d0 = xs[0] - ys[0][h]
                d1 = xs[1] - ys[1][h]
                d2 = xs[2] - ys[2][h]
                dd = d0 * d0 + d1 * d1 + d2 * d2 + xs[3] * ys[3][h]
                cs_ref[r, h * LANES:(h + 1) * LANES] = lax.rsqrt(dd).astype(jnp.bfloat16)

    def finish(idx, cs_ref):
        b = jnp.right_shift(idx, 5)
        o = idx & 31
        j = b + o
        left = jnp.dot(bs_ref[b], cs_ref[...], preferred_element_type=jnp.float32)
        left = (left * wgeo_ref[j, 3:4, :]).astype(jnp.bfloat16)
        ts_ref[b * n_off + o] = lax.dot_general(left, wpan_ref[j], (((1,), (1,)), ((), ())),
                                                preferred_element_type=jnp.float32)

    coupling(lst_ref[0], cs0_ref)

    def two_steps(t, carry):
        i = 2 * t + 1
        coupling(lst_ref[i], cs1_ref)
        finish(lst_ref[i - 1], cs0_ref)
        coupling(lst_ref[i + 1], cs0_ref)
        finish(lst_ref[i], cs1_ref)
        return carry

    lax.fori_loop(0, (n_need - 1) // 2, two_steps, 0)

    @pl.when(n_need % 2 == 0)
    def _():
        coupling(lst_ref[n_need - 1], cs1_ref)
        finish(lst_ref[n_need - 2], cs0_ref)
        finish(lst_ref[n_need - 1], cs1_ref)

    @pl.when(n_need % 2 == 1)
    def _():
        finish(lst_ref[n_need - 1], cs0_ref)

    for b in range(blk):
        for k, (o_k, live_k) in enumerate(slot_table(b)):
            t = ts_ref[b * n_off + o_k]
            t = jnp.where(live_k, t, jnp.zeros_like(t))
            cols_k = slice(k * nb_p, (k + 1) * nb_p)
            mine_ref[b, :, cols_k] = t[0:half_p]
            theirs_ref[b, :, cols_k] = t[half_p:].astype(theirs_ref.dtype)


def pack_kernel(pos_ref, len_ref, rad_ref, basis_ref, other_ref, msg_ref, *, blk, half_p, half):
    nb_p = 2 * half_p
    ci = lax.axis_index("col")
    for hsel in range(2):
        @pl.when(ci == hsel)
        def _():
            lanes = slice(hsel * half, (hsel + 1) * half)
            for w in range(blk):
                msg_ref[w, 0:half_p, :] = basis_ref[w, :, lanes]
                msg_ref[w, half_p:nb_p, :] = other_ref[w, :, lanes]
                g = jnp.concatenate([pos_ref[w, :, lanes], len_ref[w:w + 1, lanes],
                                     rad_ref[w:w + 1, lanes]], axis=0)
                hi = g.astype(jnp.bfloat16)
                r1 = g - hi.astype(jnp.float32)
                mid = r1.astype(jnp.bfloat16)
                lo = (r1 - mid.astype(jnp.float32)).astype(jnp.bfloat16)
                parts = jnp.concatenate([hi.astype(jnp.float32), mid.astype(jnp.float32),
                                         lo.astype(jnp.float32), jnp.zeros_like(g[0:1])], axis=0)
                msg_ref[w, nb_p:nb_p + 16, :] = parts.astype(jnp.bfloat16)


def on_device(basis, positions, seglen, radius, neighbours, counts):
    blk, half_p, unk = basis.shape
    nb_p = 2 * half_p
    half = unk // 2
    near = neighbours.shape[1]
    n_row = lax.axis_size("row")
    ci = lax.axis_index("col")

    other = lax.ppermute(basis, "col", [(0, 1), (1, 0)])

    msg = pl.pallas_call(
        functools.partial(pack_kernel, blk=blk, half_p=half_p, half=half),
        out_shape=jax.ShapeDtypeStruct((blk, nb_p + 16, half), jnp.bfloat16),
    )(positions, seglen, radius, basis, other)
    fwd = [(i, i + 1) for i in range(n_row - 1)]
    bwd = [(i + 1, i) for i in range(n_row - 1)]
    lo = lax.ppermute(msg, "row", fwd)
    hi = lax.ppermute(msg, "row", bwd)
    n_off = 2 * blk + 1

    def whole(shape):
        return pl.BlockSpec(shape, lambda i, *_: (0,) * len(shape))

    part_shape = (blk, half_p, near * nb_p)
    mine, theirs = pl.pallas_call(
        functools.partial(pair_kernel, blk=blk, near=near, unk=unk, half=half, half_p=half_p),
        out_shape=(jax.ShapeDtypeStruct(part_shape, jnp.float32),
                   jax.ShapeDtypeStruct(part_shape, jnp.bfloat16)),
        grid_spec=pltpu.PrefetchScalarGridSpec(
            num_scalar_prefetch=2,
            grid=(1,),
            in_specs=[whole(positions.shape), whole(seglen.shape), whole(radius.shape),
                      whole(basis.shape), whole(other.shape),
                      whole(lo.shape), whole(hi.shape)],
            out_specs=(whole(part_shape), whole(part_shape)),
            scratch_shapes=[
                pltpu.VMEM((3 * blk, 8, half), jnp.float32),
                pltpu.VMEM((3 * blk, nb_p, half), jnp.bfloat16),
                pltpu.VMEM((blk, 4, unk, LANES), jnp.float32),
                pltpu.VMEM((blk, nb_p, unk), jnp.bfloat16),
                pltpu.VMEM((unk, half), jnp.bfloat16),
                pltpu.VMEM((unk, half), jnp.bfloat16),
                pltpu.VMEM((blk * n_off, nb_p, nb_p), jnp.float32),
                pltpu.SMEM((blk * 32,), jnp.int32),
            ],
        ),
        compiler_params=pltpu.CompilerParams(dimension_semantics=("arbitrary",)),
    )(neighbours, counts, positions, seglen, radius, basis, other, lo, hi)

    return mine + lax.ppermute(theirs, "col", [(0, 1), (1, 0)]).astype(jnp.float32)


def solution(mesh):
    placed = (
        P("row", "col", None),
        P("row", None, None),
        P("row", None),
        P("row", None),
        P("row", None),
        P("row"),
    )
    return jax.shard_map(
        on_device, mesh=mesh, in_specs=placed, out_specs=P("row", "col", None), check_vma=False
    )
```

```python
import functools

import jax
import jax.numpy as jnp
from jax import lax
from jax.experimental import pallas as pl
from jax.experimental.pallas import tpu as pltpu
from jax.sharding import PartitionSpec as P


CHUNK = 8
GROUP = 128
LANES = 128


def pair_kernel(nb_ref, cnt_ref, pos_ref, len_ref, rad_ref, basis_ref, other_ref,
                hrecv_ref, hx_ref, mine_ref, theirs_ref,
                wgeo_ref, wpan_ref, bc_ref, bs_ref, cs0_ref, cs1_ref, ts_ref, lst_ref,
                *, blk, near, unk, half, half_p):
    ci = lax.axis_index("col")
    ri = lax.axis_index("row")
    n_off = 2 * blk + 1
    n_tiles = half // LANES
    nb_p = 2 * half_p

    for hsel in range(2):
        @pl.when(ci == hsel)
        def _():
            lanes = slice(hsel * half, (hsel + 1) * half)
            if hsel == 0:
                sides = ((0, hrecv_ref, lanes, False), (2, hx_ref, slice(0, half), True))
            else:
                sides = ((2, hrecv_ref, lanes, True), (0, hx_ref, slice(0, half), False))
            for side, href, hl, swapped in sides:
                for w in range(blk):
                    g = href[w, nb_p:nb_p + 16, hl].astype(jnp.float32)
                    wgeo_ref[side * blk + w, 0:5, :] = g[0:5] + g[5:10] + g[10:15]
                    first = href[w, 0:half_p, hl]
                    second = href[w, half_p:nb_p, hl]
                    lo_rows, hi_rows = (second, first) if swapped else (first, second)
                    wpan_ref[side * blk + w, 0:half_p, :] = lo_rows
                    wpan_ref[side * blk + w, half_p:, :] = hi_rows
            for w in range(blk):
                for c in range(3):
                    wgeo_ref[blk + w, c:c + 1, :] = pos_ref[c, w:w + 1, lanes]
                wgeo_ref[blk + w, 3:4, :] = len_ref[w:w + 1, lanes]
                wgeo_ref[blk + w, 4:5, :] = rad_ref[w:w + 1, lanes]
                first, second = (basis_ref, other_ref) if hsel == 0 else (other_ref, basis_ref)
                wpan_ref[blk + w, 0:half_p, :] = first[w, :, lanes]
                wpan_ref[blk + w, half_p:, :] = second[w, :, lanes]

    def slot_table(b):
        gb = ri * blk + b
        cnt = cnt_ref[b]
        out = []
        for k in range(near):
            o_k = jnp.clip(nb_ref[b, k] - gb + blk, 0, 2 * blk)
            out.append((o_k, k < cnt))
        return out

    n_need = jnp.int32(0)
    for b in range(blk):
        rows = jnp.concatenate([pos_ref[c, b:b + 1, :] for c in range(3)] + [rad_ref[b:b + 1, :],
                                jnp.zeros((LANES - 4, unk), jnp.float32)], axis=0)
        cols = jnp.transpose(rows)
        for c in range(4):
            bc_ref[b, c] = jnp.broadcast_to(cols[:, c:c + 1], (unk, LANES))
        s_row = len_ref[b:b + 1, :]
        bs_ref[b, 0:half_p, :] = (basis_ref[b].astype(jnp.float32) * s_row).astype(jnp.bfloat16)
        bs_ref[b, half_p:, :] = (other_ref[b].astype(jnp.float32) * s_row).astype(jnp.bfloat16)
        mask = jnp.int32(0)
        for o_k, live_k in slot_table(b):
            mask = mask | jnp.where(live_k, jnp.left_shift(jnp.int32(1), o_k), 0)
        for o in range(n_off):
            lst_ref[n_need] = jnp.int32(b * 32 + o)
            n_need = n_need + (jnp.right_shift(mask, o) & 1)

    def coupling(idx, cs_ref):
        b = jnp.right_shift(idx, 5)
        o = idx & 31
        wg = wgeo_ref[b + o]
        ys = [[jnp.broadcast_to(wg[c:c + 1, h * LANES:(h + 1) * LANES], (CHUNK, LANES))
               for h in range(n_tiles)] for c in (0, 1, 2, 4)]
        for mc in range(unk // CHUNK):
            r = slice(mc * CHUNK, (mc + 1) * CHUNK)
            xs = [bc_ref[b, c, r, :] for c in range(4)]
            for h in range(n_tiles):
                d0 = xs[0] - ys[0][h]
                d1 = xs[1] - ys[1][h]
                d2 = xs[2] - ys[2][h]
                dd = d0 * d0 + d1 * d1 + d2 * d2 + xs[3] * ys[3][h]
                cs_ref[r, h * LANES:(h + 1) * LANES] = lax.rsqrt(dd).astype(jnp.bfloat16)

    def finish(idx, cs_ref):
        b = jnp.right_shift(idx, 5)
        o = idx & 31
        j = b + o
        left = jnp.dot(bs_ref[b], cs_ref[...], preferred_element_type=jnp.float32)
        left = (left * wgeo_ref[j, 3:4, :]).astype(jnp.bfloat16)
        ts_ref[b * n_off + o] = lax.dot_general(left, wpan_ref[j], (((1,), (1,)), ((), ())),
                                                preferred_element_type=jnp.float32)

    coupling(lst_ref[0], cs0_ref)

    def two_steps(t, carry):
        i = 2 * t + 1
        coupling(lst_ref[i], cs1_ref)
        finish(lst_ref[i - 1], cs0_ref)
        coupling(lst_ref[i + 1], cs0_ref)
        finish(lst_ref[i], cs1_ref)
        return carry

    lax.fori_loop(0, (n_need - 1) // 2, two_steps, 0)

    @pl.when(n_need % 2 == 0)
    def _():
        coupling(lst_ref[n_need - 1], cs1_ref)
        finish(lst_ref[n_need - 2], cs0_ref)
        finish(lst_ref[n_need - 1], cs1_ref)

    @pl.when(n_need % 2 == 1)
    def _():
        finish(lst_ref[n_need - 1], cs0_ref)

    for b in range(blk):
        for k, (o_k, live_k) in enumerate(slot_table(b)):
            t = ts_ref[b * n_off + o_k]
            t = jnp.where(live_k, t, jnp.zeros_like(t))
            cols_k = slice(k * nb_p, (k + 1) * nb_p)
            mine_ref[b, :, cols_k] = t[0:half_p]
            theirs_ref[b, :, cols_k] = t[half_p:].astype(theirs_ref.dtype)


def pack_kernel(pos_ref, len_ref, rad_ref, basis_ref, other_ref, msg_ref, *, blk, half_p):
    nb_p = 2 * half_p
    for w in range(blk):
        msg_ref[w, 0:half_p, :] = basis_ref[w]
        msg_ref[w, half_p:nb_p, :] = other_ref[w]
        g = jnp.concatenate([pos_ref[c, w:w + 1, :] for c in range(3)]
                            + [len_ref[w:w + 1, :], rad_ref[w:w + 1, :]], axis=0)
        hi = g.astype(jnp.bfloat16)
        r1 = g - hi.astype(jnp.float32)
        mid = r1.astype(jnp.bfloat16)
        lo = (r1 - mid.astype(jnp.float32)).astype(jnp.bfloat16)
        parts = jnp.concatenate([hi.astype(jnp.float32), mid.astype(jnp.float32),
                                 lo.astype(jnp.float32), jnp.zeros_like(g[0:1])], axis=0)
        msg_ref[w, nb_p:nb_p + 16, :] = parts.astype(jnp.bfloat16)


def on_device(basis, positions, seglen, radius, neighbours, counts):
    blk, half_p, unk = basis.shape
    nb_p = 2 * half_p
    half = unk // 2
    near = neighbours.shape[1]
    n_row = lax.axis_size("row")
    ci = lax.axis_index("col")

    other = lax.ppermute(basis, "col", [(0, 1), (1, 0)])
    positions = jnp.transpose(positions, (1, 0, 2))

    msg = pl.pallas_call(
        functools.partial(pack_kernel, blk=blk, half_p=half_p),
        out_shape=jax.ShapeDtypeStruct((blk, nb_p + 16, unk), jnp.bfloat16),
    )(positions, seglen, radius, basis, other)
    pairs = [(2 * i, 2 * (i + 1)) for i in range(n_row - 1)]
    pairs += [(2 * (i + 1) + 1, 2 * i + 1) for i in range(n_row - 1)]
    hrecv = lax.ppermute(msg, ("row", "col"), pairs)
    hx = lax.ppermute(lax.dynamic_slice_in_dim(hrecv, (1 - ci) * half, half, axis=2),
                      "col", [(0, 1), (1, 0)])
    n_off = 2 * blk + 1

    def whole(shape):
        return pl.BlockSpec(shape, lambda i, *_: (0,) * len(shape))

    part_shape = (blk, half_p, near * nb_p)
    mine, theirs = pl.pallas_call(
        functools.partial(pair_kernel, blk=blk, near=near, unk=unk, half=half, half_p=half_p),
        out_shape=(jax.ShapeDtypeStruct(part_shape, jnp.float32),
                   jax.ShapeDtypeStruct(part_shape, jnp.bfloat16)),
        grid_spec=pltpu.PrefetchScalarGridSpec(
            num_scalar_prefetch=2,
            grid=(1,),
            in_specs=[whole(positions.shape), whole(seglen.shape), whole(radius.shape),
                      whole(basis.shape), whole(other.shape),
                      whole(hrecv.shape), whole(hx.shape)],
            out_specs=(whole(part_shape), whole(part_shape)),
            scratch_shapes=[
                pltpu.VMEM((3 * blk, 8, half), jnp.float32),
                pltpu.VMEM((3 * blk, nb_p, half), jnp.bfloat16),
                pltpu.VMEM((blk, 4, unk, LANES), jnp.float32),
                pltpu.VMEM((blk, nb_p, unk), jnp.bfloat16),
                pltpu.VMEM((unk, half), jnp.bfloat16),
                pltpu.VMEM((unk, half), jnp.bfloat16),
                pltpu.VMEM((blk * n_off, nb_p, nb_p), jnp.float32),
                pltpu.SMEM((blk * 32,), jnp.int32),
            ],
        ),
        compiler_params=pltpu.CompilerParams(dimension_semantics=("arbitrary",)),
    )(neighbours, counts, positions, seglen, radius, basis, other, hrecv, hx)

    return mine + lax.ppermute(theirs, "col", [(0, 1), (1, 0)]).astype(jnp.float32)


def solution(mesh):
    placed = (
        P("row", "col", None),
        P("row", None, None),
        P("row", None),
        P("row", None),
        P("row", None),
        P("row"),
    )
    return jax.shard_map(
        on_device, mesh=mesh, in_specs=placed, out_specs=P("row", "col", None), check_vma=False
    )
```

```python
import functools

import jax
import jax.numpy as jnp
from jax import lax
from jax.experimental import pallas as pl
from jax.experimental.pallas import tpu as pltpu
from jax.sharding import PartitionSpec as P


CHUNK = 8
GROUP = 128
LANES = 128


def pair_kernel(nb_ref, cnt_ref, pos_ref, len_ref, rad_ref, basis_ref, other_ref,
                hrecv_ref, hx_ref, mine_ref, theirs_ref,
                wgeo_ref, wpan_ref, bc_ref, bs_ref, cs0_ref, cs1_ref, ts_ref, lst_ref,
                *, blk, near, unk, half, half_p):
    ci = lax.axis_index("col")
    ri = lax.axis_index("row")
    n_off = 2 * blk + 1
    n_tiles = half // LANES
    nb_p = 2 * half_p

    for hsel in range(2):
        @pl.when(ci == hsel)
        def _():
            lanes = slice(hsel * half, (hsel + 1) * half)
            if hsel == 0:
                sides = ((0, hrecv_ref, lanes, False), (2, hx_ref, slice(0, half), True))
            else:
                sides = ((2, hrecv_ref, lanes, True), (0, hx_ref, slice(0, half), False))
            for side, href, hl, swapped in sides:
                for w in range(blk):
                    g = href[w, nb_p:nb_p + 16, hl].astype(jnp.float32)
                    wgeo_ref[side * blk + w, 0:5, :] = g[0:5] + g[5:10] + g[10:15]
                    first = href[w, 0:half_p, hl]
                    second = href[w, half_p:nb_p, hl]
                    lo_rows, hi_rows = (second, first) if swapped else (first, second)
                    wpan_ref[side * blk + w, 0:half_p, :] = lo_rows
                    wpan_ref[side * blk + w, half_p:, :] = hi_rows
            for w in range(blk):
                wgeo_ref[blk + w, 0:3, :] = pos_ref[w, :, lanes]
                wgeo_ref[blk + w, 3:4, :] = len_ref[w:w + 1, lanes]
                wgeo_ref[blk + w, 4:5, :] = rad_ref[w:w + 1, lanes]
                first, second = (basis_ref, other_ref) if hsel == 0 else (other_ref, basis_ref)
                wpan_ref[blk + w, 0:half_p, :] = first[w, :, lanes]
                wpan_ref[blk + w, half_p:, :] = second[w, :, lanes]

    def slot_table(b):
        gb = ri * blk + b
        cnt = cnt_ref[b]
        out = []
        for k in range(near):
            o_k = jnp.clip(nb_ref[b, k] - gb + blk, 0, 2 * blk)
            out.append((o_k, k < cnt))
        return out

    n_need = jnp.int32(0)
    for b in range(blk):
        rows = jnp.concatenate([pos_ref[b], rad_ref[b:b + 1, :],
                                jnp.zeros((LANES - 4, unk), jnp.float32)], axis=0)
        cols = jnp.transpose(rows)
        for c in range(4):
            bc_ref[b, c] = jnp.broadcast_to(cols[:, c:c + 1], (unk, LANES))
        s_row = len_ref[b:b + 1, :]
        bs_ref[b, 0:half_p, :] = (basis_ref[b].astype(jnp.float32) * s_row).astype(jnp.bfloat16)
        bs_ref[b, half_p:, :] = (other_ref[b].astype(jnp.float32) * s_row).astype(jnp.bfloat16)
        mask = jnp.int32(0)
        for o_k, live_k in slot_table(b):
            mask = mask | jnp.where(live_k, jnp.left_shift(jnp.int32(1), o_k), 0)
        for o in range(n_off):
            lst_ref[n_need] = jnp.int32(b * 32 + o)
            n_need = n_need + (jnp.right_shift(mask, o) & 1)

    def coupling(idx, cs_ref):
        b = jnp.right_shift(idx, 5)
        o = idx & 31
        wg = wgeo_ref[b + o]
        ys = [[jnp.broadcast_to(wg[c:c + 1, h * LANES:(h + 1) * LANES], (CHUNK, LANES))
               for h in range(n_tiles)] for c in (0, 1, 2, 4)]
        for mc in range(unk // CHUNK):
            r = slice(mc * CHUNK, (mc + 1) * CHUNK)
            xs = [bc_ref[b, c, r, :] for c in range(4)]
            for h in range(n_tiles):
                d0 = xs[0] - ys[0][h]
                d1 = xs[1] - ys[1][h]
                d2 = xs[2] - ys[2][h]
                dd = d0 * d0 + d1 * d1 + d2 * d2 + xs[3] * ys[3][h]
                cs_ref[r, h * LANES:(h + 1) * LANES] = lax.rsqrt(dd).astype(jnp.bfloat16)

    def finish(idx, cs_ref):
        b = jnp.right_shift(idx, 5)
        o = idx & 31
        j = b + o
        left = jnp.dot(bs_ref[b], cs_ref[...], preferred_element_type=jnp.float32)
        left = (left * wgeo_ref[j, 3:4, :]).astype(jnp.bfloat16)
        ts_ref[b * n_off + o] = lax.dot_general(left, wpan_ref[j], (((1,), (1,)), ((), ())),
                                                preferred_element_type=jnp.float32)

    coupling(lst_ref[0], cs0_ref)

    def two_steps(t, carry):
        i = 2 * t + 1
        coupling(lst_ref[i], cs1_ref)
        finish(lst_ref[i - 1], cs0_ref)
        coupling(lst_ref[i + 1], cs0_ref)
        finish(lst_ref[i], cs1_ref)
        return carry

    lax.fori_loop(0, (n_need - 1) // 2, two_steps, 0)

    @pl.when(n_need % 2 == 0)
    def _():
        coupling(lst_ref[n_need - 1], cs1_ref)
        finish(lst_ref[n_need - 2], cs0_ref)
        finish(lst_ref[n_need - 1], cs1_ref)

    @pl.when(n_need % 2 == 1)
    def _():
        finish(lst_ref[n_need - 1], cs0_ref)

    for b in range(blk):
        for k, (o_k, live_k) in enumerate(slot_table(b)):
            t = ts_ref[b * n_off + o_k]
            t = jnp.where(live_k, t, jnp.zeros_like(t))
            cols_k = slice(k * nb_p, (k + 1) * nb_p)
            mine_ref[b, :, cols_k] = t[0:half_p]
            theirs_ref[b, :, cols_k] = t[half_p:].astype(theirs_ref.dtype)


def pack_kernel(pos_ref, len_ref, rad_ref, basis_ref, other_ref, msg_ref, *, blk, half_p):
    nb_p = 2 * half_p
    for w in range(blk):
        msg_ref[w, 0:half_p, :] = basis_ref[w]
        msg_ref[w, half_p:nb_p, :] = other_ref[w]
        g = jnp.concatenate([pos_ref[w], len_ref[w:w + 1, :], rad_ref[w:w + 1, :]], axis=0)
        hi = g.astype(jnp.bfloat16)
        r1 = g - hi.astype(jnp.float32)
        mid = r1.astype(jnp.bfloat16)
        lo = (r1 - mid.astype(jnp.float32)).astype(jnp.bfloat16)
        parts = jnp.concatenate([hi.astype(jnp.float32), mid.astype(jnp.float32),
                                 lo.astype(jnp.float32), jnp.zeros_like(g[0:1])], axis=0)
        msg_ref[w, nb_p:nb_p + 16, :] = parts.astype(jnp.bfloat16)


def add_kernel(mine_ref, recv_ref, out_ref):
    out_ref[...] = mine_ref[...] + recv_ref[...].astype(jnp.float32)


def on_device(basis, positions, seglen, radius, neighbours, counts):
    blk, half_p, unk = basis.shape
    nb_p = 2 * half_p
    half = unk // 2
    near = neighbours.shape[1]
    n_row = lax.axis_size("row")
    ci = lax.axis_index("col")

    other = lax.ppermute(basis, "col", [(0, 1), (1, 0)])

    msg = pl.pallas_call(
        functools.partial(pack_kernel, blk=blk, half_p=half_p),
        out_shape=jax.ShapeDtypeStruct((blk, nb_p + 16, unk), jnp.bfloat16),
    )(positions, seglen, radius, basis, other)
    pairs = [(2 * i, 2 * (i + 1)) for i in range(n_row - 1)]
    pairs += [(2 * (i + 1) + 1, 2 * i + 1) for i in range(n_row - 1)]
    hrecv = lax.ppermute(msg, ("row", "col"), pairs)
    hx = lax.ppermute(lax.dynamic_slice_in_dim(hrecv, (1 - ci) * half, half, axis=2),
                      "col", [(0, 1), (1, 0)])
    n_off = 2 * blk + 1

    def whole(shape):
        return pl.BlockSpec(shape, lambda i, *_: (0,) * len(shape))

    part_shape = (blk, half_p, near * nb_p)
    mine, theirs = pl.pallas_call(
        functools.partial(pair_kernel, blk=blk, near=near, unk=unk, half=half, half_p=half_p),
        out_shape=(jax.ShapeDtypeStruct(part_shape, jnp.float32),
                   jax.ShapeDtypeStruct(part_shape, jnp.bfloat16)),
        grid_spec=pltpu.PrefetchScalarGridSpec(
            num_scalar_prefetch=2,
            grid=(1,),
            in_specs=[whole(positions.shape), whole(seglen.shape), whole(radius.shape),
                      whole(basis.shape), whole(other.shape),
                      whole(hrecv.shape), whole(hx.shape)],
            out_specs=(whole(part_shape), whole(part_shape)),
            scratch_shapes=[
                pltpu.VMEM((3 * blk, 8, half), jnp.float32),
                pltpu.VMEM((3 * blk, nb_p, half), jnp.bfloat16),
                pltpu.VMEM((blk, 4, unk, LANES), jnp.float32),
                pltpu.VMEM((blk, nb_p, unk), jnp.bfloat16),
                pltpu.VMEM((unk, half), jnp.bfloat16),
                pltpu.VMEM((unk, half), jnp.bfloat16),
                pltpu.VMEM((blk * n_off, nb_p, nb_p), jnp.float32),
                pltpu.SMEM((blk * 32,), jnp.int32),
            ],
        ),
        compiler_params=pltpu.CompilerParams(dimension_semantics=("arbitrary",)),
    )(neighbours, counts, positions, seglen, radius, basis, other, hrecv, hx)

    recv = lax.ppermute(theirs, "col", [(0, 1), (1, 0)])
    step = pl.BlockSpec((1, half_p, near * nb_p), lambda b: (b, 0, 0))
    return pl.pallas_call(
        add_kernel,
        out_shape=jax.ShapeDtypeStruct(part_shape, jnp.float32),
        grid=(blk,),
        in_specs=[step, step],
        out_specs=step,
        input_output_aliases={0: 0},
    )(mine, recv)


def solution(mesh):
    placed = (
        P("row", "col", None),
        P("row", None, None),
        P("row", None),
        P("row", None),
        P("row", None),
        P("row"),
    )
    return jax.shard_map(
        on_device, mesh=mesh, in_specs=placed, out_specs=P("row", "col", None), check_vma=False
    )
```

```python
import functools

import jax
import jax.numpy as jnp
from jax import lax
from jax.experimental import pallas as pl
from jax.experimental.pallas import tpu as pltpu
from jax.sharding import PartitionSpec as P


CHUNK = 8
GROUP = 128
LANES = 128


def pair_kernel(nb_ref, cnt_ref, pos_ref, len_ref, rad_ref, basis_ref, other_ref,
                hrecv_ref, hx_ref, bc_hbm, mine_ref, theirs_ref,
                wgeo_ref, wpan_ref, bc_ref, bs_ref, cs0_ref, cs1_ref, ts_ref, lst_ref, sem,
                *, blk, near, unk, half, half_p):
    ci = lax.axis_index("col")
    ri = lax.axis_index("row")
    n_off = 2 * blk + 1
    n_tiles = half // LANES
    nb_p = 2 * half_p
    bc_copy = pltpu.make_async_copy(bc_hbm, bc_ref, sem)
    bc_copy.start()

    for hsel in range(2):
        @pl.when(ci == hsel)
        def _():
            lanes = slice(hsel * half, (hsel + 1) * half)
            if hsel == 0:
                sides = ((0, hrecv_ref, lanes, False), (2, hx_ref, slice(0, half), True))
            else:
                sides = ((2, hrecv_ref, lanes, True), (0, hx_ref, slice(0, half), False))
            for side, href, hl, swapped in sides:
                for w in range(blk):
                    g = href[w, nb_p:nb_p + 16, hl].astype(jnp.float32)
                    wgeo_ref[side * blk + w, 0:5, :] = g[0:5] + g[5:10] + g[10:15]
                    first = href[w, 0:half_p, hl]
                    second = href[w, half_p:nb_p, hl]
                    lo_rows, hi_rows = (second, first) if swapped else (first, second)
                    wpan_ref[side * blk + w, 0:half_p, :] = lo_rows
                    wpan_ref[side * blk + w, half_p:, :] = hi_rows
            for w in range(blk):
                wgeo_ref[blk + w, 0:3, :] = pos_ref[w, :, lanes]
                wgeo_ref[blk + w, 3:4, :] = len_ref[w:w + 1, lanes]
                wgeo_ref[blk + w, 4:5, :] = rad_ref[w:w + 1, lanes]
                first, second = (basis_ref, other_ref) if hsel == 0 else (other_ref, basis_ref)
                wpan_ref[blk + w, 0:half_p, :] = first[w, :, lanes]
                wpan_ref[blk + w, half_p:, :] = second[w, :, lanes]

    def slot_table(b):
        gb = ri * blk + b
        cnt = cnt_ref[b]
        out = []
        for k in range(near):
            o_k = jnp.clip(nb_ref[b, k] - gb + blk, 0, 2 * blk)
            out.append((o_k, k < cnt))
        return out

    n_need = jnp.int32(0)
    for b in range(blk):
        s_row = len_ref[b:b + 1, :]
        bs_ref[b, 0:half_p, :] = (basis_ref[b].astype(jnp.float32) * s_row).astype(jnp.bfloat16)
        bs_ref[b, half_p:, :] = (other_ref[b].astype(jnp.float32) * s_row).astype(jnp.bfloat16)
        mask = jnp.int32(0)
        for o_k, live_k in slot_table(b):
            mask = mask | jnp.where(live_k, jnp.left_shift(jnp.int32(1), o_k), 0)
        for o in range(n_off):
            lst_ref[n_need] = jnp.int32(b * 32 + o)
            n_need = n_need + (jnp.right_shift(mask, o) & 1)

    def coupling(idx, cs_ref):
        b = jnp.right_shift(idx, 5)
        o = idx & 31
        wg = wgeo_ref[b + o]
        ys = [[jnp.broadcast_to(wg[c:c + 1, h * LANES:(h + 1) * LANES], (CHUNK, LANES))
               for h in range(n_tiles)] for c in (0, 1, 2, 4)]
        for mc in range(unk // CHUNK):
            r = slice(mc * CHUNK, (mc + 1) * CHUNK)
            xs = [bc_ref[b, c, r, :] for c in range(4)]
            for h in range(n_tiles):
                d0 = xs[0] - ys[0][h]
                d1 = xs[1] - ys[1][h]
                d2 = xs[2] - ys[2][h]
                dd = d0 * d0 + d1 * d1 + d2 * d2 + xs[3] * ys[3][h]
                cs_ref[r, h * LANES:(h + 1) * LANES] = lax.rsqrt(dd).astype(jnp.bfloat16)

    def finish(idx, cs_ref):
        b = jnp.right_shift(idx, 5)
        o = idx & 31
        j = b + o
        left = jnp.dot(bs_ref[b], cs_ref[...], preferred_element_type=jnp.float32)
        left = (left * wgeo_ref[j, 3:4, :]).astype(jnp.bfloat16)
        ts_ref[b * n_off + o] = lax.dot_general(left, wpan_ref[j], (((1,), (1,)), ((), ())),
                                                preferred_element_type=jnp.float32)

    bc_copy.wait()
    coupling(lst_ref[0], cs0_ref)

    def two_steps(t, carry):
        i = 2 * t + 1
        coupling(lst_ref[i], cs1_ref)
        finish(lst_ref[i - 1], cs0_ref)
        coupling(lst_ref[i + 1], cs0_ref)
        finish(lst_ref[i], cs1_ref)
        return carry

    lax.fori_loop(0, (n_need - 1) // 2, two_steps, 0)

    @pl.when(n_need % 2 == 0)
    def _():
        coupling(lst_ref[n_need - 1], cs1_ref)
        finish(lst_ref[n_need - 2], cs0_ref)
        finish(lst_ref[n_need - 1], cs1_ref)

    @pl.when(n_need % 2 == 1)
    def _():
        finish(lst_ref[n_need - 1], cs0_ref)

    for b in range(blk):
        for k, (o_k, live_k) in enumerate(slot_table(b)):
            t = ts_ref[b * n_off + o_k]
            t = jnp.where(live_k, t, jnp.zeros_like(t))
            cols_k = slice(k * nb_p, (k + 1) * nb_p)
            mine_ref[b, :, cols_k] = t[0:half_p]
            theirs_ref[b, :, cols_k] = t[half_p:].astype(theirs_ref.dtype)


def columns_kernel(pos_ref, rad_ref, bc_ref, *, unk):
    b = pl.program_id(0)
    rows = jnp.concatenate([pos_ref[b], rad_ref[pl.ds(b, 1), :],
                            jnp.zeros((LANES - 4, unk), jnp.float32)], axis=0)
    cols = jnp.transpose(rows)
    for c in range(4):
        bc_ref[0, c] = jnp.broadcast_to(cols[:, c:c + 1], (unk, LANES))


def pack_kernel(pos_ref, len_ref, rad_ref, basis_ref, other_ref, msg_ref, *, blk, half_p):
    nb_p = 2 * half_p
    for w in range(blk):
        msg_ref[w, 0:half_p, :] = basis_ref[w]
        msg_ref[w, half_p:nb_p, :] = other_ref[w]
        g = jnp.concatenate([pos_ref[w], len_ref[w:w + 1, :], rad_ref[w:w + 1, :]], axis=0)
        hi = g.astype(jnp.bfloat16)
        r1 = g - hi.astype(jnp.float32)
        mid = r1.astype(jnp.bfloat16)
        lo = (r1 - mid.astype(jnp.float32)).astype(jnp.bfloat16)
        parts = jnp.concatenate([hi.astype(jnp.float32), mid.astype(jnp.float32),
                                 lo.astype(jnp.float32), jnp.zeros_like(g[0:1])], axis=0)
        msg_ref[w, nb_p:nb_p + 16, :] = parts.astype(jnp.bfloat16)


def on_device(basis, positions, seglen, radius, neighbours, counts):
    blk, half_p, unk = basis.shape
    nb_p = 2 * half_p
    half = unk // 2
    near = neighbours.shape[1]
    n_row = lax.axis_size("row")
    ci = lax.axis_index("col")

    other = lax.ppermute(basis, "col", [(0, 1), (1, 0)])

    msg = pl.pallas_call(
        functools.partial(pack_kernel, blk=blk, half_p=half_p),
        out_shape=jax.ShapeDtypeStruct((blk, nb_p + 16, unk), jnp.bfloat16),
    )(positions, seglen, radius, basis, other)
    pairs = [(2 * i, 2 * (i + 1)) for i in range(n_row - 1)]
    pairs += [(2 * (i + 1) + 1, 2 * i + 1) for i in range(n_row - 1)]
    hrecv = lax.ppermute(msg, ("row", "col"), pairs)
    n_off = 2 * blk + 1

    def whole(shape):
        return pl.BlockSpec(shape, lambda i, *_: (0,) * len(shape))

    bc_shape = (blk, 4, unk, LANES)
    bc = pl.pallas_call(
        functools.partial(columns_kernel, unk=unk),
        out_shape=jax.ShapeDtypeStruct(bc_shape, jnp.float32),
        grid=(blk,),
        in_specs=[pl.BlockSpec(positions.shape, lambda b: (0, 0, 0)),
                  pl.BlockSpec(radius.shape, lambda b: (0, 0))],
        out_specs=pl.BlockSpec((1, 4, unk, LANES), lambda b: (b, 0, 0, 0)),
    )(positions, radius)
    hrecv, bc = lax.optimization_barrier((hrecv, bc))
    hx = lax.ppermute(lax.dynamic_slice_in_dim(hrecv, (1 - ci) * half, half, axis=2),
                      "col", [(0, 1), (1, 0)])

    part_shape = (blk, half_p, near * nb_p)
    mine, theirs = pl.pallas_call(
        functools.partial(pair_kernel, blk=blk, near=near, unk=unk, half=half, half_p=half_p),
        out_shape=(jax.ShapeDtypeStruct(part_shape, jnp.float32),
                   jax.ShapeDtypeStruct(part_shape, jnp.bfloat16)),
        grid_spec=pltpu.PrefetchScalarGridSpec(
            num_scalar_prefetch=2,
            grid=(1,),
            in_specs=[whole(positions.shape), whole(seglen.shape), whole(radius.shape),
                      whole(basis.shape), whole(other.shape),
                      whole(hrecv.shape), whole(hx.shape), pl.BlockSpec(memory_space=pl.ANY)],
            out_specs=(whole(part_shape), whole(part_shape)),
            scratch_shapes=[
                pltpu.VMEM((3 * blk, 8, half), jnp.float32),
                pltpu.VMEM((3 * blk, nb_p, half), jnp.bfloat16),
                pltpu.VMEM((blk, 4, unk, LANES), jnp.float32),
                pltpu.VMEM((blk, nb_p, unk), jnp.bfloat16),
                pltpu.VMEM((unk, half), jnp.bfloat16),
                pltpu.VMEM((unk, half), jnp.bfloat16),
                pltpu.VMEM((blk * n_off, nb_p, nb_p), jnp.float32),
                pltpu.SMEM((blk * 32,), jnp.int32),
                pltpu.SemaphoreType.DMA(()),
            ],
        ),
        compiler_params=pltpu.CompilerParams(dimension_semantics=("arbitrary",)),
    )(neighbours, counts, positions, seglen, radius, basis, other, hrecv, hx, bc)

    return mine + lax.ppermute(theirs, "col", [(0, 1), (1, 0)]).astype(jnp.float32)


def solution(mesh):
    placed = (
        P("row", "col", None),
        P("row", None, None),
        P("row", None),
        P("row", None),
        P("row", None),
        P("row"),
    )
    return jax.shard_map(
        on_device, mesh=mesh, in_specs=placed, out_specs=P("row", "col", None), check_vma=False
    )
```

```python
import functools

import jax
import jax.numpy as jnp
from jax import lax
from jax.experimental import pallas as pl
from jax.experimental.pallas import tpu as pltpu
from jax.sharding import PartitionSpec as P


CHUNK = 8
GROUP = 128
LANES = 128


def pair_kernel(nb_ref, cnt_ref, pos_ref, len_ref, rad_ref, basis_ref, other_ref,
                hrecv_hbm, hx_hbm, mine_ref, theirs_ref,
                wgeo_ref, wpan_ref, bc_ref, bs_ref, cs0_ref, cs1_ref, ts_ref, lst_ref,
                hrecv_ref, hx_ref, sems,
                *, blk, near, unk, half, half_p):
    ci = lax.axis_index("col")
    ri = lax.axis_index("row")
    n_off = 2 * blk + 1
    n_tiles = half // LANES
    nb_p = 2 * half_p

    copies = [pltpu.make_async_copy(hrecv_hbm, hrecv_ref, sems.at[0]),
              pltpu.make_async_copy(hx_hbm, hx_ref, sems.at[1])]
    for cp in copies:
        cp.start()

    def slot_table(b):
        gb = ri * blk + b
        cnt = cnt_ref[b]
        out = []
        for k in range(near):
            o_k = jnp.clip(nb_ref[b, k] - gb + blk, 0, 2 * blk)
            out.append((o_k, k < cnt))
        return out

    n_need = jnp.int32(0)
    for b in range(blk):
        rows = jnp.concatenate([pos_ref[b], rad_ref[b:b + 1, :],
                                jnp.zeros((LANES - 4, unk), jnp.float32)], axis=0)
        cols = jnp.transpose(rows)
        for c in range(4):
            bc_ref[b, c] = jnp.broadcast_to(cols[:, c:c + 1], (unk, LANES))
        s_row = len_ref[b:b + 1, :]
        bs_ref[b, 0:half_p, :] = (basis_ref[b].astype(jnp.float32) * s_row).astype(jnp.bfloat16)
        bs_ref[b, half_p:, :] = (other_ref[b].astype(jnp.float32) * s_row).astype(jnp.bfloat16)
        mask = jnp.int32(0)
        for o_k, live_k in slot_table(b):
            mask = mask | jnp.where(live_k, jnp.left_shift(jnp.int32(1), o_k), 0)
        for o in range(n_off):
            lst_ref[n_need] = jnp.int32(b * 32 + o)
            n_need = n_need + (jnp.right_shift(mask, o) & 1)

    for cp in copies:
        cp.wait()
    for hsel in range(2):
        @pl.when(ci == hsel)
        def _():
            lanes = slice(hsel * half, (hsel + 1) * half)
            if hsel == 0:
                sides = ((0, hrecv_ref, lanes, False), (2, hx_ref, slice(0, half), True))
            else:
                sides = ((2, hrecv_ref, lanes, True), (0, hx_ref, slice(0, half), False))
            for side, href, hl, swapped in sides:
                for w in range(blk):
                    g = href[w, nb_p:nb_p + 16, hl].astype(jnp.float32)
                    wgeo_ref[side * blk + w, 0:5, :] = g[0:5] + g[5:10] + g[10:15]
                    first = href[w, 0:half_p, hl]
                    second = href[w, half_p:nb_p, hl]
                    lo_rows, hi_rows = (second, first) if swapped else (first, second)
                    wpan_ref[side * blk + w, 0:half_p, :] = lo_rows
                    wpan_ref[side * blk + w, half_p:, :] = hi_rows
            for w in range(blk):
                wgeo_ref[blk + w, 0:3, :] = pos_ref[w, :, lanes]
                wgeo_ref[blk + w, 3:4, :] = len_ref[w:w + 1, lanes]
                wgeo_ref[blk + w, 4:5, :] = rad_ref[w:w + 1, lanes]
                first, second = (basis_ref, other_ref) if hsel == 0 else (other_ref, basis_ref)
                wpan_ref[blk + w, 0:half_p, :] = first[w, :, lanes]
                wpan_ref[blk + w, half_p:, :] = second[w, :, lanes]

    def coupling(idx, cs_ref):
        b = jnp.right_shift(idx, 5)
        o = idx & 31
        wg = wgeo_ref[b + o]
        ys = [[jnp.broadcast_to(wg[c:c + 1, h * LANES:(h + 1) * LANES], (CHUNK, LANES))
               for h in range(n_tiles)] for c in (0, 1, 2, 4)]
        for mc in range(unk // CHUNK):
            r = slice(mc * CHUNK, (mc + 1) * CHUNK)
            xs = [bc_ref[b, c, r, :] for c in range(4)]
            for h in range(n_tiles):
                d0 = xs[0] - ys[0][h]
                d1 = xs[1] - ys[1][h]
                d2 = xs[2] - ys[2][h]
                dd = d0 * d0 + d1 * d1 + d2 * d2 + xs[3] * ys[3][h]
                cs_ref[r, h * LANES:(h + 1) * LANES] = lax.rsqrt(dd).astype(jnp.bfloat16)

    def finish(idx, cs_ref):
        b = jnp.right_shift(idx, 5)
        o = idx & 31
        j = b + o
        left = jnp.dot(bs_ref[b], cs_ref[...], preferred_element_type=jnp.float32)
        left = (left * wgeo_ref[j, 3:4, :]).astype(jnp.bfloat16)
        ts_ref[b * n_off + o] = lax.dot_general(left, wpan_ref[j], (((1,), (1,)), ((), ())),
                                                preferred_element_type=jnp.float32)

    coupling(lst_ref[0], cs0_ref)

    def two_steps(t, carry):
        i = 2 * t + 1
        coupling(lst_ref[i], cs1_ref)
        finish(lst_ref[i - 1], cs0_ref)
        coupling(lst_ref[i + 1], cs0_ref)
        finish(lst_ref[i], cs1_ref)
        return carry

    lax.fori_loop(0, (n_need - 1) // 2, two_steps, 0)

    @pl.when(n_need % 2 == 0)
    def _():
        coupling(lst_ref[n_need - 1], cs1_ref)
        finish(lst_ref[n_need - 2], cs0_ref)
        finish(lst_ref[n_need - 1], cs1_ref)

    @pl.when(n_need % 2 == 1)
    def _():
        finish(lst_ref[n_need - 1], cs0_ref)

    for b in range(blk):
        for k, (o_k, live_k) in enumerate(slot_table(b)):
            t = ts_ref[b * n_off + o_k]
            t = jnp.where(live_k, t, jnp.zeros_like(t))
            cols_k = slice(k * nb_p, (k + 1) * nb_p)
            mine_ref[b, :, cols_k] = t[0:half_p]
            theirs_ref[b, :, cols_k] = t[half_p:].astype(theirs_ref.dtype)


def pack_kernel(pos_ref, len_ref, rad_ref, basis_ref, other_ref, msg_ref, *, blk, half_p):
    nb_p = 2 * half_p
    for w in range(blk):
        msg_ref[w, 0:half_p, :] = basis_ref[w]
        msg_ref[w, half_p:nb_p, :] = other_ref[w]
        g = jnp.concatenate([pos_ref[w], len_ref[w:w + 1, :], rad_ref[w:w + 1, :]], axis=0)
        hi = g.astype(jnp.bfloat16)
        r1 = g - hi.astype(jnp.float32)
        mid = r1.astype(jnp.bfloat16)
        lo = (r1 - mid.astype(jnp.float32)).astype(jnp.bfloat16)
        parts = jnp.concatenate([hi.astype(jnp.float32), mid.astype(jnp.float32),
                                 lo.astype(jnp.float32), jnp.zeros_like(g[0:1])], axis=0)
        msg_ref[w, nb_p:nb_p + 16, :] = parts.astype(jnp.bfloat16)


def on_device(basis, positions, seglen, radius, neighbours, counts):
    blk, half_p, unk = basis.shape
    nb_p = 2 * half_p
    half = unk // 2
    near = neighbours.shape[1]
    n_row = lax.axis_size("row")
    ci = lax.axis_index("col")

    other = lax.ppermute(basis, "col", [(0, 1), (1, 0)])

    msg = pl.pallas_call(
        functools.partial(pack_kernel, blk=blk, half_p=half_p),
        out_shape=jax.ShapeDtypeStruct((blk, nb_p + 16, unk), jnp.bfloat16),
    )(positions, seglen, radius, basis, other)
    pairs = [(2 * i, 2 * (i + 1)) for i in range(n_row - 1)]
    pairs += [(2 * (i + 1) + 1, 2 * i + 1) for i in range(n_row - 1)]
    hrecv = lax.ppermute(msg, ("row", "col"), pairs)
    hx = lax.ppermute(lax.dynamic_slice_in_dim(hrecv, (1 - ci) * half, half, axis=2),
                      "col", [(0, 1), (1, 0)])
    n_off = 2 * blk + 1

    def whole(shape):
        return pl.BlockSpec(shape, lambda i, *_: (0,) * len(shape))

    part_shape = (blk, half_p, near * nb_p)
    mine, theirs = pl.pallas_call(
        functools.partial(pair_kernel, blk=blk, near=near, unk=unk, half=half, half_p=half_p),
        out_shape=(jax.ShapeDtypeStruct(part_shape, jnp.float32),
                   jax.ShapeDtypeStruct(part_shape, jnp.bfloat16)),
        grid_spec=pltpu.PrefetchScalarGridSpec(
            num_scalar_prefetch=2,
            grid=(1,),
            in_specs=[whole(positions.shape), whole(seglen.shape), whole(radius.shape),
                      whole(basis.shape), whole(other.shape),
                      pl.BlockSpec(memory_space=pl.ANY), pl.BlockSpec(memory_space=pl.ANY)],
            out_specs=(whole(part_shape), whole(part_shape)),
            scratch_shapes=[
                pltpu.VMEM((3 * blk, 8, half), jnp.float32),
                pltpu.VMEM((3 * blk, nb_p, half), jnp.bfloat16),
                pltpu.VMEM((blk, 4, unk, LANES), jnp.float32),
                pltpu.VMEM((blk, nb_p, unk), jnp.bfloat16),
                pltpu.VMEM((unk, half), jnp.bfloat16),
                pltpu.VMEM((unk, half), jnp.bfloat16),
                pltpu.VMEM((blk * n_off, nb_p, nb_p), jnp.float32),
                pltpu.SMEM((blk * 32,), jnp.int32),
                pltpu.VMEM(hrecv.shape, jnp.bfloat16),
                pltpu.VMEM(hx.shape, jnp.bfloat16),
                pltpu.SemaphoreType.DMA((2,)),
            ],
        ),
        compiler_params=pltpu.CompilerParams(dimension_semantics=("arbitrary",)),
    )(neighbours, counts, positions, seglen, radius, basis, other, hrecv, hx)

    return mine + lax.ppermute(theirs, "col", [(0, 1), (1, 0)]).astype(jnp.float32)


def solution(mesh):
    placed = (
        P("row", "col", None),
        P("row", None, None),
        P("row", None),
        P("row", None),
        P("row", None),
        P("row"),
    )
    return jax.shard_map(
        on_device, mesh=mesh, in_specs=placed, out_specs=P("row", "col", None), check_vma=False
    )
```

```python
import functools

import jax
import jax.numpy as jnp
from jax import lax
from jax.experimental import pallas as pl
from jax.experimental.pallas import tpu as pltpu
from jax.sharding import PartitionSpec as P


CHUNK = 8
GROUP = 128
LANES = 128


def pair_kernel(nb_ref, cnt_ref, pos_ref, len_ref, rad_ref, basis_ref, other_ref,
                hrecv_hbm, hx_hbm, mine_ref, theirs_ref,
                wgeo_ref, wpan_ref, bc_ref, bs_ref, cs0_ref, cs1_ref, ts_ref, lst_ref,
                hrecv_ref, hx_ref, sems,
                *, blk, near, unk, half, half_p):
    ci = lax.axis_index("col")
    ri = lax.axis_index("row")
    n_off = 2 * blk + 1
    n_tiles = half // LANES
    nb_p = 2 * half_p

    copies = [pltpu.make_async_copy(hrecv_hbm, hrecv_ref, sems.at[0]),
              pltpu.make_async_copy(hx_hbm, hx_ref, sems.at[1])]
    for cp in copies:
        cp.start()

    def slot_table(b):
        gb = ri * blk + b
        cnt = cnt_ref[b]
        out = []
        for k in range(near):
            o_k = jnp.clip(nb_ref[b, k] - gb + blk, 0, 2 * blk)
            out.append((o_k, k < cnt))
        return out

    n_need = jnp.int32(0)
    for b in range(blk):
        rows = jnp.concatenate([pos_ref[c, b:b + 1, :] for c in range(3)] + [rad_ref[b:b + 1, :],
                                jnp.zeros((LANES - 4, unk), jnp.float32)], axis=0)
        cols = jnp.transpose(rows)
        for c in range(4):
            bc_ref[b, c] = jnp.broadcast_to(cols[:, c:c + 1], (unk, LANES))
        s_row = len_ref[b:b + 1, :]
        bs_ref[b, 0:half_p, :] = (basis_ref[b].astype(jnp.float32) * s_row).astype(jnp.bfloat16)
        bs_ref[b, half_p:, :] = (other_ref[b].astype(jnp.float32) * s_row).astype(jnp.bfloat16)
        mask = jnp.int32(0)
        for o_k, live_k in slot_table(b):
            mask = mask | jnp.where(live_k, jnp.left_shift(jnp.int32(1), o_k), 0)
        for o in range(n_off):
            lst_ref[n_need] = jnp.int32(b * 32 + o)
            n_need = n_need + (jnp.right_shift(mask, o) & 1)

    for cp in copies:
        cp.wait()
    for hsel in range(2):
        @pl.when(ci == hsel)
        def _():
            lanes = slice(hsel * half, (hsel + 1) * half)
            if hsel == 0:
                sides = ((0, hrecv_ref, lanes, False), (2, hx_ref, slice(0, half), True))
            else:
                sides = ((2, hrecv_ref, lanes, True), (0, hx_ref, slice(0, half), False))
            for side, href, hl, swapped in sides:
                for w in range(blk):
                    g = href[w, nb_p:nb_p + 16, hl].astype(jnp.float32)
                    wgeo_ref[side * blk + w, 0:5, :] = g[0:5] + g[5:10] + g[10:15]
                    first = href[w, 0:half_p, hl]
                    second = href[w, half_p:nb_p, hl]
                    lo_rows, hi_rows = (second, first) if swapped else (first, second)
                    wpan_ref[side * blk + w, 0:half_p, :] = lo_rows
                    wpan_ref[side * blk + w, half_p:, :] = hi_rows
            for w in range(blk):
                for c in range(3):
                    wgeo_ref[blk + w, c:c + 1, :] = pos_ref[c, w:w + 1, lanes]
                wgeo_ref[blk + w, 3:4, :] = len_ref[w:w + 1, lanes]
                wgeo_ref[blk + w, 4:5, :] = rad_ref[w:w + 1, lanes]
                first, second = (basis_ref, other_ref) if hsel == 0 else (other_ref, basis_ref)
                wpan_ref[blk + w, 0:half_p, :] = first[w, :, lanes]
                wpan_ref[blk + w, half_p:, :] = second[w, :, lanes]

    def coupling(idx, cs_ref):
        b = jnp.right_shift(idx, 5)
        o = idx & 31
        wg = wgeo_ref[b + o]
        ys = [[jnp.broadcast_to(wg[c:c + 1, h * LANES:(h + 1) * LANES], (CHUNK, LANES))
               for h in range(n_tiles)] for c in (0, 1, 2, 4)]
        for mc in range(unk // CHUNK):
            r = slice(mc * CHUNK, (mc + 1) * CHUNK)
            xs = [bc_ref[b, c, r, :] for c in range(4)]
            for h in range(n_tiles):
                d0 = xs[0] - ys[0][h]
                d1 = xs[1] - ys[1][h]
                d2 = xs[2] - ys[2][h]
                dd = d0 * d0 + d1 * d1 + d2 * d2 + xs[3] * ys[3][h]
                cs_ref[r, h * LANES:(h + 1) * LANES] = lax.rsqrt(dd).astype(jnp.bfloat16)

    def finish(idx, cs_ref):
        b = jnp.right_shift(idx, 5)
        o = idx & 31
        j = b + o
        left = jnp.dot(bs_ref[b], cs_ref[...], preferred_element_type=jnp.float32)
        left = (left * wgeo_ref[j, 3:4, :]).astype(jnp.bfloat16)
        ts_ref[b * n_off + o] = lax.dot_general(left, wpan_ref[j], (((1,), (1,)), ((), ())),
                                                preferred_element_type=jnp.float32)

    coupling(lst_ref[0], cs0_ref)

    def two_steps(t, carry):
        i = 2 * t + 1
        coupling(lst_ref[i], cs1_ref)
        finish(lst_ref[i - 1], cs0_ref)
        coupling(lst_ref[i + 1], cs0_ref)
        finish(lst_ref[i], cs1_ref)
        return carry

    lax.fori_loop(0, (n_need - 1) // 2, two_steps, 0)

    @pl.when(n_need % 2 == 0)
    def _():
        coupling(lst_ref[n_need - 1], cs1_ref)
        finish(lst_ref[n_need - 2], cs0_ref)
        finish(lst_ref[n_need - 1], cs1_ref)

    @pl.when(n_need % 2 == 1)
    def _():
        finish(lst_ref[n_need - 1], cs0_ref)

    for b in range(blk):
        for k, (o_k, live_k) in enumerate(slot_table(b)):
            t = ts_ref[b * n_off + o_k]
            t = jnp.where(live_k, t, jnp.zeros_like(t))
            cols_k = slice(k * nb_p, (k + 1) * nb_p)
            mine_ref[b, :, cols_k] = t[0:half_p]
            theirs_ref[b, :, cols_k] = t[half_p:].astype(theirs_ref.dtype)


def pack_kernel(pos_ref, len_ref, rad_ref, basis_ref, other_ref, msg_ref, *, blk, half_p):
    nb_p = 2 * half_p
    for w in range(blk):
        msg_ref[w, 0:half_p, :] = basis_ref[w]
        msg_ref[w, half_p:nb_p, :] = other_ref[w]
        g = jnp.concatenate([pos_ref[c, w:w + 1, :] for c in range(3)]
                            + [len_ref[w:w + 1, :], rad_ref[w:w + 1, :]], axis=0)
        hi = g.astype(jnp.bfloat16)
        r1 = g - hi.astype(jnp.float32)
        mid = r1.astype(jnp.bfloat16)
        lo = (r1 - mid.astype(jnp.float32)).astype(jnp.bfloat16)
        parts = jnp.concatenate([hi.astype(jnp.float32), mid.astype(jnp.float32),
                                 lo.astype(jnp.float32), jnp.zeros_like(g[0:1])], axis=0)
        msg_ref[w, nb_p:nb_p + 16, :] = parts.astype(jnp.bfloat16)


def on_device(basis, positions, seglen, radius, neighbours, counts):
    blk, half_p, unk = basis.shape
    nb_p = 2 * half_p
    half = unk // 2
    near = neighbours.shape[1]
    n_row = lax.axis_size("row")
    ci = lax.axis_index("col")

    other = lax.ppermute(basis, "col", [(0, 1), (1, 0)])
    positions = jnp.transpose(positions, (1, 0, 2))

    msg = pl.pallas_call(
        functools.partial(pack_kernel, blk=blk, half_p=half_p),
        out_shape=jax.ShapeDtypeStruct((blk, nb_p + 16, unk), jnp.bfloat16),
    )(positions, seglen, radius, basis, other)
    pairs = [(2 * i, 2 * (i + 1)) for i in range(n_row - 1)]
    pairs += [(2 * (i + 1) + 1, 2 * i + 1) for i in range(n_row - 1)]
    hrecv = lax.ppermute(msg, ("row", "col"), pairs)
    hx = lax.ppermute(lax.dynamic_slice_in_dim(hrecv, (1 - ci) * half, half, axis=2),
                      "col", [(0, 1), (1, 0)])
    n_off = 2 * blk + 1

    def whole(shape):
        return pl.BlockSpec(shape, lambda i, *_: (0,) * len(shape))

    part_shape = (blk, half_p, near * nb_p)
    mine, theirs = pl.pallas_call(
        functools.partial(pair_kernel, blk=blk, near=near, unk=unk, half=half, half_p=half_p),
        out_shape=(jax.ShapeDtypeStruct(part_shape, jnp.float32),
                   jax.ShapeDtypeStruct(part_shape, jnp.bfloat16)),
        grid_spec=pltpu.PrefetchScalarGridSpec(
            num_scalar_prefetch=2,
            grid=(1,),
            in_specs=[whole(positions.shape), whole(seglen.shape), whole(radius.shape),
                      whole(basis.shape), whole(other.shape),
                      pl.BlockSpec(memory_space=pl.ANY), pl.BlockSpec(memory_space=pl.ANY)],
            out_specs=(whole(part_shape), whole(part_shape)),
            scratch_shapes=[
                pltpu.VMEM((3 * blk, 8, half), jnp.float32),
                pltpu.VMEM((3 * blk, nb_p, half), jnp.bfloat16),
                pltpu.VMEM((blk, 4, unk, LANES), jnp.float32),
                pltpu.VMEM((blk, nb_p, unk), jnp.bfloat16),
                pltpu.VMEM((unk, half), jnp.bfloat16),
                pltpu.VMEM((unk, half), jnp.bfloat16),
                pltpu.VMEM((blk * n_off, nb_p, nb_p), jnp.float32),
                pltpu.SMEM((blk * 32,), jnp.int32),
                pltpu.VMEM(hrecv.shape, jnp.bfloat16),
                pltpu.VMEM(hx.shape, jnp.bfloat16),
                pltpu.SemaphoreType.DMA((2,)),
            ],
        ),
        compiler_params=pltpu.CompilerParams(dimension_semantics=("arbitrary",)),
    )(neighbours, counts, positions, seglen, radius, basis, other, hrecv, hx)

    return mine + lax.ppermute(theirs, "col", [(0, 1), (1, 0)]).astype(jnp.float32)


def solution(mesh):
    placed = (
        P("row", "col", None),
        P("row", None, None),
        P("row", None),
        P("row", None),
        P("row", None),
        P("row"),
    )
    return jax.shard_map(
        on_device, mesh=mesh, in_specs=placed, out_specs=P("row", "col", None), check_vma=False
    )
```

```python
import functools

import jax
import jax.numpy as jnp
from jax import lax
from jax.experimental import pallas as pl
from jax.experimental.pallas import tpu as pltpu
from jax.sharding import PartitionSpec as P


CHUNK = 16
GROUP = 128
LANES = 128


def pair_kernel(nb_ref, cnt_ref, pos_ref, len_ref, rad_ref, basis_ref, other_ref,
                hrecv_ref, hx_ref, mine_ref, theirs_ref,
                wgeo_ref, wpan_ref, bc_ref, bs_ref, cs0_ref, cs1_ref, ts_ref, lst_ref,
                *, blk, near, unk, half, half_p):
    ci = lax.axis_index("col")
    ri = lax.axis_index("row")
    n_off = 2 * blk + 1
    n_tiles = half // LANES
    nb_p = 2 * half_p

    for hsel in range(2):
        @pl.when(ci == hsel)
        def _():
            lanes = slice(hsel * half, (hsel + 1) * half)
            if hsel == 0:
                sides = ((0, hrecv_ref, lanes, False), (2, hx_ref, slice(0, half), True))
            else:
                sides = ((2, hrecv_ref, lanes, True), (0, hx_ref, slice(0, half), False))
            for side, href, hl, swapped in sides:
                for w in range(blk):
                    g = href[w, nb_p:nb_p + 16, hl].astype(jnp.float32)
                    wgeo_ref[side * blk + w, 0:5, :] = g[0:5] + g[5:10] + g[10:15]
                    first = href[w, 0:half_p, hl]
                    second = href[w, half_p:nb_p, hl]
                    lo_rows, hi_rows = (second, first) if swapped else (first, second)
                    wpan_ref[side * blk + w, 0:half_p, :] = lo_rows
                    wpan_ref[side * blk + w, half_p:, :] = hi_rows
            for w in range(blk):
                wgeo_ref[blk + w, 0:3, :] = pos_ref[w, :, lanes]
                wgeo_ref[blk + w, 3:4, :] = len_ref[w:w + 1, lanes]
                wgeo_ref[blk + w, 4:5, :] = rad_ref[w:w + 1, lanes]
                first, second = (basis_ref, other_ref) if hsel == 0 else (other_ref, basis_ref)
                wpan_ref[blk + w, 0:half_p, :] = first[w, :, lanes]
                wpan_ref[blk + w, half_p:, :] = second[w, :, lanes]

    def slot_table(b):
        gb = ri * blk + b
        cnt = cnt_ref[b]
        out = []
        for k in range(near):
            o_k = jnp.clip(nb_ref[b, k] - gb + blk, 0, 2 * blk)
            out.append((o_k, k < cnt))
        return out

    n_need = jnp.int32(0)
    for b in range(blk):
        rows = jnp.concatenate([pos_ref[b], rad_ref[b:b + 1, :],
                                jnp.zeros((LANES - 4, unk), jnp.float32)], axis=0)
        cols = jnp.transpose(rows)
        for c in range(4):
            bc_ref[b, c] = jnp.broadcast_to(cols[:, c:c + 1], (unk, LANES))
        s_row = len_ref[b:b + 1, :]
        bs_ref[b, 0:half_p, :] = (basis_ref[b].astype(jnp.float32) * s_row).astype(jnp.bfloat16)
        bs_ref[b, half_p:, :] = (other_ref[b].astype(jnp.float32) * s_row).astype(jnp.bfloat16)
        mask = jnp.int32(0)
        for o_k, live_k in slot_table(b):
            mask = mask | jnp.where(live_k, jnp.left_shift(jnp.int32(1), o_k), 0)
        for o in range(n_off):
            lst_ref[n_need] = jnp.int32(b * 32 + o)
            n_need = n_need + (jnp.right_shift(mask, o) & 1)

    def coupling(idx, cs_ref):
        b = jnp.right_shift(idx, 5)
        o = idx & 31
        wg = wgeo_ref[b + o]
        ys = [[jnp.broadcast_to(wg[c:c + 1, h * LANES:(h + 1) * LANES], (CHUNK, LANES))
               for h in range(n_tiles)] for c in (0, 1, 2, 4)]
        for mc in range(unk // CHUNK):
            r = slice(mc * CHUNK, (mc + 1) * CHUNK)
            xs = [bc_ref[b, c, r, :] for c in range(4)]
            for h in range(n_tiles):
                d0 = xs[0] - ys[0][h]
                d1 = xs[1] - ys[1][h]
                d2 = xs[2] - ys[2][h]
                dd = d0 * d0 + d1 * d1 + d2 * d2 + xs[3] * ys[3][h]
                cs_ref[r, h * LANES:(h + 1) * LANES] = lax.rsqrt(dd).astype(jnp.bfloat16)

    def finish(idx, cs_ref):
        b = jnp.right_shift(idx, 5)
        o = idx & 31
        j = b + o
        left = jnp.dot(bs_ref[b], cs_ref[...], preferred_element_type=jnp.float32)
        left = (left * wgeo_ref[j, 3:4, :]).astype(jnp.bfloat16)
        ts_ref[b * n_off + o] = lax.dot_general(left, wpan_ref[j], (((1,), (1,)), ((), ())),
                                                preferred_element_type=jnp.float32)

    coupling(lst_ref[0], cs0_ref)

    def two_steps(t, carry):
        i = 2 * t + 1
        coupling(lst_ref[i], cs1_ref)
        finish(lst_ref[i - 1], cs0_ref)
        coupling(lst_ref[i + 1], cs0_ref)
        finish(lst_ref[i], cs1_ref)
        return carry

    lax.fori_loop(0, (n_need - 1) // 2, two_steps, 0)

    @pl.when(n_need % 2 == 0)
    def _():
        coupling(lst_ref[n_need - 1], cs1_ref)
        finish(lst_ref[n_need - 2], cs0_ref)
        finish(lst_ref[n_need - 1], cs1_ref)

    @pl.when(n_need % 2 == 1)
    def _():
        finish(lst_ref[n_need - 1], cs0_ref)

    for b in range(blk):
        for k, (o_k, live_k) in enumerate(slot_table(b)):
            t = ts_ref[b * n_off + o_k]
            t = jnp.where(live_k, t, jnp.zeros_like(t))
            cols_k = slice(k * nb_p, (k + 1) * nb_p)
            mine_ref[b, :, cols_k] = t[0:half_p]
            theirs_ref[b, :, cols_k] = t[half_p:].astype(theirs_ref.dtype)


def pack_kernel(pos_ref, len_ref, rad_ref, basis_ref, other_ref, msg_ref, *, blk, half_p):
    nb_p = 2 * half_p
    for w in range(blk):
        msg_ref[w, 0:half_p, :] = basis_ref[w]
        msg_ref[w, half_p:nb_p, :] = other_ref[w]
        g = jnp.concatenate([pos_ref[w], len_ref[w:w + 1, :], rad_ref[w:w + 1, :]], axis=0)
        hi = g.astype(jnp.bfloat16)
        r1 = g - hi.astype(jnp.float32)
        mid = r1.astype(jnp.bfloat16)
        lo = (r1 - mid.astype(jnp.float32)).astype(jnp.bfloat16)
        parts = jnp.concatenate([hi.astype(jnp.float32), mid.astype(jnp.float32),
                                 lo.astype(jnp.float32), jnp.zeros_like(g[0:1])], axis=0)
        msg_ref[w, nb_p:nb_p + 16, :] = parts.astype(jnp.bfloat16)


def on_device(basis, positions, seglen, radius, neighbours, counts):
    blk, half_p, unk = basis.shape
    nb_p = 2 * half_p
    half = unk // 2
    near = neighbours.shape[1]
    n_row = lax.axis_size("row")
    ci = lax.axis_index("col")

    other = lax.ppermute(basis, "col", [(0, 1), (1, 0)])

    msg = pl.pallas_call(
        functools.partial(pack_kernel, blk=blk, half_p=half_p),
        out_shape=jax.ShapeDtypeStruct((blk, nb_p + 16, unk), jnp.bfloat16),
    )(positions, seglen, radius, basis, other)
    pairs = [(2 * i, 2 * (i + 1)) for i in range(n_row - 1)]
    pairs += [(2 * (i + 1) + 1, 2 * i + 1) for i in range(n_row - 1)]
    hrecv = lax.ppermute(msg, ("row", "col"), pairs)
    hx = lax.ppermute(lax.dynamic_slice_in_dim(hrecv, (1 - ci) * half, half, axis=2),
                      "col", [(0, 1), (1, 0)])
    n_off = 2 * blk + 1

    def whole(shape):
        return pl.BlockSpec(shape, lambda i, *_: (0,) * len(shape))

    part_shape = (blk, half_p, near * nb_p)
    mine, theirs = pl.pallas_call(
        functools.partial(pair_kernel, blk=blk, near=near, unk=unk, half=half, half_p=half_p),
        out_shape=(jax.ShapeDtypeStruct(part_shape, jnp.float32),
                   jax.ShapeDtypeStruct(part_shape, jnp.bfloat16)),
        grid_spec=pltpu.PrefetchScalarGridSpec(
            num_scalar_prefetch=2,
            grid=(1,),
            in_specs=[whole(positions.shape), whole(seglen.shape), whole(radius.shape),
                      whole(basis.shape), whole(other.shape),
                      whole(hrecv.shape), whole(hx.shape)],
            out_specs=(whole(part_shape), whole(part_shape)),
            scratch_shapes=[
                pltpu.VMEM((3 * blk, 8, half), jnp.float32),
                pltpu.VMEM((3 * blk, nb_p, half), jnp.bfloat16),
                pltpu.VMEM((blk, 4, unk, LANES), jnp.float32),
                pltpu.VMEM((blk, nb_p, unk), jnp.bfloat16),
                pltpu.VMEM((unk, half), jnp.bfloat16),
                pltpu.VMEM((unk, half), jnp.bfloat16),
                pltpu.VMEM((blk * n_off, nb_p, nb_p), jnp.float32),
                pltpu.SMEM((blk * 32,), jnp.int32),
            ],
        ),
        compiler_params=pltpu.CompilerParams(dimension_semantics=("arbitrary",)),
    )(neighbours, counts, positions, seglen, radius, basis, other, hrecv, hx)

    return mine + lax.ppermute(theirs, "col", [(0, 1), (1, 0)]).astype(jnp.float32)


def solution(mesh):
    placed = (
        P("row", "col", None),
        P("row", None, None),
        P("row", None),
        P("row", None),
        P("row", None),
        P("row"),
    )
    return jax.shard_map(
        on_device, mesh=mesh, in_specs=placed, out_specs=P("row", "col", None), check_vma=False
    )
```
